32 devices in a mesh: blk: 32 (over z, y, x, core).
Axes of the slice: x: 2, y: 2, z: 4, core: 2. Of those that a mesh axis runs over, the one named last changes fastest.
Arguments:
- populations: float32 [19, 256, 16, 256], P(None, 'blk'), may hold values from 0.01 to 0.2
- solute: float32 [7, 256, 16, 256], P(None, 'blk'), may hold values from 0.05 to 0.4
- mineral: float32 [256, 16, 256], P('blk'), may hold values from 0.2 to 1
- solid: int32 [256, 16, 256], P('blk'), may hold values 0 or 1
- plane_moves: int32 [32, 2], replicated, may hold values from 0 to 3, as said below
Outputs:
- flow_out: float32 [19, 448, 16, 256], P(None, 'blk')
- acid_out: float32 [7, 448, 16, 256], P(None, 'blk')
- mineral_out: float32 [448, 16, 256], P('blk')
- solid_out: int32 [448, 16, 256], P('blk')
The draws below stay inside these ranges and needn't reach their ends.
Inputs may be any that keep to these rules, and one draw needn't show every extreme that they name: `plane_moves`: counts at most 3 each, and some entry equals 3.
All inputs are finite; a program needn't handle non-finite values. No bound on the sum of `solid` on one device may be relied on, other than what follows from the above.
Results may differ from the reference program's by a relative error of at most 0.0003.
Values sent between devices are 32-bit elements; how exact they have to be, the bound alone decides.
No kernel may reach another device: no remote copies, remote signals or barrier semaphores. Data moves between devices by JAX's collectives and lax.ppermute only.
A program may use at most 128 MiB of HBM per device.

```python
import jax
import jax.numpy as jnp

CZ = 8
XW = 16
NY = 256
MOVE_MOST = 3
NZ = 256
CAP = 14
N_BLK = 32


def draw_plane_moves(key, part):
    drawn_moves = jax.random.randint(jax.random.fold_in(key, 11), (N_BLK * 2,), 0, MOVE_MOST + 1)
    chosen_entry = jax.random.randint(jax.random.fold_in(key, 12), (), 0, N_BLK * 2)
    entry_ids = jnp.arange(N_BLK * 2)
    flat_moves = jnp.where(entry_ids == chosen_entry, MOVE_MOST, drawn_moves)
    return flat_moves.reshape(N_BLK, 2).astype(jnp.int32)


def place_ends(entries, key, smallest, top_value):
    shape = entries.shape
    spot = [jax.random.randint(jax.random.fold_in(key, axis), (), 0, shape[axis]) for axis in range(len(shape))]
    entries = entries.at[tuple(spot)].set(smallest)
    longest = shape.index(max(shape))
    spot[longest] = (spot[longest] + 1) % shape[longest]
    return entries.at[tuple(spot)].set(top_value)


def steps_of(own_key, dims, pieces, least, largest):
    def one(dim, shards_of):
        steps = jax.random.uniform(jax.random.fold_in(jax.random.fold_in(own_key, 6), dim), (shards_of,), jnp.float32, least / len(pieces), largest / len(pieces))
        return jnp.repeat(jnp.exp(steps), dims[dim] // shards_of).reshape((-1,) + (1,) * (len(dims) - dim - 1))

    gain = one(*pieces[0])
    for cut in pieces[1:]:
        gain = gain * one(*cut)
    return gain


def setup_inputs(seed: int = 0) -> dict:
    seeds = jax.random.split(jax.random.key(seed), 6)
    populations = jnp.clip(0.01 + 0.19 * jax.random.uniform(seeds[0], (19, NZ, XW, NY), jnp.float32) ** steps_of(seeds[0], (19, NZ, XW, NY), ((1, 32),), -0.2, 0.2), 0.01, 0.2)
    solute = jnp.clip(0.05 + 0.35 * jax.random.uniform(seeds[1], (7, NZ, XW, NY), jnp.float32) ** steps_of(seeds[1], (7, NZ, XW, NY), ((1, 32),), -0.2, 0.2), 0.05, 0.4)
    mineral = jnp.clip(0.2 + 0.8 * jax.random.uniform(seeds[2], (NZ, XW, NY), jnp.float32) ** steps_of(seeds[2], (NZ, XW, NY), ((0, 32),), -0.2, 0.2), 0.2, 1.0)
    solid = place_ends((jax.random.randint(seeds[3], (NZ, XW, NY), 0, 3) < 1).astype(jnp.int32), jax.random.fold_in(seeds[3], 1), 0, 1)
    plane_moves = draw_plane_moves(jax.random.fold_in(seeds[5], 71), 0)
    return dict(populations=populations, solute=solute, mineral=mineral, solid=solid, plane_moves=plane_moves)


flow_vel = [(0, 0, 1), (1, 0, 1), (-1, 0, 1), (0, 1, 1), (0, -1, 1), (0, 0, -1), (1, 0, -1), (-1, 0, -1), (0, 1, -1), (0, -1, -1), (0, 0, 0), (1, 0, 0), (-1, 0, 0), (0, 1, 0), (0, -1, 0), (1, 1, 0), (-1, -1, 0), (1, -1, 0), (-1, 1, 0)]
flow_weight = [1.0 / 18, 1.0 / 36, 1.0 / 36, 1.0 / 36, 1.0 / 36, 1.0 / 18, 1.0 / 36, 1.0 / 36, 1.0 / 36, 1.0 / 36, 1.0 / 3, 1.0 / 18, 1.0 / 18, 1.0 / 18, 1.0 / 18, 1.0 / 36, 1.0 / 36, 1.0 / 36, 1.0 / 36]
acid_vel = [(0, 0, 1), (0, 0, -1), (0, 0, 0), (1, 0, 0), (-1, 0, 0), (0, 1, 0), (0, -1, 0)]
acid_weight = [0.125, 0.125, 0.25, 0.125, 0.125, 0.125, 0.125]
relax_flow = 1.25
relax_acid = 0.8
body_force = 0.001
react_rate = 0.1
dissolve_rate = 0.5


def shifted(block_in, shift_x, shift_y):
    return jnp.roll(jnp.roll(block_in, shift_x, axis=1), shift_y, axis=2)


def neighbours(padded):
    middle = padded[1:-1]
    total = padded[:-2] + padded[2:]
    total = total + shifted(middle, 1, 0) + shifted(middle, -1, 0)
    return total + shifted(middle, 0, 1) + shifted(middle, 0, -1)


def collide(flow_now, acid_now, state_pad):
    solid_pad, conc_pad, mineral_pad = state_pad[0], state_pad[1], state_pad[2]
    solid_own = solid_pad[1:-1]
    density = jnp.sum(flow_now, axis=0)
    vel_x = jnp.zeros_like(density)
    vel_y = jnp.zeros_like(density)
    vel_z = jnp.zeros_like(density)
    for slot_id, (shift_x, shift_y, shift_z) in enumerate(flow_vel):
        vel_x = vel_x + shift_x * flow_now[slot_id]
        vel_y = vel_y + shift_y * flow_now[slot_id]
        vel_z = vel_z + shift_z * flow_now[slot_id]
    vel_x = vel_x / density
    vel_y = vel_y / density
    vel_z = vel_z / density
    speed_sq = vel_x * vel_x + vel_y * vel_y + vel_z * vel_z
    relaxed_list = []
    for slot_id, (shift_x, shift_y, shift_z) in enumerate(flow_vel):
        along_vel = shift_x * vel_x + shift_y * vel_y + shift_z * vel_z
        equilibrium = flow_weight[slot_id] * density * (1.0 + 3.0 * along_vel + 4.5 * along_vel * along_vel - 1.5 * speed_sq)
        relaxed = flow_now[slot_id] - (flow_now[slot_id] - equilibrium) / relax_flow + 3.0 * flow_weight[slot_id] * shift_z * body_force * density
        relaxed_list.append(jnp.where(solid_own > 0.5, flow_now[slot_id], relaxed))
    flow_post = jnp.stack(relaxed_list)
    concentration = conc_pad[1:-1]
    acid_sink = react_rate * concentration * neighbours(solid_pad * mineral_pad)
    relaxed_list = []
    for slot_id, (shift_x, shift_y, shift_z) in enumerate(acid_vel):
        along_vel = shift_x * vel_x + shift_y * vel_y + shift_z * vel_z
        equilibrium = acid_weight[slot_id] * concentration * (1.0 + 4.0 * along_vel)
        relaxed = acid_now[slot_id] - (acid_now[slot_id] - equilibrium) / relax_acid - acid_weight[slot_id] * acid_sink
        relaxed_list.append(jnp.where(solid_own > 0.5, acid_now[slot_id], relaxed))
    acid_post = jnp.stack(relaxed_list)
    mineral_own = mineral_pad[1:-1]
    mineral_loss = dissolve_rate * react_rate * mineral_own * neighbours((1.0 - solid_pad) * conc_pad)
    return flow_post, acid_post, mineral_own - solid_own * mineral_loss


def propagate(padded, velocity_table, solid_pad):
    plane_count = padded.shape[1]
    result_list = []
    for slot_id, (shift_x, shift_y, shift_z) in enumerate(velocity_table):
        opposite = velocity_table.index((-shift_x, -shift_y, -shift_z))
        pulled = shifted(padded[slot_id, 1 - shift_z:plane_count - 1 - shift_z], shift_x, shift_y)
        solid_source = shifted(solid_pad[1 - shift_z:plane_count - 1 - shift_z], shift_x, shift_y)
        arrived = jnp.where(solid_source > 0.5, padded[opposite, 1:plane_count - 1], pulled)
        arrived = jnp.where(solid_pad[1:plane_count - 1] > 0.5, padded[slot_id, 1:plane_count - 1], arrived)
        result_list.append(arrived)
    return jnp.stack(result_list)


def wrap_pad(block_in):
    return jnp.concatenate([block_in[:, -1:], block_in, block_in[:, :1]], axis=1)


def reference(populations, solute, mineral, solid, plane_moves):
    solid_float = solid.astype(jnp.float32)
    flow_now, acid_now, mineral_now = populations, solute, mineral
    for step_id in range(2):
        state_now = jnp.stack([solid_float, jnp.sum(acid_now, axis=0), mineral_now])
        state_pad = wrap_pad(state_now)
        flow_post, acid_post, mineral_now = collide(flow_now, acid_now, state_pad)
        flow_now = propagate(wrap_pad(flow_post), flow_vel, state_pad[0])
        acid_now = propagate(wrap_pad(acid_post), acid_vel, state_pad[0])
    owner_ids = jnp.arange(N_BLK, dtype=jnp.int32)
    lower_peer = jnp.mod(owner_ids - 1, N_BLK)
    upper_peer = jnp.mod(owner_ids + 1, N_BLK)
    from_low = plane_moves[lower_peer, 1][:, None]
    send_low = plane_moves[:, 0][:, None]
    send_high = plane_moves[:, 1][:, None]
    from_high = plane_moves[upper_peer, 0][:, None]
    kept_planes = CZ - send_low - send_high
    slot_ids = jnp.arange(CAP, dtype=jnp.int32)[None, :]
    source_ids = jnp.where(slot_ids < from_low, lower_peer[:, None] * CZ + CZ - from_low + slot_ids,
                           jnp.where(slot_ids < from_low + kept_planes, owner_ids[:, None] * CZ + send_low + slot_ids - from_low,
                                     upper_peer[:, None] * CZ + slot_ids - from_low - kept_planes))
    is_valid = (slot_ids < from_low + kept_planes + from_high).reshape(-1)
    source_ids = jnp.clip(source_ids, 0, NZ - 1).reshape(-1).astype(jnp.int32)
    flow_out = jnp.where(is_valid[None, :, None, None], jnp.take(flow_now, source_ids, axis=1), 0.0)
    acid_out = jnp.where(is_valid[None, :, None, None], jnp.take(acid_now, source_ids, axis=1), 0.0)
    mineral_out = jnp.where(is_valid[:, None, None], jnp.take(mineral_now, source_ids, axis=0), 0.0)
    solid_out = jnp.where(is_valid[:, None, None], jnp.take(solid, source_ids, axis=0), 0).astype(jnp.int32)
    return (flow_out, acid_out, mineral_out, solid_out)
```

```python
import functools

import jax
import jax.numpy as jnp
from jax import lax
from jax.experimental import pallas as pl
from jax.experimental.pallas import tpu as pltpu
from jax.sharding import PartitionSpec as P

MOVE_MOST = 3
HALO = 3

flow_vel = [
    (0, 0, 1),
    (1, 0, 1),
    (-1, 0, 1),
    (0, 1, 1),
    (0, -1, 1),
    (0, 0, -1),
    (1, 0, -1),
    (-1, 0, -1),
    (0, 1, -1),
    (0, -1, -1),
    (0, 0, 0),
    (1, 0, 0),
    (-1, 0, 0),
    (0, 1, 0),
    (0, -1, 0),
    (1, 1, 0),
    (-1, -1, 0),
    (1, -1, 0),
    (-1, 1, 0),
]
flow_weight = [
    1.0 / 18,
    1.0 / 36,
    1.0 / 36,
    1.0 / 36,
    1.0 / 36,
    1.0 / 18,
    1.0 / 36,
    1.0 / 36,
    1.0 / 36,
    1.0 / 36,
    1.0 / 3,
    1.0 / 18,
    1.0 / 18,
    1.0 / 18,
    1.0 / 18,
    1.0 / 36,
    1.0 / 36,
    1.0 / 36,
    1.0 / 36,
]
acid_vel = [(0, 0, 1), (0, 0, -1), (0, 0, 0), (1, 0, 0), (-1, 0, 0), (0, 1, 0), (0, -1, 0)]
acid_weight = [0.125, 0.125, 0.25, 0.125, 0.125, 0.125, 0.125]
relax_flow = 1.25
relax_acid = 0.8
body_force = 0.001
react_rate = 0.1
dissolve_rate = 0.5

NF = len(flow_vel)
NG = len(acid_vel)
NC = NF + NG + 2


def roll_xy(a, cx, cy):
    if cx:
        a = pltpu.roll(a, cx % a.shape[0], 0)
    if cy:
        a = pltpu.roll(a, cy % a.shape[1], 1)
    return a


def face_sum(ref, i):
    mid = ref[i]
    total = ref[i - 1] + ref[i + 1]
    total = total + (roll_xy(mid, 1, 0) + roll_xy(mid, -1, 0))
    return total + (roll_xy(mid, 0, 1) + roll_xy(mid, 0, -1))


def edge_state(sx, gx, mx, cx, sm, cf, i):
    conc = gx[0, i]
    for j in range(1, NG):
        conc = conc + gx[j, i]
    cx[i] = conc
    solid = sx[i] > 0.5
    sm[i] = jnp.where(solid, mx[i], 0.0)
    cf[i] = jnp.where(solid, 0.0, conc)


def collide_plane(fx, gx, sx, cx, sm, fs, gs, i):
    solid = sx[i] > 0.5
    f = [fx[q, i] for q in range(NF)]
    density = f[0]
    for q in range(1, NF):
        density = density + f[q]
    moments = []
    for axis in range(3):
        total = None
        for q, vel in enumerate(flow_vel):
            if vel[axis] == 0:
                continue
            term = f[q] if vel[axis] > 0 else -f[q]
            total = term if total is None else total + term
        moments.append(total)
    inv = 1.0 / density
    vel_x, vel_y, vel_z = (m * inv for m in moments)
    speed_term = 1.0 - 1.5 * (vel_x * vel_x + vel_y * vel_y + vel_z * vel_z)
    weighted = {}
    for w in set(flow_weight):
        weighted[w] = w * density
    comps = (vel_x, vel_y, vel_z)

    def along(vel):
        total = None
        for axis in range(3):
            if vel[axis] == 0:
                continue
            term = comps[axis] if vel[axis] > 0 else -comps[axis]
            total = term if total is None else total + term
        return total

    for q, vel in enumerate(flow_vel):
        cu = along(vel)
        if cu is None:
            poly = speed_term
        else:
            poly = speed_term + cu * (3.0 + 4.5 * cu)
        equilibrium = weighted[flow_weight[q]] * poly
        relaxed = f[q] - (f[q] - equilibrium) * (1.0 / relax_flow)
        if vel[2]:
            relaxed = relaxed + (3.0 * flow_weight[q] * vel[2] * body_force) * density
        fs[q, i] = jnp.where(solid, f[q], relaxed)
    conc = cx[i]
    sink = (react_rate * conc) * face_sum(sm, i)
    for j, vel in enumerate(acid_vel):
        g = gx[j, i]
        cu = along(vel)
        base = acid_weight[j] * conc
        equilibrium = base if cu is None else base * (1.0 + 4.0 * cu)
        relaxed = g - (g - equilibrium) * (1.0 / relax_acid) - acid_weight[j] * sink
        gs[j, i] = jnp.where(solid, g, relaxed)


def dissolve_plane(sx, mx_src, cf, mx_dst, i):
    solid = sx[i] > 0.5
    mineral = mx_src[i]
    loss = (dissolve_rate * react_rate) * mineral * face_sum(cf, i)
    mx_dst[i] = jnp.where(solid, mineral - loss, mineral)


def stream_plane(fs, gs, sx, fdst, gdst, i):
    solid = sx[i] > 0.5
    masks = {}
    for q, vel in enumerate(flow_vel):
        cx, cy, cz = vel
        if vel == (0, 0, 0):
            fdst[q, i] = fs[q, i]
            continue
        opp = flow_vel.index((-cx, -cy, -cz))
        src = i - cz
        pulled = roll_xy(fs[q, src], cx, cy)
        blocked = roll_xy(sx[src], cx, cy) > 0.5
        masks[vel] = blocked
        arrived = jnp.where(blocked, fs[opp, i], pulled)
        fdst[q, i] = jnp.where(solid, fs[q, i], arrived)
    for j, vel in enumerate(acid_vel):
        cx, cy, cz = vel
        if vel == (0, 0, 0):
            gdst[j, i] = gs[j, i]
            continue
        opp = acid_vel.index((-cx, -cy, -cz))
        pulled = roll_xy(gs[j, i - cz], cx, cy)
        arrived = jnp.where(masks[vel], gs[opp, i], pulled)
        gdst[j, i] = jnp.where(solid, gs[j, i], arrived)


def loop(lo, hi, fn):
    def body(i, carry):
        fn(i)
        return carry

    lax.fori_loop(lo, hi, body, 0)


def main_kernel(
    mv, pop, sol, mnr, sld, hlo, hhi,
    out_f, out_g, out_m, out_s, send_lo, send_hi,
    fx, gx, fs, gs, mx, m1, sx, cx, sm, cf, sem, osem,
):
    planes = sld.shape[0]
    ext = planes + 2 * HALO
    top = HALO + planes
    fill = [
        (pop, fx.at[:, HALO:top]),
        (sol, gx.at[:, HALO:top]),
        (mnr, mx.at[HALO:top]),
        (hlo.at[0:NF], fx.at[:, 0:HALO]),
        (hlo.at[NF:NF + NG], gx.at[:, 0:HALO]),
        (hlo.at[NF + NG], mx.at[0:HALO]),
        (hlo.at[NF + NG + 1], sx.at[0:HALO]),
        (hhi.at[0:NF], fx.at[:, top:ext]),
        (hhi.at[NF:NF + NG], gx.at[:, top:ext]),
        (hhi.at[NF + NG], mx.at[top:ext]),
        (hhi.at[NF + NG + 1], sx.at[top:ext]),
    ]
    copies = [pltpu.make_async_copy(s, d, sem.at[k]) for k, (s, d) in enumerate(fill)]
    for c in copies:
        c.start()
    sx[HALO:top] = sld[...].astype(jnp.float32)
    for c in copies:
        c.wait()

    loop(0, ext, lambda i: edge_state(sx, gx, mx, cx, sm, cf, i))

    def step1(i):
        dissolve_plane(sx, mx, cf, m1, i)
        collide_plane(fx, gx, sx, cx, sm, fs, gs, i)

    loop(1, ext - 1, step1)
    loop(2, ext - 2, lambda i: stream_plane(fs, gs, sx, fx, gx, i))

    loop(1, ext - 1, lambda i: edge_state(sx, gx, m1, cx, sm, cf, i))

    def step2(i):
        dissolve_plane(sx, m1, cf, mx, i)
        collide_plane(fx, gx, sx, cx, sm, fs, gs, i)

    loop(2, ext - 2, step2)
    loop(HALO, top, lambda i: stream_plane(fs, gs, sx, fx, gx, i))

    from_low, send_low, send_high = mv[0], mv[1], mv[2]
    outs = []
    for k, (lo, dst) in enumerate(((HALO, send_lo), (top - HALO, send_hi))):
        parts = [
            (fx.at[:, lo:lo + HALO], dst.at[0:NF]),
            (gx.at[:, lo:lo + HALO], dst.at[NF:NF + NG]),
            (mx.at[lo:lo + HALO], dst.at[NF + NG]),
            (sx.at[lo:lo + HALO], dst.at[NF + NG + 1]),
        ]
        for m, (s, d) in enumerate(parts):
            outs.append(pltpu.make_async_copy(s, d, osem.at[k, m]))
    for c in outs:
        c.start()

    def plane_copies(p):
        slot = p - send_low + from_low
        return [
            pltpu.make_async_copy(fx.at[:, HALO + p], out_f.at[:, slot], osem.at[2 + p, 0]),
            pltpu.make_async_copy(gx.at[:, HALO + p], out_g.at[:, slot], osem.at[2 + p, 1]),
            pltpu.make_async_copy(mx.at[HALO + p], out_m.at[slot], osem.at[2 + p, 2]),
            pltpu.make_async_copy(sld.at[p], out_s.at[slot], osem.at[2 + p, 3]),
        ]

    for p in range(planes):
        @pl.when((p >= send_low) & (p < planes - send_high))
        def _():
            for c in plane_copies(p):
                c.start()

    for c in outs:
        c.wait()
    for p in range(planes):
        @pl.when((p >= send_low) & (p < planes - send_high))
        def _():
            for c in plane_copies(p):
                c.wait()


def fill_kernel(
    mv, rlo, rhi, f_in, g_in, m_in, s_in,
    out_f, out_g, out_m, out_s,
    zf, zi, slo, shi, sem,
):
    from_low, send_low, send_high, from_high = mv[0], mv[1], mv[2], mv[3]
    planes = mv[4]
    cap = out_s.shape[0]
    kept_end = from_low + planes - send_low - send_high
    zf[...] = jnp.zeros(zf.shape, zf.dtype)
    zi[...] = jnp.zeros(zi.shape, zi.dtype)
    slo[...] = (rlo[NF + NG + 1] > 0.5).astype(jnp.int32)
    shi[...] = (rhi[NF + NG + 1] > 0.5).astype(jnp.int32)

    def plane_from(buf, ints, idx, s):
        return [
            pltpu.make_async_copy(buf.at[0:NF, idx], out_f.at[:, s], sem.at[s, 0]),
            pltpu.make_async_copy(buf.at[NF:NF + NG, idx], out_g.at[:, s], sem.at[s, 1]),
            pltpu.make_async_copy(buf.at[NF + NG, idx], out_m.at[s], sem.at[s, 2]),
            pltpu.make_async_copy(ints.at[idx], out_s.at[s], sem.at[s, 3]),
        ]

    def zero_plane(s):
        return [
            pltpu.make_async_copy(zf, out_f.at[:, s], sem.at[s, 0]),
            pltpu.make_async_copy(zf.at[0:NG], out_g.at[:, s], sem.at[s, 1]),
            pltpu.make_async_copy(zf.at[0], out_m.at[s], sem.at[s, 2]),
            pltpu.make_async_copy(zi, out_s.at[s], sem.at[s, 3]),
        ]

    def cases(s):
        lo_idx = jnp.clip(HALO - from_low + s, 0, HALO - 1)
        hi_idx = jnp.clip(s - kept_end, 0, HALO - 1)
        return [
            (s < from_low, lambda: plane_from(rlo, slo, lo_idx, s)),
            ((s >= kept_end) & (s < kept_end + from_high), lambda: plane_from(rhi, shi, hi_idx, s)),
            (s >= kept_end + from_high, lambda: zero_plane(s)),
        ]

    for s in range(cap):
        for cond, make in cases(s):
            @pl.when(cond)
            def _():
                for c in make():
                    c.start()
    for s in range(cap):
        for cond, make in cases(s):
            @pl.when(cond)
            def _():
                for c in make():
                    c.wait()


def shards(populations, solute, mineral, solid, plane_moves):
    planes = populations.shape[1]
    cap = planes + 2 * MOVE_MOST
    ext = planes + 2 * HALO
    count = lax.axis_size("blk")
    forward = [(i, (i + 1) % count) for i in range(count)]
    backward = [(i, (i - 1) % count) for i in range(count)]

    def edge(lo):
        return jnp.concatenate(
            [
                populations[:, lo:lo + HALO],
                solute[:, lo:lo + HALO],
                mineral[None, lo:lo + HALO],
                solid[None, lo:lo + HALO].astype(jnp.float32),
            ],
            axis=0,
        )

    halo_lo = lax.ppermute(edge(planes - HALO), "blk", forward)
    halo_hi = lax.ppermute(edge(0), "blk", backward)

    me = lax.axis_index("blk")
    from_low = plane_moves[jnp.mod(me - 1, count), 1]
    send_low = plane_moves[me, 0]
    send_high = plane_moves[me, 1]
    from_high = plane_moves[jnp.mod(me + 1, count), 0]
    mv = jnp.stack([from_low, send_low, send_high, from_high, jnp.int32(planes)]).astype(jnp.int32)

    plane = populations.shape[2:]
    f32 = jnp.float32
    any_spec = pl.BlockSpec(memory_space=pl.ANY)
    vmem = pl.BlockSpec(memory_space=pltpu.VMEM)
    smem = pl.BlockSpec(memory_space=pltpu.SMEM)
    out_f, out_g, out_m, out_s, send_lo, send_hi = pl.pallas_call(
        main_kernel,
        out_shape=(
            jax.ShapeDtypeStruct((NF, cap) + plane, f32),
            jax.ShapeDtypeStruct((NG, cap) + plane, f32),
            jax.ShapeDtypeStruct((cap,) + plane, f32),
            jax.ShapeDtypeStruct((cap,) + plane, jnp.int32),
            jax.ShapeDtypeStruct((NC, HALO) + plane, f32),
            jax.ShapeDtypeStruct((NC, HALO) + plane, f32),
        ),
        in_specs=[smem, any_spec, any_spec, any_spec, vmem, any_spec, any_spec],
        out_specs=[any_spec] * 6,
        scratch_shapes=[
            pltpu.VMEM((NF, ext) + plane, f32),
            pltpu.VMEM((NG, ext) + plane, f32),
            pltpu.VMEM((NF, ext) + plane, f32),
            pltpu.VMEM((NG, ext) + plane, f32),
            pltpu.VMEM((ext,) + plane, f32),
            pltpu.VMEM((ext,) + plane, f32),
            pltpu.VMEM((ext,) + plane, f32),
            pltpu.VMEM((ext,) + plane, f32),
            pltpu.VMEM((ext,) + plane, f32),
            pltpu.VMEM((ext,) + plane, f32),
            pltpu.SemaphoreType.DMA((11,)),
            pltpu.SemaphoreType.DMA((2 + planes, 4)),
        ],
        compiler_params=pltpu.CompilerParams(vmem_limit_bytes=100 * 1024 * 1024 // 2),
    )(mv, populations, solute, mineral, solid, halo_lo, halo_hi)

    recv_lo = lax.ppermute(send_hi, "blk", forward)
    recv_hi = lax.ppermute(send_lo, "blk", backward)

    out_f, out_g, out_m, out_s = pl.pallas_call(
        fill_kernel,
        out_shape=(
            jax.ShapeDtypeStruct((NF, cap) + plane, f32),
            jax.ShapeDtypeStruct((NG, cap) + plane, f32),
            jax.ShapeDtypeStruct((cap,) + plane, f32),
            jax.ShapeDtypeStruct((cap,) + plane, jnp.int32),
        ),
        in_specs=[smem, vmem, vmem, any_spec, any_spec, any_spec, any_spec],
        out_specs=[any_spec] * 4,
        scratch_shapes=[
            pltpu.VMEM((NF,) + plane, f32),
            pltpu.VMEM(plane, jnp.int32),
            pltpu.VMEM((HALO,) + plane, jnp.int32),
            pltpu.VMEM((HALO,) + plane, jnp.int32),
            pltpu.SemaphoreType.DMA((cap, 4)),
        ],
        input_output_aliases={3: 0, 4: 1, 5: 2, 6: 3},
    )(mv, recv_lo, recv_hi, out_f, out_g, out_m, out_s)
    return out_f, out_g, out_m, out_s


def solution(mesh):
    return jax.shard_map(
        shards,
        mesh=mesh,
        in_specs=(
            P(None, "blk", None, None),
            P(None, "blk", None, None),
            P("blk", None, None),
            P("blk", None, None),
            P(),
        ),
        out_specs=(
            P(None, "blk", None, None),
            P(None, "blk", None, None),
            P("blk", None, None),
            P("blk", None, None),
        ),
        check_vma=False,
    )
```

```python
import functools

import jax
import jax.numpy as jnp
from jax import lax
from jax.experimental import pallas as pl
from jax.experimental.pallas import tpu as pltpu
from jax.sharding import PartitionSpec as P

MOVE_MOST = 3
HALO = 3

flow_vel = [
    (0, 0, 1),
    (1, 0, 1),
    (-1, 0, 1),
    (0, 1, 1),
    (0, -1, 1),
    (0, 0, -1),
    (1, 0, -1),
    (-1, 0, -1),
    (0, 1, -1),
    (0, -1, -1),
    (0, 0, 0),
    (1, 0, 0),
    (-1, 0, 0),
    (0, 1, 0),
    (0, -1, 0),
    (1, 1, 0),
    (-1, -1, 0),
    (1, -1, 0),
    (-1, 1, 0),
]
flow_weight = [
    1.0 / 18,
    1.0 / 36,
    1.0 / 36,
    1.0 / 36,
    1.0 / 36,
    1.0 / 18,
    1.0 / 36,
    1.0 / 36,
    1.0 / 36,
    1.0 / 36,
    1.0 / 3,
    1.0 / 18,
    1.0 / 18,
    1.0 / 18,
    1.0 / 18,
    1.0 / 36,
    1.0 / 36,
    1.0 / 36,
    1.0 / 36,
]
acid_vel = [(0, 0, 1), (0, 0, -1), (0, 0, 0), (1, 0, 0), (-1, 0, 0), (0, 1, 0), (0, -1, 0)]
acid_weight = [0.125, 0.125, 0.25, 0.125, 0.125, 0.125, 0.125]
relax_flow = 1.25
relax_acid = 0.8
body_force = 0.001
react_rate = 0.1
dissolve_rate = 0.5

NF = len(flow_vel)
NG = len(acid_vel)


def roll_xy(a, cx, cy):
    if cx:
        a = pltpu.roll(a, cx % a.shape[0], 0)
    if cy:
        a = pltpu.roll(a, cy % a.shape[1], 1)
    return a


def face_sum(ref, i):
    mid = ref[i]
    total = ref[i - 1] + ref[i + 1]
    total = total + (roll_xy(mid, 1, 0) + roll_xy(mid, -1, 0))
    return total + (roll_xy(mid, 0, 1) + roll_xy(mid, 0, -1))


def edge_state(sx, gx, mx, cx, sm, cf, i):
    conc = gx[0, i]
    for j in range(1, NG):
        conc = conc + gx[j, i]
    cx[i] = conc
    solid = sx[i] > 0.5
    sm[i] = jnp.where(solid, mx[i], 0.0)
    cf[i] = jnp.where(solid, 0.0, conc)


def collide_plane(fx, gx, sx, cx, sm, fs, gs, i):
    solid = sx[i] > 0.5
    f = [fx[q, i] for q in range(NF)]
    density = f[0]
    for q in range(1, NF):
        density = density + f[q]
    moments = []
    for axis in range(3):
        total = None
        for q, vel in enumerate(flow_vel):
            if vel[axis] == 0:
                continue
            term = f[q] if vel[axis] > 0 else -f[q]
            total = term if total is None else total + term
        moments.append(total)
    inv = 1.0 / density
    vel_x, vel_y, vel_z = (m * inv for m in moments)
    speed_term = 1.0 - 1.5 * (vel_x * vel_x + vel_y * vel_y + vel_z * vel_z)
    weighted = {}
    for w in set(flow_weight):
        weighted[w] = w * density
    comps = (vel_x, vel_y, vel_z)

    def along(vel):
        total = None
        for axis in range(3):
            if vel[axis] == 0:
                continue
            term = comps[axis] if vel[axis] > 0 else -comps[axis]
            total = term if total is None else total + term
        return total

    for q, vel in enumerate(flow_vel):
        cu = along(vel)
        if cu is None:
            poly = speed_term
        else:
            poly = speed_term + cu * (3.0 + 4.5 * cu)
        equilibrium = weighted[flow_weight[q]] * poly
        relaxed = f[q] - (f[q] - equilibrium) * (1.0 / relax_flow)
        if vel[2]:
            relaxed = relaxed + (3.0 * flow_weight[q] * vel[2] * body_force) * density
        fs[q, i] = jnp.where(solid, f[q], relaxed)
    conc = cx[i]
    sink = (react_rate * conc) * face_sum(sm, i)
    for j, vel in enumerate(acid_vel):
        g = gx[j, i]
        cu = along(vel)
        base = acid_weight[j] * conc
        equilibrium = base if cu is None else base * (1.0 + 4.0 * cu)
        relaxed = g - (g - equilibrium) * (1.0 / relax_acid) - acid_weight[j] * sink
        gs[j, i] = jnp.where(solid, g, relaxed)


def dissolve_plane(sx, mx_src, cf, mx_dst, i):
    solid = sx[i] > 0.5
    mineral = mx_src[i]
    loss = (dissolve_rate * react_rate) * mineral * face_sum(cf, i)
    mx_dst[i] = jnp.where(solid, mineral - loss, mineral)


def stream_plane(fs, gs, sx, fdst, gdst, i):
    solid = sx[i] > 0.5
    masks = {}
    for q, vel in enumerate(flow_vel):
        cx, cy, cz = vel
        if vel == (0, 0, 0):
            fdst[q, i] = fs[q, i]
            continue
        opp = flow_vel.index((-cx, -cy, -cz))
        src = i - cz
        pulled = roll_xy(fs[q, src], cx, cy)
        blocked = roll_xy(sx[src], cx, cy) > 0.5
        masks[vel] = blocked
        arrived = jnp.where(blocked, fs[opp, i], pulled)
        fdst[q, i] = jnp.where(solid, fs[q, i], arrived)
    for j, vel in enumerate(acid_vel):
        cx, cy, cz = vel
        if vel == (0, 0, 0):
            gdst[j, i] = gs[j, i]
            continue
        opp = acid_vel.index((-cx, -cy, -cz))
        pulled = roll_xy(gs[j, i - cz], cx, cy)
        arrived = jnp.where(masks[vel], gs[opp, i], pulled)
        gdst[j, i] = jnp.where(solid, gs[j, i], arrived)


def loop(lo, hi, fn):
    def body(i, carry):
        fn(i)
        return carry

    lax.fori_loop(lo, hi, body, 0)


UP_Q = [q for q, vel in enumerate(flow_vel) if vel[2] == 1]
DOWN_Q = [q for q, vel in enumerate(flow_vel) if vel[2] == -1]
UP_J = acid_vel.index((0, 0, 1))
DOWN_J = acid_vel.index((0, 0, -1))
NFLUX = 3 + 2 * (len(UP_Q) + 1) + 2


def flux_kernel(pop, sol, mnr, sld, up, down, fs, gs, f1, g1, m1, sx, cx, sm, cf):
    planes = sld.shape[0]
    hi, lo = planes - HALO - 1, HALO
    sx[...] = sld[...].astype(jnp.float32)
    loop(lo - 2, hi + 3, lambda i: edge_state(sx, sol, mnr, cx, sm, cf, i))

    def step1(i):
        dissolve_plane(sx, mnr, cf, m1, i)
        collide_plane(pop, sol, sx, cx, sm, fs, gs, i)

    loop(lo - 1, hi + 2, step1)
    for dst, i, qs, j in ((up, hi, UP_Q, UP_J), (down, lo, DOWN_Q, DOWN_J)):
        dst[0] = sx[i]
        dst[1] = sm[i]
        dst[2] = cf[i]
        for n, q in enumerate(qs):
            dst[3 + n] = fs[q, i]
        dst[3 + len(qs)] = gs[j, i]
    loop(lo, hi + 1, lambda i: stream_plane(fs, gs, sx, f1, g1, i))
    for i in range(lo - 1, hi + 2):
        sm[i] = jnp.where(sx[i] > 0.5, m1[i], 0.0)
    for i in range(lo, hi + 1):
        conc = g1[0, i]
        for j in range(1, NG):
            conc = conc + g1[j, i]
        cx[i] = conc
        cf[i] = jnp.where(sx[i] > 0.5, 0.0, conc)
    loop(lo, hi + 1, lambda i: collide_plane(f1, g1, sx, cx, sm, fs, gs, i))
    base = 4 + len(UP_Q)
    for dst, i, qs, j in ((up, hi, UP_Q, UP_J), (down, lo, DOWN_Q, DOWN_J)):
        dst[base] = sm[i]
        dst[base + 1] = cf[i]
        for n, q in enumerate(qs):
            dst[base + 2 + n] = fs[q, i]
        dst[base + 2 + len(qs)] = gs[j, i]


def set_bounds(flo, fhi, sm, cf, fs, gs, last, base):
    sm[0] = flo[base]
    cf[0] = flo[base + 1]
    sm[last] = fhi[base]
    cf[last] = fhi[base + 1]

    def posts():
        for n, q in enumerate(UP_Q):
            fs[q, 0] = flo[base + 2 + n]
        gs[UP_J, 0] = flo[base + 2 + len(UP_Q)]
        for n, q in enumerate(DOWN_Q):
            fs[q, last] = fhi[base + 2 + n]
        gs[DOWN_J, last] = fhi[base + 2 + len(DOWN_Q)]

    return posts


def main_kernel(
    mv, pop, sol, mnr, sld, hlo, hhi, flo, fhi,
    out_f, out_g, out_m, out_s,
    fx, gx, fs, gs, mx, m1, sx, si, cx, sm, cf, zf, zi, sem, osem,
):
    planes = sld.shape[0]
    cap = out_s.shape[0]
    last = planes + 2 * HALO + 1
    own = HALO + 1
    top = own + planes
    fill = [
        (pop, fx.at[:, own:top]),
        (sol, gx.at[:, own:top]),
        (mnr, mx.at[own:top]),
        (hlo.at[0:NF], fx.at[:, 1:own]),
        (hlo.at[NF:NF + NG], gx.at[:, 1:own]),
        (hlo.at[NF + NG], mx.at[1:own]),
        (hlo.at[NF + NG + 1], sx.at[1:own]),
        (hhi.at[0:NF], fx.at[:, top:last]),
        (hhi.at[NF:NF + NG], gx.at[:, top:last]),
        (hhi.at[NF + NG], mx.at[top:last]),
        (hhi.at[NF + NG + 1], sx.at[top:last]),
    ]
    copies = [pltpu.make_async_copy(s, d, sem.at[k]) for k, (s, d) in enumerate(fill)]
    for c in copies:
        c.start()
    sx[own:top] = sld[...].astype(jnp.float32)
    si[own:top] = sld[...]
    sx[0] = flo[0]
    sx[last] = fhi[0]
    zf[...] = jnp.zeros(zf.shape, zf.dtype)
    zi[...] = jnp.zeros(zi.shape, zi.dtype)
    for c in copies:
        c.wait()
    si[1:own] = (sx[1:own] > 0.5).astype(jnp.int32)
    si[top:last] = (sx[top:last] > 0.5).astype(jnp.int32)

    posts = set_bounds(flo, fhi, sm, cf, fs, gs, last, 1)
    loop(1, last, lambda i: edge_state(sx, gx, mx, cx, sm, cf, i))

    def step1(i):
        dissolve_plane(sx, mx, cf, m1, i)
        collide_plane(fx, gx, sx, cx, sm, fs, gs, i)

    loop(1, last, step1)
    posts()
    loop(1, last, lambda i: stream_plane(fs, gs, sx, fx, gx, i))

    posts = set_bounds(flo, fhi, sm, cf, fs, gs, last, 4 + len(UP_Q))
    loop(1, last, lambda i: edge_state(sx, gx, m1, cx, sm, cf, i))

    def step2(i):
        dissolve_plane(sx, m1, cf, mx, i)
        collide_plane(fx, gx, sx, cx, sm, fs, gs, i)

    loop(1, last, step2)
    posts()
    loop(1, last, lambda i: stream_plane(fs, gs, sx, fx, gx, i))

    from_low, send_low, send_high, from_high = mv[0], mv[1], mv[2], mv[3]
    kept_end = from_low + planes - send_low - send_high
    valid_end = kept_end + from_high

    def slot_copies(s, valid):
        if valid:
            plane = s - from_low + own
            plane = plane + jnp.where(s >= from_low, send_low, 0)
            plane = plane + jnp.where(s >= kept_end, send_high, 0)
            plane = jnp.clip(plane, 1, last - 1)
            srcs = (fx.at[:, plane], gx.at[:, plane], mx.at[plane], si.at[plane])
        else:
            srcs = (zf, zf.at[0:NG], zf.at[0], zi)
        dsts = (out_f.at[:, s], out_g.at[:, s], out_m.at[s], out_s.at[s])
        return [pltpu.make_async_copy(a, b, osem.at[s, k]) for k, (a, b) in enumerate(zip(srcs, dsts))]

    for phase in ("start", "wait"):
        for s in range(cap):
            for valid in (True, False):
                cond = (s < valid_end) if valid else (s >= valid_end)

                @pl.when(cond)
                def _():
                    for c in slot_copies(s, valid):
                        getattr(c, phase)()


def shards(populations, solute, mineral, solid, plane_moves):
    planes = populations.shape[1]
    cap = planes + 2 * MOVE_MOST
    ext = planes + 2 * HALO + 2
    count = lax.axis_size("blk")
    forward = [(i, (i + 1) % count) for i in range(count)]
    backward = [(i, (i - 1) % count) for i in range(count)]

    def edge(lo):
        return jnp.concatenate(
            [
                populations[:, lo:lo + HALO],
                solute[:, lo:lo + HALO],
                mineral[None, lo:lo + HALO],
                solid[None, lo:lo + HALO].astype(jnp.float32),
            ],
            axis=0,
        )

    halo_lo = lax.ppermute(edge(planes - HALO), "blk", forward)
    halo_hi = lax.ppermute(edge(0), "blk", backward)

    plane = populations.shape[2:]
    f32 = jnp.float32
    any_spec = pl.BlockSpec(memory_space=pl.ANY)
    vmem = pl.BlockSpec(memory_space=pltpu.VMEM)
    smem = pl.BlockSpec(memory_space=pltpu.SMEM)

    up, down = pl.pallas_call(
        flux_kernel,
        out_shape=(
            jax.ShapeDtypeStruct((NFLUX,) + plane, f32),
            jax.ShapeDtypeStruct((NFLUX,) + plane, f32),
        ),
        in_specs=[vmem] * 4,
        out_specs=[vmem] * 2,
        scratch_shapes=[
            pltpu.VMEM((NF, planes) + plane, f32),
            pltpu.VMEM((NG, planes) + plane, f32),
            pltpu.VMEM((NF, planes) + plane, f32),
            pltpu.VMEM((NG, planes) + plane, f32),
        ]
        + [pltpu.VMEM((planes,) + plane, f32)] * 5,
    )(populations, solute, mineral, solid)
    flux_lo = lax.ppermute(up, "blk", forward)
    flux_hi = lax.ppermute(down, "blk", backward)

    me = lax.axis_index("blk")
    from_low = plane_moves[jnp.mod(me - 1, count), 1]
    send_low = plane_moves[me, 0]
    send_high = plane_moves[me, 1]
    from_high = plane_moves[jnp.mod(me + 1, count), 0]
    mv = jnp.stack([from_low, send_low, send_high, from_high]).astype(jnp.int32)

    return pl.pallas_call(
        main_kernel,
        out_shape=(
            jax.ShapeDtypeStruct((NF, cap) + plane, f32),
            jax.ShapeDtypeStruct((NG, cap) + plane, f32),
            jax.ShapeDtypeStruct((cap,) + plane, f32),
            jax.ShapeDtypeStruct((cap,) + plane, jnp.int32),
        ),
        in_specs=[smem, any_spec, any_spec, any_spec, vmem, any_spec, any_spec, vmem, vmem],
        out_specs=[any_spec] * 4,
        scratch_shapes=[
            pltpu.VMEM((NF, ext) + plane, f32),
            pltpu.VMEM((NG, ext) + plane, f32),
            pltpu.VMEM((NF, ext) + plane, f32),
            pltpu.VMEM((NG, ext) + plane, f32),
            pltpu.VMEM((ext,) + plane, f32),
            pltpu.VMEM((ext,) + plane, f32),
            pltpu.VMEM((ext,) + plane, f32),
            pltpu.VMEM((ext,) + plane, jnp.int32),
            pltpu.VMEM((ext,) + plane, f32),
            pltpu.VMEM((ext,) + plane, f32),
            pltpu.VMEM((ext,) + plane, f32),
            pltpu.VMEM((NF,) + plane, f32),
            pltpu.VMEM(plane, jnp.int32),
            pltpu.SemaphoreType.DMA((11,)),
            pltpu.SemaphoreType.DMA((cap, 4)),
        ],
        compiler_params=pltpu.CompilerParams(vmem_limit_bytes=50 * 1024 * 1024),
    )(mv, populations, solute, mineral, solid, halo_lo, halo_hi, flux_lo, flux_hi)


def solution(mesh):
    return jax.shard_map(
        shards,
        mesh=mesh,
        in_specs=(
            P(None, "blk", None, None),
            P(None, "blk", None, None),
            P("blk", None, None),
            P("blk", None, None),
            P(),
        ),
        out_specs=(
            P(None, "blk", None, None),
            P(None, "blk", None, None),
            P("blk", None, None),
            P("blk", None, None),
        ),
        check_vma=False,
    )
```

```python
import functools

import jax
import jax.numpy as jnp
from jax import lax
from jax.experimental import pallas as pl
from jax.experimental.pallas import tpu as pltpu
from jax.sharding import PartitionSpec as P

MOVE_MOST = 3
HALO = 3

flow_vel = [
    (0, 0, 1),
    (1, 0, 1),
    (-1, 0, 1),
    (0, 1, 1),
    (0, -1, 1),
    (0, 0, -1),
    (1, 0, -1),
    (-1, 0, -1),
    (0, 1, -1),
    (0, -1, -1),
    (0, 0, 0),
    (1, 0, 0),
    (-1, 0, 0),
    (0, 1, 0),
    (0, -1, 0),
    (1, 1, 0),
    (-1, -1, 0),
    (1, -1, 0),
    (-1, 1, 0),
]
flow_weight = [
    1.0 / 18,
    1.0 / 36,
    1.0 / 36,
    1.0 / 36,
    1.0 / 36,
    1.0 / 18,
    1.0 / 36,
    1.0 / 36,
    1.0 / 36,
    1.0 / 36,
    1.0 / 3,
    1.0 / 18,
    1.0 / 18,
    1.0 / 18,
    1.0 / 18,
    1.0 / 36,
    1.0 / 36,
    1.0 / 36,
    1.0 / 36,
]
acid_vel = [(0, 0, 1), (0, 0, -1), (0, 0, 0), (1, 0, 0), (-1, 0, 0), (0, 1, 0), (0, -1, 0)]
acid_weight = [0.125, 0.125, 0.25, 0.125, 0.125, 0.125, 0.125]
relax_flow = 1.25
relax_acid = 0.8
body_force = 0.001
react_rate = 0.1
dissolve_rate = 0.5

NF = len(flow_vel)
NG = len(acid_vel)


def roll_xy(a, cx, cy):
    if cx:
        a = pltpu.roll(a, cx % a.shape[0], 0)
    if cy:
        a = pltpu.roll(a, cy % a.shape[1], 1)
    return a


def face_sum(ref, i):
    mid = ref[i]
    total = ref[i - 1] + ref[i + 1]
    total = total + (roll_xy(mid, 1, 0) + roll_xy(mid, -1, 0))
    return total + (roll_xy(mid, 0, 1) + roll_xy(mid, 0, -1))


def edge_state(sx, gx, mx, cx, sm, cf, i):
    conc = gx[0, i]
    for j in range(1, NG):
        conc = conc + gx[j, i]
    cx[i] = conc
    solid = sx[i] > 0.5
    sm[i] = jnp.where(solid, mx[i], 0.0)
    cf[i] = jnp.where(solid, 0.0, conc)


def collide_plane(fx, gx, sx, cx, sm, fs, gs, i):
    solid = sx[i] > 0.5
    f = [fx[q, i] for q in range(NF)]
    density = f[0]
    for q in range(1, NF):
        density = density + f[q]
    moments = []
    for axis in range(3):
        total = None
        for q, vel in enumerate(flow_vel):
            if vel[axis] == 0:
                continue
            term = f[q] if vel[axis] > 0 else -f[q]
            total = term if total is None else total + term
        moments.append(total)
    inv = 1.0 / density
    vel_x, vel_y, vel_z = (m * inv for m in moments)
    speed_term = 1.0 - 1.5 * (vel_x * vel_x + vel_y * vel_y + vel_z * vel_z)
    weighted = {}
    for w in set(flow_weight):
        weighted[w] = w * density
    comps = (vel_x, vel_y, vel_z)

    def along(vel):
        total = None
        for axis in range(3):
            if vel[axis] == 0:
                continue
            term = comps[axis] if vel[axis] > 0 else -comps[axis]
            total = term if total is None else total + term
        return total

    for q, vel in enumerate(flow_vel):
        cu = along(vel)
        if cu is None:
            poly = speed_term
        else:
            poly = speed_term + cu * (3.0 + 4.5 * cu)
        equilibrium = weighted[flow_weight[q]] * poly
        relaxed = f[q] - (f[q] - equilibrium) * (1.0 / relax_flow)
        if vel[2]:
            relaxed = relaxed + (3.0 * flow_weight[q] * vel[2] * body_force) * density
        fs[q, i] = jnp.where(solid, f[q], relaxed)
    conc = cx[i]
    sink = (react_rate * conc) * face_sum(sm, i)
    for j, vel in enumerate(acid_vel):
        g = gx[j, i]
        cu = along(vel)
        base = acid_weight[j] * conc
        equilibrium = base if cu is None else base * (1.0 + 4.0 * cu)
        relaxed = g - (g - equilibrium) * (1.0 / relax_acid) - acid_weight[j] * sink
        gs[j, i] = jnp.where(solid, g, relaxed)


def dissolve_plane(sx, mx_src, cf, mx_dst, i):
    solid = sx[i] > 0.5
    mineral = mx_src[i]
    loss = (dissolve_rate * react_rate) * mineral * face_sum(cf, i)
    mx_dst[i] = jnp.where(solid, mineral - loss, mineral)


def stream_plane(fs, gs, sx, fdst, gdst, i):
    solid = sx[i] > 0.5
    masks = {}
    for q, vel in enumerate(flow_vel):
        cx, cy, cz = vel
        if vel == (0, 0, 0):
            fdst[q, i] = fs[q, i]
            continue
        opp = flow_vel.index((-cx, -cy, -cz))
        src = i - cz
        pulled = roll_xy(fs[q, src], cx, cy)
        blocked = roll_xy(sx[src], cx, cy) > 0.5
        masks[vel] = blocked
        arrived = jnp.where(blocked, fs[opp, i], pulled)
        fdst[q, i] = jnp.where(solid, fs[q, i], arrived)
    for j, vel in enumerate(acid_vel):
        cx, cy, cz = vel
        if vel == (0, 0, 0):
            gdst[j, i] = gs[j, i]
            continue
        opp = acid_vel.index((-cx, -cy, -cz))
        pulled = roll_xy(gs[j, i - cz], cx, cy)
        arrived = jnp.where(masks[vel], gs[opp, i], pulled)
        gdst[j, i] = jnp.where(solid, gs[j, i], arrived)


def loop(lo, hi, fn):
    def body(i, carry):
        fn(i)
        return carry

    lax.fori_loop(lo, hi, body, 0)


UP_Q = [q for q, vel in enumerate(flow_vel) if vel[2] == 1]
DOWN_Q = [q for q, vel in enumerate(flow_vel) if vel[2] == -1]
UP_J = acid_vel.index((0, 0, 1))
DOWN_J = acid_vel.index((0, 0, -1))
NFLUX = 3 + 2 * (len(UP_Q) + 1) + 2


def flux_kernel(pop, sol, mnr, sld, up, down, fs, gs, f1, g1, m1, sx, cx, sm, cf):
    planes = sld.shape[0]
    hi, lo = planes - HALO - 1, HALO
    sx[...] = sld[...].astype(jnp.float32)
    loop(lo - 2, hi + 3, lambda i: edge_state(sx, sol, mnr, cx, sm, cf, i))

    def step1(i):
        dissolve_plane(sx, mnr, cf, m1, i)
        collide_plane(pop, sol, sx, cx, sm, fs, gs, i)

    loop(lo - 1, hi + 2, step1)
    for dst, i, qs, j in ((up, hi, UP_Q, UP_J), (down, lo, DOWN_Q, DOWN_J)):
        dst[0] = sx[i]
        dst[1] = sm[i]
        dst[2] = cf[i]
        for n, q in enumerate(qs):
            dst[3 + n] = fs[q, i]
        dst[3 + len(qs)] = gs[j, i]
    loop(lo, hi + 1, lambda i: stream_plane(fs, gs, sx, f1, g1, i))
    for i in range(lo - 1, hi + 2):
        sm[i] = jnp.where(sx[i] > 0.5, m1[i], 0.0)
    for i in range(lo, hi + 1):
        conc = g1[0, i]
        for j in range(1, NG):
            conc = conc + g1[j, i]
        cx[i] = conc
        cf[i] = jnp.where(sx[i] > 0.5, 0.0, conc)
    loop(lo, hi + 1, lambda i: collide_plane(f1, g1, sx, cx, sm, fs, gs, i))
    base = 4 + len(UP_Q)
    for dst, i, qs, j in ((up, hi, UP_Q, UP_J), (down, lo, DOWN_Q, DOWN_J)):
        dst[base] = sm[i]
        dst[base + 1] = cf[i]
        for n, q in enumerate(qs):
            dst[base + 2 + n] = fs[q, i]
        dst[base + 2 + len(qs)] = gs[j, i]


def set_bounds(flo, fhi, sm, cf, fs, gs, last, base):
    sm[0] = flo[base]
    cf[0] = flo[base + 1]
    sm[last] = fhi[base]
    cf[last] = fhi[base + 1]

    def posts():
        for n, q in enumerate(UP_Q):
            fs[q, 0] = flo[base + 2 + n]
        gs[UP_J, 0] = flo[base + 2 + len(UP_Q)]
        for n, q in enumerate(DOWN_Q):
            fs[q, last] = fhi[base + 2 + n]
        gs[DOWN_J, last] = fhi[base + 2 + len(DOWN_Q)]

    return posts


def main_kernel(
    mv, pop, sol, mnr, sld, pop_lo, sol_lo, mnr_lo, sld_lo, pop_hi, sol_hi, mnr_hi, sld_hi, flo, fhi,
    out_f, out_g, out_m, out_s,
    fx, gx, fs, gs, mx, m1, sx, si, cx, sm, cf, zf, zi, sem, osem,
):
    planes = sld.shape[0]
    cap = out_s.shape[0]
    last = planes + 2 * HALO + 1
    own = HALO + 1
    top = own + planes
    fill = [
        (pop, fx.at[:, own:top]),
        (sol, gx.at[:, own:top]),
        (mnr, mx.at[own:top]),
        (pop_lo, fx.at[:, 1:own]),
        (sol_lo, gx.at[:, 1:own]),
        (mnr_lo, mx.at[1:own]),
        (sld_lo, si.at[1:own]),
        (pop_hi, fx.at[:, top:last]),
        (sol_hi, gx.at[:, top:last]),
        (mnr_hi, mx.at[top:last]),
        (sld_hi, si.at[top:last]),
    ]
    copies = [pltpu.make_async_copy(s, d, sem.at[k]) for k, (s, d) in enumerate(fill)]
    for c in copies:
        c.start()
    sx[own:top] = sld[...].astype(jnp.float32)
    si[own:top] = sld[...]
    sx[0] = flo[0]
    sx[last] = fhi[0]
    zf[...] = jnp.zeros(zf.shape, zf.dtype)
    zi[...] = jnp.zeros(zi.shape, zi.dtype)
    for c in copies:
        c.wait()
    sx[1:own] = si[1:own].astype(jnp.float32)
    sx[top:last] = si[top:last].astype(jnp.float32)

    posts = set_bounds(flo, fhi, sm, cf, fs, gs, last, 1)
    loop(1, last, lambda i: edge_state(sx, gx, mx, cx, sm, cf, i))

    def step1(i):
        dissolve_plane(sx, mx, cf, m1, i)
        collide_plane(fx, gx, sx, cx, sm, fs, gs, i)

    loop(1, last, step1)
    posts()
    loop(1, last, lambda i: stream_plane(fs, gs, sx, fx, gx, i))

    posts = set_bounds(flo, fhi, sm, cf, fs, gs, last, 4 + len(UP_Q))
    loop(1, last, lambda i: edge_state(sx, gx, m1, cx, sm, cf, i))

    def step2(i):
        dissolve_plane(sx, m1, cf, mx, i)
        collide_plane(fx, gx, sx, cx, sm, fs, gs, i)

    loop(1, last, step2)
    posts()
    loop(1, last, lambda i: stream_plane(fs, gs, sx, fx, gx, i))

    from_low, send_low, send_high, from_high = mv[0], mv[1], mv[2], mv[3]
    kept_end = from_low + planes - send_low - send_high
    valid_end = kept_end + from_high

    def slot_copies(s, valid):
        if valid:
            plane = s - from_low + own
            plane = plane + jnp.where(s >= from_low, send_low, 0)
            plane = plane + jnp.where(s >= kept_end, send_high, 0)
            plane = jnp.clip(plane, 1, last - 1)
            srcs = (fx.at[:, plane], gx.at[:, plane], mx.at[plane], si.at[plane])
        else:
            srcs = (zf, zf.at[0:NG], zf.at[0], zi)
        dsts = (out_f.at[:, s], out_g.at[:, s], out_m.at[s], out_s.at[s])
        return [pltpu.make_async_copy(a, b, osem.at[s, k]) for k, (a, b) in enumerate(zip(srcs, dsts))]

    for phase in ("start", "wait"):
        for s in range(cap):
            for valid in (True, False):
                cond = (s < valid_end) if valid else (s >= valid_end)

                @pl.when(cond)
                def _():
                    for c in slot_copies(s, valid):
                        getattr(c, phase)()


def shards(populations, solute, mineral, solid, plane_moves):
    planes = populations.shape[1]
    cap = planes + 2 * MOVE_MOST
    ext = planes + 2 * HALO + 2
    count = lax.axis_size("blk")
    forward = [(i, (i + 1) % count) for i in range(count)]
    backward = [(i, (i - 1) % count) for i in range(count)]

    def edge(lo):
        return (
            populations[:, lo:lo + HALO],
            solute[:, lo:lo + HALO],
            mineral[lo:lo + HALO],
            solid[lo:lo + HALO],
        )

    top_edge, bottom_edge = edge(planes - HALO), edge(0)
    halo_lo, halo_hi = [], []
    for k in range(4):
        halo_lo.append(lax.ppermute(top_edge[k], "blk", forward))
        halo_hi.append(lax.ppermute(bottom_edge[k], "blk", backward))

    plane = populations.shape[2:]
    f32 = jnp.float32
    any_spec = pl.BlockSpec(memory_space=pl.ANY)
    vmem = pl.BlockSpec(memory_space=pltpu.VMEM)
    smem = pl.BlockSpec(memory_space=pltpu.SMEM)

    up, down = pl.pallas_call(
        flux_kernel,
        out_shape=(
            jax.ShapeDtypeStruct((NFLUX,) + plane, f32),
            jax.ShapeDtypeStruct((NFLUX,) + plane, f32),
        ),
        in_specs=[vmem] * 4,
        out_specs=[vmem] * 2,
        scratch_shapes=[
            pltpu.VMEM((NF, planes) + plane, f32),
            pltpu.VMEM((NG, planes) + plane, f32),
            pltpu.VMEM((NF, planes) + plane, f32),
            pltpu.VMEM((NG, planes) + plane, f32),
        ]
        + [pltpu.VMEM((planes,) + plane, f32)] * 5,
    )(populations, solute, mineral, solid)
    flux_lo = lax.ppermute(up, "blk", forward)
    flux_hi = lax.ppermute(down, "blk", backward)

    me = lax.axis_index("blk")
    from_low = plane_moves[jnp.mod(me - 1, count), 1]
    send_low = plane_moves[me, 0]
    send_high = plane_moves[me, 1]
    from_high = plane_moves[jnp.mod(me + 1, count), 0]
    mv = jnp.stack([from_low, send_low, send_high, from_high]).astype(jnp.int32)

    return pl.pallas_call(
        main_kernel,
        out_shape=(
            jax.ShapeDtypeStruct((NF, cap) + plane, f32),
            jax.ShapeDtypeStruct((NG, cap) + plane, f32),
            jax.ShapeDtypeStruct((cap,) + plane, f32),
            jax.ShapeDtypeStruct((cap,) + plane, jnp.int32),
        ),
        in_specs=[smem, any_spec, any_spec, any_spec, vmem] + [any_spec] * 8 + [vmem, vmem],
        out_specs=[any_spec] * 4,
        scratch_shapes=[
            pltpu.VMEM((NF, ext) + plane, f32),
            pltpu.VMEM((NG, ext) + plane, f32),
            pltpu.VMEM((NF, ext) + plane, f32),
            pltpu.VMEM((NG, ext) + plane, f32),
            pltpu.VMEM((ext,) + plane, f32),
            pltpu.VMEM((ext,) + plane, f32),
            pltpu.VMEM((ext,) + plane, f32),
            pltpu.VMEM((ext,) + plane, jnp.int32),
            pltpu.VMEM((ext,) + plane, f32),
            pltpu.VMEM((ext,) + plane, f32),
            pltpu.VMEM((ext,) + plane, f32),
            pltpu.VMEM((NF,) + plane, f32),
            pltpu.VMEM(plane, jnp.int32),
            pltpu.SemaphoreType.DMA((11,)),
            pltpu.SemaphoreType.DMA((cap, 4)),
        ],
        compiler_params=pltpu.CompilerParams(vmem_limit_bytes=50 * 1024 * 1024),
    )(mv, populations, solute, mineral, solid, *halo_lo, *halo_hi, flux_lo, flux_hi)


def solution(mesh):
    return jax.shard_map(
        shards,
        mesh=mesh,
        in_specs=(
            P(None, "blk", None, None),
            P(None, "blk", None, None),
            P("blk", None, None),
            P("blk", None, None),
            P(),
        ),
        out_specs=(
            P(None, "blk", None, None),
            P(None, "blk", None, None),
            P("blk", None, None),
            P("blk", None, None),
        ),
        check_vma=False,
    )
```

```python
import functools

import jax
import jax.numpy as jnp
from jax import lax
from jax.experimental import pallas as pl
from jax.experimental.pallas import tpu as pltpu
from jax.sharding import PartitionSpec as P

MOVE_MOST = 3
HALO = 3

flow_vel = [
    (0, 0, 1),
    (1, 0, 1),
    (-1, 0, 1),
    (0, 1, 1),
    (0, -1, 1),
    (0, 0, -1),
    (1, 0, -1),
    (-1, 0, -1),
    (0, 1, -1),
    (0, -1, -1),
    (0, 0, 0),
    (1, 0, 0),
    (-1, 0, 0),
    (0, 1, 0),
    (0, -1, 0),
    (1, 1, 0),
    (-1, -1, 0),
    (1, -1, 0),
    (-1, 1, 0),
]
flow_weight = [
    1.0 / 18,
    1.0 / 36,
    1.0 / 36,
    1.0 / 36,
    1.0 / 36,
    1.0 / 18,
    1.0 / 36,
    1.0 / 36,
    1.0 / 36,
    1.0 / 36,
    1.0 / 3,
    1.0 / 18,
    1.0 / 18,
    1.0 / 18,
    1.0 / 18,
    1.0 / 36,
    1.0 / 36,
    1.0 / 36,
    1.0 / 36,
]
acid_vel = [(0, 0, 1), (0, 0, -1), (0, 0, 0), (1, 0, 0), (-1, 0, 0), (0, 1, 0), (0, -1, 0)]
acid_weight = [0.125, 0.125, 0.25, 0.125, 0.125, 0.125, 0.125]
relax_flow = 1.25
relax_acid = 0.8
body_force = 0.001
react_rate = 0.1
dissolve_rate = 0.5

NF = len(flow_vel)
NG = len(acid_vel)


def roll_xy(a, cx, cy):
    if cx:
        a = pltpu.roll(a, cx % a.shape[0], 0)
    if cy:
        a = pltpu.roll(a, cy % a.shape[1], 1)
    return a


def face_sum(ref, i):
    mid = ref[i]
    total = ref[i - 1] + ref[i + 1]
    total = total + (roll_xy(mid, 1, 0) + roll_xy(mid, -1, 0))
    return total + (roll_xy(mid, 0, 1) + roll_xy(mid, 0, -1))


def edge_state(sx, gx, mx, cx, sm, cf, i):
    conc = gx[0, i]
    for j in range(1, NG):
        conc = conc + gx[j, i]
    cx[i] = conc
    solid = sx[i] > 0.5
    sm[i] = jnp.where(solid, mx[i], 0.0)
    cf[i] = jnp.where(solid, 0.0, conc)


def collide_plane(fx, gx, sx, cx, sm, fs, gs, i):
    solid = sx[i] > 0.5
    f = [fx[q, i] for q in range(NF)]
    density = f[0]
    for q in range(1, NF):
        density = density + f[q]
    moments = []
    for axis in range(3):
        total = None
        for q, vel in enumerate(flow_vel):
            if vel[axis] == 0:
                continue
            term = f[q] if vel[axis] > 0 else -f[q]
            total = term if total is None else total + term
        moments.append(total)
    inv = 1.0 / density
    comps = [m * inv for m in moments]
    base = 1.0 - 1.5 * (comps[0] * comps[0] + comps[1] * comps[1] + comps[2] * comps[2])
    keep = 1.0 - 1.0 / relax_flow
    scaled = {}
    for w in set(flow_weight):
        scaled[w] = (w / relax_flow) * density

    def along(vel):
        total = None
        for axis in range(3):
            if vel[axis] == 0:
                continue
            term = comps[axis] if vel[axis] > 0 else -comps[axis]
            total = term if total is None else total + term
        return total

    done = set()
    for q, vel in enumerate(flow_vel):
        if q in done:
            continue
        opp = flow_vel.index(tuple(-c for c in vel))
        done |= {q, opp}
        weight = scaled[flow_weight[q]]
        if opp == q:
            fs[q, i] = jnp.where(solid, f[q], keep * f[q] + weight * base)
            continue
        cu = along(vel)
        even = base + 4.5 * (cu * cu)
        odd = 3.0 * cu
        if vel[2]:
            odd = odd + 3.0 * body_force * relax_flow * vel[2]
        for member, poly in ((q, even + odd), (opp, even - odd)):
            fs[member, i] = jnp.where(solid, f[member], keep * f[member] + weight * poly)
    conc = cx[i]
    sink = (react_rate * conc) * face_sum(sm, i)
    rate = 1.0 / relax_acid
    shared = rate * conc - sink
    slope = (4.0 * rate) * conc
    done = set()
    for j, vel in enumerate(acid_vel):
        if j in done:
            continue
        opp = acid_vel.index(tuple(-c for c in vel))
        done |= {j, opp}
        if opp == j:
            parts = ((j, shared),)
        else:
            cu = slope * along(vel)
            parts = ((j, shared + cu), (opp, shared - cu))
        for member, inner in parts:
            g = gx[member, i]
            relaxed = acid_weight[member] * inner - (rate - 1.0) * g
            gs[member, i] = jnp.where(solid, g, relaxed)


def dissolve_plane(sx, mx_src, cf, mx_dst, i):
    solid = sx[i] > 0.5
    mineral = mx_src[i]
    loss = (dissolve_rate * react_rate) * mineral * face_sum(cf, i)
    mx_dst[i] = jnp.where(solid, mineral - loss, mineral)


SHIFTS = [(cx, cy) for cx in (-1, 0, 1) for cy in (-1, 0, 1) if cx or cy]


def shift_masks(sx, bm, i):
    for c, (cx, cy) in enumerate(SHIFTS):
        bm[c, i] = roll_xy(sx[i], cx, cy)


def stream_plane(fs, gs, sx, fdst, gdst, i, bm=None):
    solid = sx[i] > 0.5
    masks = {}
    for q, vel in enumerate(flow_vel):
        cx, cy, cz = vel
        if vel == (0, 0, 0):
            fdst[q, i] = fs[q, i]
            continue
        opp = flow_vel.index((-cx, -cy, -cz))
        src = i - cz
        pulled = roll_xy(fs[q, src], cx, cy)
        if bm is None or (cx, cy) == (0, 0):
            blocked = roll_xy(sx[src], cx, cy) > 0.5
        else:
            blocked = bm[SHIFTS.index((cx, cy)), src] > 0.5
        masks[vel] = blocked
        arrived = jnp.where(blocked, fs[opp, i], pulled)
        fdst[q, i] = jnp.where(solid, fs[q, i], arrived)
    for j, vel in enumerate(acid_vel):
        cx, cy, cz = vel
        if vel == (0, 0, 0):
            gdst[j, i] = gs[j, i]
            continue
        opp = acid_vel.index((-cx, -cy, -cz))
        pulled = roll_xy(gs[j, i - cz], cx, cy)
        arrived = jnp.where(masks[vel], gs[opp, i], pulled)
        gdst[j, i] = jnp.where(solid, gs[j, i], arrived)


def loop(lo, hi, fn):
    def body(i, carry):
        fn(i)
        return carry

    lax.fori_loop(lo, hi, body, 0)


UP_Q = [q for q, vel in enumerate(flow_vel) if vel[2] == 1]
DOWN_Q = [q for q, vel in enumerate(flow_vel) if vel[2] == -1]
UP_J = acid_vel.index((0, 0, 1))
DOWN_J = acid_vel.index((0, 0, -1))
NFLUX = 3 + 2 * (len(UP_Q) + 1) + 2


def flux_kernel(pop, sol, mnr, sld, up, down, fs, gs, f1, g1, m1, sx, cx, sm, cf):
    planes = sld.shape[0]
    hi, lo = planes - HALO - 1, HALO
    sx[...] = sld[...].astype(jnp.float32)
    loop(lo - 2, hi + 3, lambda i: edge_state(sx, sol, mnr, cx, sm, cf, i))

    def step1(i):
        dissolve_plane(sx, mnr, cf, m1, i)
        collide_plane(pop, sol, sx, cx, sm, fs, gs, i)

    loop(lo - 1, hi + 2, step1)
    for dst, i, qs, j in ((up, hi, UP_Q, UP_J), (down, lo, DOWN_Q, DOWN_J)):
        dst[0] = sx[i]
        dst[1] = sm[i]
        dst[2] = cf[i]
        for n, q in enumerate(qs):
            dst[3 + n] = fs[q, i]
        dst[3 + len(qs)] = gs[j, i]
    loop(lo, hi + 1, lambda i: stream_plane(fs, gs, sx, f1, g1, i))
    for i in range(lo - 1, hi + 2):
        sm[i] = jnp.where(sx[i] > 0.5, m1[i], 0.0)
    for i in range(lo, hi + 1):
        conc = g1[0, i]
        for j in range(1, NG):
            conc = conc + g1[j, i]
        cx[i] = conc
        cf[i] = jnp.where(sx[i] > 0.5, 0.0, conc)
    loop(lo, hi + 1, lambda i: collide_plane(f1, g1, sx, cx, sm, fs, gs, i))
    base = 4 + len(UP_Q)
    for dst, i, qs, j in ((up, hi, UP_Q, UP_J), (down, lo, DOWN_Q, DOWN_J)):
        dst[base] = sm[i]
        dst[base + 1] = cf[i]
        for n, q in enumerate(qs):
            dst[base + 2 + n] = fs[q, i]
        dst[base + 2 + len(qs)] = gs[j, i]


def set_bounds(flo, fhi, sm, cf, fs, gs, last, base):
    sm[0] = flo[base]
    cf[0] = flo[base + 1]
    sm[last] = fhi[base]
    cf[last] = fhi[base + 1]

    def posts():
        for n, q in enumerate(UP_Q):
            fs[q, 0] = flo[base + 2 + n]
        gs[UP_J, 0] = flo[base + 2 + len(UP_Q)]
        for n, q in enumerate(DOWN_Q):
            fs[q, last] = fhi[base + 2 + n]
        gs[DOWN_J, last] = fhi[base + 2 + len(DOWN_Q)]

    return posts


def main_kernel(
    mv, pop, sol, mnr, sld, hlo, hhi, flo, fhi,
    out_f, out_g, out_m, out_s,
    fx, gx, fs, gs, mx, m1, sx, si, cx, sm, cf, zf, zi, bm, sem, osem,
):
    planes = sld.shape[0]
    cap = out_s.shape[0]
    last = planes + 2 * HALO + 1
    own = HALO + 1
    top = own + planes
    fill = [
        (pop, fx.at[:, own:top]),
        (sol, gx.at[:, own:top]),
        (mnr, mx.at[own:top]),
        (hlo.at[0:NF], fx.at[:, 1:own]),
        (hlo.at[NF:NF + NG], gx.at[:, 1:own]),
        (hlo.at[NF + NG], mx.at[1:own]),
        (hlo.at[NF + NG + 1], sx.at[1:own]),
        (hhi.at[0:NF], fx.at[:, top:last]),
        (hhi.at[NF:NF + NG], gx.at[:, top:last]),
        (hhi.at[NF + NG], mx.at[top:last]),
        (hhi.at[NF + NG + 1], sx.at[top:last]),
    ]
    copies = [pltpu.make_async_copy(s, d, sem.at[k]) for k, (s, d) in enumerate(fill)]
    for c in copies:
        c.start()
    sx[own:top] = sld[...].astype(jnp.float32)
    si[own:top] = sld[...]
    sx[0] = flo[0]
    sx[last] = fhi[0]
    zf[...] = jnp.zeros(zf.shape, zf.dtype)
    zi[...] = jnp.zeros(zi.shape, zi.dtype)
    for c in copies:
        c.wait()
    si[1:own] = (sx[1:own] > 0.5).astype(jnp.int32)
    si[top:last] = (sx[top:last] > 0.5).astype(jnp.int32)

    loop(0, last + 1, lambda i: shift_masks(sx, bm, i))

    posts = set_bounds(flo, fhi, sm, cf, fs, gs, last, 1)
    loop(1, last, lambda i: edge_state(sx, gx, mx, cx, sm, cf, i))

    def step1(i):
        dissolve_plane(sx, mx, cf, m1, i)
        collide_plane(fx, gx, sx, cx, sm, fs, gs, i)

    loop(1, last, step1)
    posts()
    loop(1, last, lambda i: stream_plane(fs, gs, sx, fx, gx, i, bm))

    posts = set_bounds(flo, fhi, sm, cf, fs, gs, last, 4 + len(UP_Q))
    loop(1, last, lambda i: edge_state(sx, gx, m1, cx, sm, cf, i))

    def step2(i):
        dissolve_plane(sx, m1, cf, mx, i)
        collide_plane(fx, gx, sx, cx, sm, fs, gs, i)

    loop(1, last, step2)
    posts()
    loop(1, last, lambda i: stream_plane(fs, gs, sx, fx, gx, i, bm))

    from_low, send_low, send_high, from_high = mv[0], mv[1], mv[2], mv[3]
    kept_end = from_low + planes - send_low - send_high
    valid_end = kept_end + from_high

    def slot_copies(s, valid):
        if valid:
            plane = s - from_low + own
            plane = plane + jnp.where(s >= from_low, send_low, 0)
            plane = plane + jnp.where(s >= kept_end, send_high, 0)
            plane = jnp.clip(plane, 1, last - 1)
            srcs = (fx.at[:, plane], gx.at[:, plane], mx.at[plane], si.at[plane])
        else:
            srcs = (zf, zf.at[0:NG], zf.at[0], zi)
        dsts = (out_f.at[:, s], out_g.at[:, s], out_m.at[s], out_s.at[s])
        return [pltpu.make_async_copy(a, b, osem.at[s, k]) for k, (a, b) in enumerate(zip(srcs, dsts))]

    for phase in ("start", "wait"):
        for s in range(cap):
            for valid in (True, False):
                cond = (s < valid_end) if valid else (s >= valid_end)

                @pl.when(cond)
                def _():
                    for c in slot_copies(s, valid):
                        getattr(c, phase)()


def shards(populations, solute, mineral, solid, plane_moves):
    planes = populations.shape[1]
    cap = planes + 2 * MOVE_MOST
    ext = planes + 2 * HALO + 2
    count = lax.axis_size("blk")
    forward = [(i, (i + 1) % count) for i in range(count)]
    backward = [(i, (i - 1) % count) for i in range(count)]

    def edge(lo):
        return jnp.concatenate(
            [
                populations[:, lo:lo + HALO],
                solute[:, lo:lo + HALO],
                mineral[None, lo:lo + HALO],
                solid[None, lo:lo + HALO].astype(jnp.float32),
            ],
            axis=0,
        )

    halo_lo = lax.ppermute(edge(planes - HALO), "blk", forward)
    halo_hi = lax.ppermute(edge(0), "blk", backward)

    plane = populations.shape[2:]
    f32 = jnp.float32
    any_spec = pl.BlockSpec(memory_space=pl.ANY)
    vmem = pl.BlockSpec(memory_space=pltpu.VMEM)
    smem = pl.BlockSpec(memory_space=pltpu.SMEM)

    up, down = pl.pallas_call(
        flux_kernel,
        out_shape=(
            jax.ShapeDtypeStruct((NFLUX,) + plane, f32),
            jax.ShapeDtypeStruct((NFLUX,) + plane, f32),
        ),
        in_specs=[vmem] * 4,
        out_specs=[vmem] * 2,
        scratch_shapes=[
            pltpu.VMEM((NF, planes) + plane, f32),
            pltpu.VMEM((NG, planes) + plane, f32),
            pltpu.VMEM((NF, planes) + plane, f32),
            pltpu.VMEM((NG, planes) + plane, f32),
        ]
        + [pltpu.VMEM((planes,) + plane, f32)] * 5,
    )(populations, solute, mineral, solid)
    flux_lo = lax.ppermute(up, "blk", forward)
    flux_hi = lax.ppermute(down, "blk", backward)

    me = lax.axis_index("blk")
    from_low = plane_moves[jnp.mod(me - 1, count), 1]
    send_low = plane_moves[me, 0]
    send_high = plane_moves[me, 1]
    from_high = plane_moves[jnp.mod(me + 1, count), 0]
    mv = jnp.stack([from_low, send_low, send_high, from_high]).astype(jnp.int32)

    return pl.pallas_call(
        main_kernel,
        out_shape=(
            jax.ShapeDtypeStruct((NF, cap) + plane, f32),
            jax.ShapeDtypeStruct((NG, cap) + plane, f32),
            jax.ShapeDtypeStruct((cap,) + plane, f32),
            jax.ShapeDtypeStruct((cap,) + plane, jnp.int32),
        ),
        in_specs=[smem, any_spec, any_spec, any_spec, vmem, any_spec, any_spec, vmem, vmem],
        out_specs=[any_spec] * 4,
        scratch_shapes=[
            pltpu.VMEM((NF, ext) + plane, f32),
            pltpu.VMEM((NG, ext) + plane, f32),
            pltpu.VMEM((NF, ext) + plane, f32),
            pltpu.VMEM((NG, ext) + plane, f32),
            pltpu.VMEM((ext,) + plane, f32),
            pltpu.VMEM((ext,) + plane, f32),
            pltpu.VMEM((ext,) + plane, f32),
            pltpu.VMEM((ext,) + plane, jnp.int32),
            pltpu.VMEM((ext,) + plane, f32),
            pltpu.VMEM((ext,) + plane, f32),
            pltpu.VMEM((ext,) + plane, f32),
            pltpu.VMEM((NF,) + plane, f32),
            pltpu.VMEM(plane, jnp.int32),
            pltpu.VMEM((len(SHIFTS), ext) + plane, f32),
            pltpu.SemaphoreType.DMA((11,)),
            pltpu.SemaphoreType.DMA((cap, 4)),
        ],
        compiler_params=pltpu.CompilerParams(vmem_limit_bytes=50 * 1024 * 1024),
    )(mv, populations, solute, mineral, solid, halo_lo, halo_hi, flux_lo, flux_hi)


def solution(mesh):
    return jax.shard_map(
        shards,
        mesh=mesh,
        in_specs=(
            P(None, "blk", None, None),
            P(None, "blk", None, None),
            P("blk", None, None),
            P("blk", None, None),
            P(),
        ),
        out_specs=(
            P(None, "blk", None, None),
            P(None, "blk", None, None),
            P("blk", None, None),
            P("blk", None, None),
        ),
        check_vma=False,
    )
```

```python
import functools

import jax
import jax.numpy as jnp
from jax import lax
from jax.experimental import pallas as pl
from jax.experimental.pallas import tpu as pltpu
from jax.sharding import PartitionSpec as P

MOVE_MOST = 3
HALO = 3

flow_vel = [
    (0, 0, 1),
    (1, 0, 1),
    (-1, 0, 1),
    (0, 1, 1),
    (0, -1, 1),
    (0, 0, -1),
    (1, 0, -1),
    (-1, 0, -1),
    (0, 1, -1),
    (0, -1, -1),
    (0, 0, 0),
    (1, 0, 0),
    (-1, 0, 0),
    (0, 1, 0),
    (0, -1, 0),
    (1, 1, 0),
    (-1, -1, 0),
    (1, -1, 0),
    (-1, 1, 0),
]
flow_weight = [
    1.0 / 18,
    1.0 / 36,
    1.0 / 36,
    1.0 / 36,
    1.0 / 36,
    1.0 / 18,
    1.0 / 36,
    1.0 / 36,
    1.0 / 36,
    1.0 / 36,
    1.0 / 3,
    1.0 / 18,
    1.0 / 18,
    1.0 / 18,
    1.0 / 18,
    1.0 / 36,
    1.0 / 36,
    1.0 / 36,
    1.0 / 36,
]
acid_vel = [(0, 0, 1), (0, 0, -1), (0, 0, 0), (1, 0, 0), (-1, 0, 0), (0, 1, 0), (0, -1, 0)]
acid_weight = [0.125, 0.125, 0.25, 0.125, 0.125, 0.125, 0.125]
relax_flow = 1.25
relax_acid = 0.8
body_force = 0.001
react_rate = 0.1
dissolve_rate = 0.5

NF = len(flow_vel)
NG = len(acid_vel)


def roll_xy(a, cx, cy):
    if cx:
        a = pltpu.roll(a, cx % a.shape[0], 0)
    if cy:
        a = pltpu.roll(a, cy % a.shape[1], 1)
    return a


def face_sum(ref, i):
    mid = ref[i]
    total = ref[i - 1] + ref[i + 1]
    total = total + (roll_xy(mid, 1, 0) + roll_xy(mid, -1, 0))
    return total + (roll_xy(mid, 0, 1) + roll_xy(mid, 0, -1))


def edge_state(sx, gx, mx, cx, sm, cf, i):
    conc = gx[0, i]
    for j in range(1, NG):
        conc = conc + gx[j, i]
    cx[i] = conc
    solid = sx[i] > 0.5
    sm[i] = jnp.where(solid, mx[i], 0.0)
    cf[i] = jnp.where(solid, 0.0, conc)


def collide_plane(fx, gx, sx, cx, sm, fs, gs, i):
    solid = sx[i] > 0.5
    f = [fx[q, i] for q in range(NF)]
    density = f[0]
    for q in range(1, NF):
        density = density + f[q]
    moments = []
    for axis in range(3):
        total = None
        for q, vel in enumerate(flow_vel):
            if vel[axis] == 0:
                continue
            term = f[q] if vel[axis] > 0 else -f[q]
            total = term if total is None else total + term
        moments.append(total)
    inv = 1.0 / density
    comps = [m * inv for m in moments]
    base = 1.0 - 1.5 * (comps[0] * comps[0] + comps[1] * comps[1] + comps[2] * comps[2])
    keep = 1.0 - 1.0 / relax_flow
    scaled = {}
    for w in set(flow_weight):
        scaled[w] = (w / relax_flow) * density

    def along(vel):
        total = None
        for axis in range(3):
            if vel[axis] == 0:
                continue
            term = comps[axis] if vel[axis] > 0 else -comps[axis]
            total = term if total is None else total + term
        return total

    done = set()
    for q, vel in enumerate(flow_vel):
        if q in done:
            continue
        opp = flow_vel.index(tuple(-c for c in vel))
        done |= {q, opp}
        weight = scaled[flow_weight[q]]
        if opp == q:
            fs[q, i] = jnp.where(solid, f[q], keep * f[q] + weight * base)
            continue
        cu = along(vel)
        even = base + 4.5 * (cu * cu)
        odd = 3.0 * cu
        if vel[2]:
            odd = odd + 3.0 * body_force * relax_flow * vel[2]
        for member, poly in ((q, even + odd), (opp, even - odd)):
            fs[member, i] = jnp.where(solid, f[member], keep * f[member] + weight * poly)
    conc = cx[i]
    sink = (react_rate * conc) * face_sum(sm, i)
    rate = 1.0 / relax_acid
    shared = rate * conc - sink
    slope = (4.0 * rate) * conc
    done = set()
    for j, vel in enumerate(acid_vel):
        if j in done:
            continue
        opp = acid_vel.index(tuple(-c for c in vel))
        done |= {j, opp}
        if opp == j:
            parts = ((j, shared),)
        else:
            cu = slope * along(vel)
            parts = ((j, shared + cu), (opp, shared - cu))
        for member, inner in parts:
            g = gx[member, i]
            relaxed = acid_weight[member] * inner - (rate - 1.0) * g
            gs[member, i] = jnp.where(solid, g, relaxed)


def dissolve_plane(sx, mx_src, cf, mx_dst, i):
    solid = sx[i] > 0.5
    mineral = mx_src[i]
    loss = (dissolve_rate * react_rate) * mineral * face_sum(cf, i)
    mx_dst[i] = jnp.where(solid, mineral - loss, mineral)


SHIFTS = [(cx, cy) for cx in (-1, 0, 1) for cy in (-1, 0, 1) if cx or cy]


def shift_masks(sx, bm, i):
    for c, (cx, cy) in enumerate(SHIFTS):
        bm[c, i] = roll_xy(sx[i], cx, cy)


def stream_plane(fs, gs, sx, fdst, gdst, i, bm=None):
    solid = sx[i] > 0.5
    masks = {}
    for q, vel in enumerate(flow_vel):
        cx, cy, cz = vel
        if vel == (0, 0, 0):
            fdst[q, i] = fs[q, i]
            continue
        opp = flow_vel.index((-cx, -cy, -cz))
        src = i - cz
        pulled = roll_xy(fs[q, src], cx, cy)
        if bm is None or (cx, cy) == (0, 0):
            blocked = roll_xy(sx[src], cx, cy) > 0.5
        else:
            blocked = bm[SHIFTS.index((cx, cy)), src] > 0.5
        masks[vel] = blocked
        arrived = jnp.where(blocked, fs[opp, i], pulled)
        fdst[q, i] = jnp.where(solid, fs[q, i], arrived)
    for j, vel in enumerate(acid_vel):
        cx, cy, cz = vel
        if vel == (0, 0, 0):
            gdst[j, i] = gs[j, i]
            continue
        opp = acid_vel.index((-cx, -cy, -cz))
        pulled = roll_xy(gs[j, i - cz], cx, cy)
        arrived = jnp.where(masks[vel], gs[opp, i], pulled)
        gdst[j, i] = jnp.where(solid, gs[j, i], arrived)


def loop(lo, hi, fn):
    def body(i, carry):
        fn(i)
        return carry

    lax.fori_loop(lo, hi, body, 0)


UP_Q = [q for q, vel in enumerate(flow_vel) if vel[2] == 1]
DOWN_Q = [q for q, vel in enumerate(flow_vel) if vel[2] == -1]
UP_J = acid_vel.index((0, 0, 1))
DOWN_J = acid_vel.index((0, 0, -1))
NFLUX = 3 + 2 * (len(UP_Q) + 1) + 2


def flux_kernel(pop, sol, mnr, sld, up, down, fs, gs, f1, g1, m1, sx, cx, sm, cf):
    planes = sld.shape[0]
    hi, lo = planes - HALO - 1, HALO
    sx[...] = sld[...].astype(jnp.float32)
    loop(lo - 2, hi + 3, lambda i: edge_state(sx, sol, mnr, cx, sm, cf, i))

    def step1(i):
        dissolve_plane(sx, mnr, cf, m1, i)
        collide_plane(pop, sol, sx, cx, sm, fs, gs, i)

    loop(lo - 1, hi + 2, step1)
    for dst, i, qs, j in ((up, hi, UP_Q, UP_J), (down, lo, DOWN_Q, DOWN_J)):
        dst[0] = sx[i]
        dst[1] = sm[i]
        dst[2] = cf[i]
        for n, q in enumerate(qs):
            dst[3 + n] = fs[q, i]
        dst[3 + len(qs)] = gs[j, i]
    loop(lo, hi + 1, lambda i: stream_plane(fs, gs, sx, f1, g1, i))
    for i in range(lo - 1, hi + 2):
        sm[i] = jnp.where(sx[i] > 0.5, m1[i], 0.0)
    for i in range(lo, hi + 1):
        conc = g1[0, i]
        for j in range(1, NG):
            conc = conc + g1[j, i]
        cx[i] = conc
        cf[i] = jnp.where(sx[i] > 0.5, 0.0, conc)
    loop(lo, hi + 1, lambda i: collide_plane(f1, g1, sx, cx, sm, fs, gs, i))
    base = 4 + len(UP_Q)
    for dst, i, qs, j in ((up, hi, UP_Q, UP_J), (down, lo, DOWN_Q, DOWN_J)):
        dst[base] = sm[i]
        dst[base + 1] = cf[i]
        for n, q in enumerate(qs):
            dst[base + 2 + n] = fs[q, i]
        dst[base + 2 + len(qs)] = gs[j, i]


def set_bounds(flo, fhi, sm, cf, fs, gs, last, base):
    sm[0] = flo[base]
    cf[0] = flo[base + 1]
    sm[last] = fhi[base]
    cf[last] = fhi[base + 1]

    def posts():
        for n, q in enumerate(UP_Q):
            fs[q, 0] = flo[base + 2 + n]
        gs[UP_J, 0] = flo[base + 2 + len(UP_Q)]
        for n, q in enumerate(DOWN_Q):
            fs[q, last] = fhi[base + 2 + n]
        gs[DOWN_J, last] = fhi[base + 2 + len(DOWN_Q)]

    return posts


def main_kernel(
    mv, pop, sol, mnr, sld, hlo, hhi, flo, fhi,
    out_f, out_g, out_m, out_s,
    fx, gx, fs, gs, mx, m1, sx, si, cx, sm, cf, zf, zi, bm, sem, osem, zsem,
):
    planes = sld.shape[0]
    cap = out_s.shape[0]
    last = planes + 2 * HALO + 1
    own = HALO + 1
    top = own + planes
    fill = [
        (pop, fx.at[:, own:top]),
        (sol, gx.at[:, own:top]),
        (mnr, mx.at[own:top]),
        (hlo.at[0:NF], fx.at[:, 1:own]),
        (hlo.at[NF:NF + NG], gx.at[:, 1:own]),
        (hlo.at[NF + NG], mx.at[1:own]),
        (hlo.at[NF + NG + 1], sx.at[1:own]),
        (hhi.at[0:NF], fx.at[:, top:last]),
        (hhi.at[NF:NF + NG], gx.at[:, top:last]),
        (hhi.at[NF + NG], mx.at[top:last]),
        (hhi.at[NF + NG + 1], sx.at[top:last]),
    ]
    copies = [pltpu.make_async_copy(s, d, sem.at[k]) for k, (s, d) in enumerate(fill)]
    for c in copies:
        c.start()
    sx[own:top] = sld[...].astype(jnp.float32)
    si[own:top] = sld[...]
    sx[0] = flo[0]
    sx[last] = fhi[0]
    zf[...] = jnp.zeros(zf.shape, zf.dtype)
    zi[...] = jnp.zeros(zi.shape, zi.dtype)
    for c in copies:
        c.wait()
    si[1:own] = (sx[1:own] > 0.5).astype(jnp.int32)
    si[top:last] = (sx[top:last] > 0.5).astype(jnp.int32)

    from_low, send_low, send_high, from_high = mv[0], mv[1], mv[2], mv[3]
    valid_end = from_low + planes - send_low - send_high + from_high

    def plane_valid(i):
        p = i - own
        low = (p >= -from_low) & (p < 0)
        kept = (p >= send_low) & (p < planes - send_high)
        high = (p >= planes) & (p < planes + from_high)
        return low | kept | high

    def plane_copies(i):
        p = i - own
        s = p + from_low - jnp.where(p >= send_low, send_low, 0) - jnp.where(p >= planes, send_high, 0)
        s = jnp.clip(s, 0, cap - 1)
        srcs = (fx.at[:, i], gx.at[:, i], mx.at[i], si.at[i])
        dsts = (out_f.at[:, s], out_g.at[:, s], out_m.at[s], out_s.at[s])
        return [pltpu.make_async_copy(x, y, osem.at[i, k]) for k, (x, y) in enumerate(zip(srcs, dsts))]

    def zero_copies(s):
        srcs = (zf, zf.at[0:NG], zf.at[0], zi)
        dsts = (out_f.at[:, s], out_g.at[:, s], out_m.at[s], out_s.at[s])
        return [pltpu.make_async_copy(x, y, zsem.at[s, k]) for k, (x, y) in enumerate(zip(srcs, dsts))]

    for s in range(cap):
        @pl.when(s >= valid_end)
        def _():
            for c in zero_copies(s):
                c.start()

    loop(0, last + 1, lambda i: shift_masks(sx, bm, i))

    posts = set_bounds(flo, fhi, sm, cf, fs, gs, last, 1)
    loop(1, last, lambda i: edge_state(sx, gx, mx, cx, sm, cf, i))

    def step1(i):
        dissolve_plane(sx, mx, cf, m1, i)
        collide_plane(fx, gx, sx, cx, sm, fs, gs, i)

    loop(1, last, step1)
    posts()
    loop(1, last, lambda i: stream_plane(fs, gs, sx, fx, gx, i, bm))

    posts = set_bounds(flo, fhi, sm, cf, fs, gs, last, 4 + len(UP_Q))
    loop(1, last, lambda i: edge_state(sx, gx, m1, cx, sm, cf, i))

    def step2(i):
        dissolve_plane(sx, m1, cf, mx, i)
        collide_plane(fx, gx, sx, cx, sm, fs, gs, i)

    loop(1, last, step2)
    posts()

    def send_plane(i):
        @pl.when(plane_valid(i))
        def _():
            for c in plane_copies(i):
                c.start()

    def final(i):
        stream_plane(fs, gs, sx, fx, gx, i, bm)

        @pl.when(i > 1)
        def _():
            send_plane(i - 1)

    loop(1, last, final)
    send_plane(last - 1)
    for i in range(1, last):
        @pl.when(plane_valid(i))
        def _():
            for c in plane_copies(i):
                c.wait()
    for s in range(cap):
        @pl.when(s >= valid_end)
        def _():
            for c in zero_copies(s):
                c.wait()


def shards(populations, solute, mineral, solid, plane_moves):
    planes = populations.shape[1]
    cap = planes + 2 * MOVE_MOST
    ext = planes + 2 * HALO + 2
    count = lax.axis_size("blk")
    forward = [(i, (i + 1) % count) for i in range(count)]
    backward = [(i, (i - 1) % count) for i in range(count)]

    def edge(lo):
        return jnp.concatenate(
            [
                populations[:, lo:lo + HALO],
                solute[:, lo:lo + HALO],
                mineral[None, lo:lo + HALO],
                solid[None, lo:lo + HALO].astype(jnp.float32),
            ],
            axis=0,
        )

    halo_lo = lax.ppermute(edge(planes - HALO), "blk", forward)
    halo_hi = lax.ppermute(edge(0), "blk", backward)

    plane = populations.shape[2:]
    f32 = jnp.float32
    any_spec = pl.BlockSpec(memory_space=pl.ANY)
    vmem = pl.BlockSpec(memory_space=pltpu.VMEM)
    smem = pl.BlockSpec(memory_space=pltpu.SMEM)

    up, down = pl.pallas_call(
        flux_kernel,
        out_shape=(
            jax.ShapeDtypeStruct((NFLUX,) + plane, f32),
            jax.ShapeDtypeStruct((NFLUX,) + plane, f32),
        ),
        in_specs=[vmem] * 4,
        out_specs=[vmem] * 2,
        scratch_shapes=[
            pltpu.VMEM((NF, planes) + plane, f32),
            pltpu.VMEM((NG, planes) + plane, f32),
            pltpu.VMEM((NF, planes) + plane, f32),
            pltpu.VMEM((NG, planes) + plane, f32),
        ]
        + [pltpu.VMEM((planes,) + plane, f32)] * 5,
    )(populations, solute, mineral, solid)
    flux_lo = lax.ppermute(up, "blk", forward)
    flux_hi = lax.ppermute(down, "blk", backward)

    me = lax.axis_index("blk")
    from_low = plane_moves[jnp.mod(me - 1, count), 1]
    send_low = plane_moves[me, 0]
    send_high = plane_moves[me, 1]
    from_high = plane_moves[jnp.mod(me + 1, count), 0]
    mv = jnp.stack([from_low, send_low, send_high, from_high]).astype(jnp.int32)

    return pl.pallas_call(
        main_kernel,
        out_shape=(
            jax.ShapeDtypeStruct((NF, cap) + plane, f32),
            jax.ShapeDtypeStruct((NG, cap) + plane, f32),
            jax.ShapeDtypeStruct((cap,) + plane, f32),
            jax.ShapeDtypeStruct((cap,) + plane, jnp.int32),
        ),
        in_specs=[smem, any_spec, any_spec, any_spec, vmem, any_spec, any_spec, vmem, vmem],
        out_specs=[any_spec] * 4,
        scratch_shapes=[
            pltpu.VMEM((NF, ext) + plane, f32),
            pltpu.VMEM((NG, ext) + plane, f32),
            pltpu.VMEM((NF, ext) + plane, f32),
            pltpu.VMEM((NG, ext) + plane, f32),
            pltpu.VMEM((ext,) + plane, f32),
            pltpu.VMEM((ext,) + plane, f32),
            pltpu.VMEM((ext,) + plane, f32),
            pltpu.VMEM((ext,) + plane, jnp.int32),
            pltpu.VMEM((ext,) + plane, f32),
            pltpu.VMEM((ext,) + plane, f32),
            pltpu.VMEM((ext,) + plane, f32),
            pltpu.VMEM((NF,) + plane, f32),
            pltpu.VMEM(plane, jnp.int32),
            pltpu.VMEM((len(SHIFTS), ext) + plane, f32),
            pltpu.SemaphoreType.DMA((11,)),
            pltpu.SemaphoreType.DMA((ext, 4)),
            pltpu.SemaphoreType.DMA((cap, 4)),
        ],
        compiler_params=pltpu.CompilerParams(vmem_limit_bytes=50 * 1024 * 1024),
    )(mv, populations, solute, mineral, solid, halo_lo, halo_hi, flux_lo, flux_hi)


def solution(mesh):
    return jax.shard_map(
        shards,
        mesh=mesh,
        in_specs=(
            P(None, "blk", None, None),
            P(None, "blk", None, None),
            P("blk", None, None),
            P("blk", None, None),
            P(),
        ),
        out_specs=(
            P(None, "blk", None, None),
            P(None, "blk", None, None),
            P("blk", None, None),
            P("blk", None, None),
        ),
        check_vma=False,
    )
```

```python
import functools

import jax
import jax.numpy as jnp
from jax import lax
from jax.experimental import pallas as pl
from jax.experimental.pallas import tpu as pltpu
from jax.sharding import PartitionSpec as P

MOVE_MOST = 3
HALO = 3

flow_vel = [
    (0, 0, 1),
    (1, 0, 1),
    (-1, 0, 1),
    (0, 1, 1),
    (0, -1, 1),
    (0, 0, -1),
    (1, 0, -1),
    (-1, 0, -1),
    (0, 1, -1),
    (0, -1, -1),
    (0, 0, 0),
    (1, 0, 0),
    (-1, 0, 0),
    (0, 1, 0),
    (0, -1, 0),
    (1, 1, 0),
    (-1, -1, 0),
    (1, -1, 0),
    (-1, 1, 0),
]
flow_weight = [
    1.0 / 18,
    1.0 / 36,
    1.0 / 36,
    1.0 / 36,
    1.0 / 36,
    1.0 / 18,
    1.0 / 36,
    1.0 / 36,
    1.0 / 36,
    1.0 / 36,
    1.0 / 3,
    1.0 / 18,
    1.0 / 18,
    1.0 / 18,
    1.0 / 18,
    1.0 / 36,
    1.0 / 36,
    1.0 / 36,
    1.0 / 36,
]
acid_vel = [(0, 0, 1), (0, 0, -1), (0, 0, 0), (1, 0, 0), (-1, 0, 0), (0, 1, 0), (0, -1, 0)]
acid_weight = [0.125, 0.125, 0.25, 0.125, 0.125, 0.125, 0.125]
relax_flow = 1.25
relax_acid = 0.8
body_force = 0.001
react_rate = 0.1
dissolve_rate = 0.5

NF = len(flow_vel)
NG = len(acid_vel)


def roll_xy(a, cx, cy):
    if cx:
        a = pltpu.roll(a, cx % a.shape[0], 0)
    if cy:
        a = pltpu.roll(a, cy % a.shape[1], 1)
    return a


def face_sum(ref, i):
    mid = ref[i]
    total = ref[i - 1] + ref[i + 1]
    total = total + (roll_xy(mid, 1, 0) + roll_xy(mid, -1, 0))
    return total + (roll_xy(mid, 0, 1) + roll_xy(mid, 0, -1))


def edge_state(sx, gx, mx, cx, sm, cf, i):
    conc = gx[0, i]
    for j in range(1, NG):
        conc = conc + gx[j, i]
    cx[i] = conc
    solid = sx[i] > 0.5
    sm[i] = jnp.where(solid, mx[i], 0.0)
    cf[i] = jnp.where(solid, 0.0, conc)


def collide_plane(fx, gx, sx, cx, sm, fs, gs, i):
    solid = sx[i] > 0.5
    f = [fx[q, i] for q in range(NF)]
    density = f[0]
    for q in range(1, NF):
        density = density + f[q]
    moments = []
    for axis in range(3):
        total = None
        for q, vel in enumerate(flow_vel):
            if vel[axis] == 0:
                continue
            term = f[q] if vel[axis] > 0 else -f[q]
            total = term if total is None else total + term
        moments.append(total)
    inv = 1.0 / density
    comps = [m * inv for m in moments]
    base = 1.0 - 1.5 * (comps[0] * comps[0] + comps[1] * comps[1] + comps[2] * comps[2])
    keep = 1.0 - 1.0 / relax_flow
    scaled = {}
    for w in set(flow_weight):
        scaled[w] = (w / relax_flow) * density

    def along(vel):
        total = None
        for axis in range(3):
            if vel[axis] == 0:
                continue
            term = comps[axis] if vel[axis] > 0 else -comps[axis]
            total = term if total is None else total + term
        return total

    done = set()
    for q, vel in enumerate(flow_vel):
        if q in done:
            continue
        opp = flow_vel.index(tuple(-c for c in vel))
        done |= {q, opp}
        weight = scaled[flow_weight[q]]
        if opp == q:
            fs[q, i] = jnp.where(solid, f[q], keep * f[q] + weight * base)
            continue
        cu = along(vel)
        even = base + 4.5 * (cu * cu)
        odd = 3.0 * cu
        if vel[2]:
            odd = odd + 3.0 * body_force * relax_flow * vel[2]
        for member, poly in ((q, even + odd), (opp, even - odd)):
            fs[member, i] = jnp.where(solid, f[member], keep * f[member] + weight * poly)
    conc = cx[i]
    sink = (react_rate * conc) * face_sum(sm, i)
    rate = 1.0 / relax_acid
    shared = rate * conc - sink
    slope = (4.0 * rate) * conc
    done = set()
    for j, vel in enumerate(acid_vel):
        if j in done:
            continue
        opp = acid_vel.index(tuple(-c for c in vel))
        done |= {j, opp}
        if opp == j:
            parts = ((j, shared),)
        else:
            cu = slope * along(vel)
            parts = ((j, shared + cu), (opp, shared - cu))
        for member, inner in parts:
            g = gx[member, i]
            relaxed = acid_weight[member] * inner - (rate - 1.0) * g
            gs[member, i] = jnp.where(solid, g, relaxed)


def dissolve_plane(sx, mx_src, cf, mx_dst, i):
    solid = sx[i] > 0.5
    mineral = mx_src[i]
    loss = (dissolve_rate * react_rate) * mineral * face_sum(cf, i)
    mx_dst[i] = jnp.where(solid, mineral - loss, mineral)


SHIFTS = [(cx, cy) for cx in (-1, 0, 1) for cy in (-1, 0, 1) if cx or cy]


def shift_masks(sx, bm, i):
    for c, (cx, cy) in enumerate(SHIFTS):
        bm[c, i] = roll_xy(sx[i], cx, cy)


def stream_plane(fs, gs, sx, fdst, gdst, i, bm=None):
    solid = sx[i] > 0.5
    masks = {}
    for q, vel in enumerate(flow_vel):
        cx, cy, cz = vel
        if vel == (0, 0, 0):
            fdst[q, i] = fs[q, i]
            continue
        opp = flow_vel.index((-cx, -cy, -cz))
        src = i - cz
        pulled = roll_xy(fs[q, src], cx, cy)
        if bm is None or (cx, cy) == (0, 0):
            blocked = roll_xy(sx[src], cx, cy) > 0.5
        else:
            blocked = bm[SHIFTS.index((cx, cy)), src] > 0.5
        masks[vel] = blocked
        arrived = jnp.where(blocked, fs[opp, i], pulled)
        fdst[q, i] = jnp.where(solid, fs[q, i], arrived)
    for j, vel in enumerate(acid_vel):
        cx, cy, cz = vel
        if vel == (0, 0, 0):
            gdst[j, i] = gs[j, i]
            continue
        opp = acid_vel.index((-cx, -cy, -cz))
        pulled = roll_xy(gs[j, i - cz], cx, cy)
        arrived = jnp.where(masks[vel], gs[opp, i], pulled)
        gdst[j, i] = jnp.where(solid, gs[j, i], arrived)


def loop(lo, hi, fn):
    def body(i, carry):
        fn(i)
        return carry

    lax.fori_loop(lo, hi, body, 0)


UP_Q = [q for q, vel in enumerate(flow_vel) if vel[2] == 1]
DOWN_Q = [q for q, vel in enumerate(flow_vel) if vel[2] == -1]
UP_J = acid_vel.index((0, 0, 1))
DOWN_J = acid_vel.index((0, 0, -1))
NFLUX = 3 + 2 * (len(UP_Q) + 1) + 2


def flux_kernel(pop, sol, mnr, sld, up, down, fs, gs, f1, g1, m1, sx, cx, sm, cf):
    planes = sld.shape[0]
    hi, lo = planes - HALO - 1, HALO
    sx[...] = sld[...].astype(jnp.float32)
    loop(lo - 2, hi + 3, lambda i: edge_state(sx, sol, mnr, cx, sm, cf, i))

    def step1(i):
        dissolve_plane(sx, mnr, cf, m1, i)
        collide_plane(pop, sol, sx, cx, sm, fs, gs, i)

    loop(lo - 1, hi + 2, step1)
    for dst, i, qs, j in ((up, hi, UP_Q, UP_J), (down, lo, DOWN_Q, DOWN_J)):
        dst[0] = sx[i]
        dst[1] = sm[i]
        dst[2] = cf[i]
        for n, q in enumerate(qs):
            dst[3 + n] = fs[q, i]
        dst[3 + len(qs)] = gs[j, i]
    loop(lo, hi + 1, lambda i: stream_plane(fs, gs, sx, f1, g1, i))
    for i in range(lo - 1, hi + 2):
        sm[i] = jnp.where(sx[i] > 0.5, m1[i], 0.0)
    for i in range(lo, hi + 1):
        conc = g1[0, i]
        for j in range(1, NG):
            conc = conc + g1[j, i]
        cx[i] = conc
        cf[i] = jnp.where(sx[i] > 0.5, 0.0, conc)
    loop(lo, hi + 1, lambda i: collide_plane(f1, g1, sx, cx, sm, fs, gs, i))
    base = 4 + len(UP_Q)
    for dst, i, qs, j in ((up, hi, UP_Q, UP_J), (down, lo, DOWN_Q, DOWN_J)):
        dst[base] = sm[i]
        dst[base + 1] = cf[i]
        for n, q in enumerate(qs):
            dst[base + 2 + n] = fs[q, i]
        dst[base + 2 + len(qs)] = gs[j, i]


def set_bounds(flo, fhi, sm, cf, fs, gs, last, base):
    sm[0] = flo[base]
    cf[0] = flo[base + 1]
    sm[last] = fhi[base]
    cf[last] = fhi[base + 1]

    def posts():
        for n, q in enumerate(UP_Q):
            fs[q, 0] = flo[base + 2 + n]
        gs[UP_J, 0] = flo[base + 2 + len(UP_Q)]
        for n, q in enumerate(DOWN_Q):
            fs[q, last] = fhi[base + 2 + n]
        gs[DOWN_J, last] = fhi[base + 2 + len(DOWN_Q)]

    return posts


def main_kernel(
    mv, pop, sol, mnr, sld, hlo, hhi, flo, fhi,
    out_f, out_g, out_m, out_s,
    fx, gx, fs, gs, mx, m1, sx, si, cx, sm, cf, zf, zi, bm, sem, osem, zsem,
):
    planes = sld.shape[0]
    cap = out_s.shape[0]
    last = planes + 2 * HALO + 1
    own = HALO + 1
    top = own + planes
    fill = [
        (pop, fx.at[:, own:top]),
        (sol, gx.at[:, own:top]),
        (mnr, mx.at[own:top]),
        (hlo.at[0:NF], fx.at[:, 1:own]),
        (hlo.at[NF:NF + NG], gx.at[:, 1:own]),
        (hlo.at[NF + NG], mx.at[1:own]),
        (hlo.at[NF + NG + 1], sx.at[1:own]),
        (hhi.at[0:NF], fx.at[:, top:last]),
        (hhi.at[NF:NF + NG], gx.at[:, top:last]),
        (hhi.at[NF + NG], mx.at[top:last]),
        (hhi.at[NF + NG + 1], sx.at[top:last]),
    ]
    copies = [pltpu.make_async_copy(s, d, sem.at[k]) for k, (s, d) in enumerate(fill)]
    for c in copies:
        c.start()
    sx[own:top] = sld[...].astype(jnp.float32)
    si[own:top] = sld[...]
    sx[0] = flo[0]
    sx[last] = fhi[0]
    zf[...] = jnp.zeros(zf.shape, zf.dtype)
    zi[...] = jnp.zeros(zi.shape, zi.dtype)
    for c in copies:
        c.wait()
    si[1:own] = (sx[1:own] > 0.5).astype(jnp.int32)
    si[top:last] = (sx[top:last] > 0.5).astype(jnp.int32)

    from_low, send_low, send_high, from_high = mv[0], mv[1], mv[2], mv[3]
    valid_end = from_low + planes - send_low - send_high + from_high

    def plane_valid(i):
        p = i - own
        low = (p >= -from_low) & (p < 0)
        kept = (p >= send_low) & (p < planes - send_high)
        high = (p >= planes) & (p < planes + from_high)
        return low | kept | high

    def plane_copies(i):
        p = i - own
        s = p + from_low - jnp.where(p >= send_low, send_low, 0) - jnp.where(p >= planes, send_high, 0)
        s = jnp.clip(s, 0, cap - 1)
        srcs = (fx.at[:, i], gx.at[:, i], mx.at[i], si.at[i])
        dsts = (out_f.at[:, s], out_g.at[:, s], out_m.at[s], out_s.at[s])
        return [pltpu.make_async_copy(x, y, osem.at[i, k]) for k, (x, y) in enumerate(zip(srcs, dsts))]

    def zero_copies(s):
        srcs = (zf, zf.at[0:NG], zf.at[0], zi)
        dsts = (out_f.at[:, s], out_g.at[:, s], out_m.at[s], out_s.at[s])
        return [pltpu.make_async_copy(x, y, zsem.at[s, k]) for k, (x, y) in enumerate(zip(srcs, dsts))]

    for s in range(cap):
        @pl.when(s >= valid_end)
        def _():
            for c in zero_copies(s):
                c.start()

    loop(0, last + 1, lambda i: shift_masks(sx, bm, i))

    posts = set_bounds(flo, fhi, sm, cf, fs, gs, last, 1)
    loop(1, last, lambda i: edge_state(sx, gx, mx, cx, sm, cf, i))

    def step1(i):
        dissolve_plane(sx, mx, cf, m1, i)
        collide_plane(fx, gx, sx, cx, sm, fs, gs, i)

    loop(1, last, step1)
    posts()
    loop(1, last, lambda i: stream_plane(fs, gs, sx, fx, gx, i, bm))

    posts = set_bounds(flo, fhi, sm, cf, fs, gs, last, 4 + len(UP_Q))
    loop(1, last, lambda i: edge_state(sx, gx, m1, cx, sm, cf, i))

    def step2(i):
        dissolve_plane(sx, m1, cf, mx, i)
        collide_plane(fx, gx, sx, cx, sm, fs, gs, i)

    loop(1, last, step2)
    posts()

    def send_plane(i):
        @pl.when(plane_valid(i))
        def _():
            for c in plane_copies(i):
                c.start()

    def final(i):
        stream_plane(fs, gs, sx, fx, gx, i, bm)

        @pl.when(i > 1)
        def _():
            send_plane(i - 1)

    loop(1, last, final)
    send_plane(last - 1)
    for i in range(1, last):
        @pl.when(plane_valid(i))
        def _():
            for c in plane_copies(i):
                c.wait()
    for s in range(cap):
        @pl.when(s >= valid_end)
        def _():
            for c in zero_copies(s):
                c.wait()


def edge_kernel(lo, pop, sol, mnr, sld, out, sem):
    parts = [
        (pop.at[:, lo:lo + HALO], out.at[0:NF]),
        (sol.at[:, lo:lo + HALO], out.at[NF:NF + NG]),
        (mnr.at[lo:lo + HALO], out.at[NF + NG]),
    ]
    copies = [pltpu.make_async_copy(s, d, sem.at[k]) for k, (s, d) in enumerate(parts)]
    for c in copies:
        c.start()
    out[NF + NG + 1] = sld[lo:lo + HALO].astype(jnp.float32)
    for c in copies:
        c.wait()


def shards(populations, solute, mineral, solid, plane_moves):
    planes = populations.shape[1]
    cap = planes + 2 * MOVE_MOST
    ext = planes + 2 * HALO + 2
    count = lax.axis_size("blk")
    forward = [(i, (i + 1) % count) for i in range(count)]
    backward = [(i, (i - 1) % count) for i in range(count)]

    plane = populations.shape[2:]
    f32 = jnp.float32
    any_spec = pl.BlockSpec(memory_space=pl.ANY)
    vmem = pl.BlockSpec(memory_space=pltpu.VMEM)
    smem = pl.BlockSpec(memory_space=pltpu.SMEM)

    def edge(lo):
        return pl.pallas_call(
            functools.partial(edge_kernel, lo),
            out_shape=jax.ShapeDtypeStruct((NF + NG + 2, HALO) + plane, f32),
            in_specs=[any_spec, any_spec, any_spec, vmem],
            out_specs=vmem,
            scratch_shapes=[pltpu.SemaphoreType.DMA((3,))],
        )(populations, solute, mineral, solid)

    halo_lo = lax.ppermute(edge(planes - HALO), "blk", forward)
    halo_hi = lax.ppermute(edge(0), "blk", backward)

    up, down = pl.pallas_call(
        flux_kernel,
        out_shape=(
            jax.ShapeDtypeStruct((NFLUX,) + plane, f32),
            jax.ShapeDtypeStruct((NFLUX,) + plane, f32),
        ),
        in_specs=[vmem] * 4,
        out_specs=[vmem] * 2,
        scratch_shapes=[
            pltpu.VMEM((NF, planes) + plane, f32),
            pltpu.VMEM((NG, planes) + plane, f32),
            pltpu.VMEM((NF, planes) + plane, f32),
            pltpu.VMEM((NG, planes) + plane, f32),
        ]
        + [pltpu.VMEM((planes,) + plane, f32)] * 5,
    )(populations, solute, mineral, solid)
    flux_lo = lax.ppermute(up, "blk", forward)
    flux_hi = lax.ppermute(down, "blk", backward)

    me = lax.axis_index("blk")
    from_low = plane_moves[jnp.mod(me - 1, count), 1]
    send_low = plane_moves[me, 0]
    send_high = plane_moves[me, 1]
    from_high = plane_moves[jnp.mod(me + 1, count), 0]
    mv = jnp.stack([from_low, send_low, send_high, from_high]).astype(jnp.int32)

    return pl.pallas_call(
        main_kernel,
        out_shape=(
            jax.ShapeDtypeStruct((NF, cap) + plane, f32),
            jax.ShapeDtypeStruct((NG, cap) + plane, f32),
            jax.ShapeDtypeStruct((cap,) + plane, f32),
            jax.ShapeDtypeStruct((cap,) + plane, jnp.int32),
        ),
        in_specs=[smem, any_spec, any_spec, any_spec, vmem, any_spec, any_spec, vmem, vmem],
        out_specs=[any_spec] * 4,
        scratch_shapes=[
            pltpu.VMEM((NF, ext) + plane, f32),
            pltpu.VMEM((NG, ext) + plane, f32),
            pltpu.VMEM((NF, ext) + plane, f32),
            pltpu.VMEM((NG, ext) + plane, f32),
            pltpu.VMEM((ext,) + plane, f32),
            pltpu.VMEM((ext,) + plane, f32),
            pltpu.VMEM((ext,) + plane, f32),
            pltpu.VMEM((ext,) + plane, jnp.int32),
            pltpu.VMEM((ext,) + plane, f32),
            pltpu.VMEM((ext,) + plane, f32),
            pltpu.VMEM((ext,) + plane, f32),
            pltpu.VMEM((NF,) + plane, f32),
            pltpu.VMEM(plane, jnp.int32),
            pltpu.VMEM((len(SHIFTS), ext) + plane, f32),
            pltpu.SemaphoreType.DMA((11,)),
            pltpu.SemaphoreType.DMA((ext, 4)),
            pltpu.SemaphoreType.DMA((cap, 4)),
        ],
        compiler_params=pltpu.CompilerParams(vmem_limit_bytes=50 * 1024 * 1024),
    )(mv, populations, solute, mineral, solid, halo_lo, halo_hi, flux_lo, flux_hi)


def solution(mesh):
    return jax.shard_map(
        shards,
        mesh=mesh,
        in_specs=(
            P(None, "blk", None, None),
            P(None, "blk", None, None),
            P("blk", None, None),
            P("blk", None, None),
            P(),
        ),
        out_specs=(
            P(None, "blk", None, None),
            P(None, "blk", None, None),
            P("blk", None, None),
            P("blk", None, None),
        ),
        check_vma=False,
    )
```

```python
import functools

import jax
import jax.numpy as jnp
from jax import lax
from jax.experimental import pallas as pl
from jax.experimental.pallas import tpu as pltpu
from jax.sharding import PartitionSpec as P

MOVE_MOST = 3
HALO = 3

flow_vel = [
    (0, 0, 1),
    (1, 0, 1),
    (-1, 0, 1),
    (0, 1, 1),
    (0, -1, 1),
    (0, 0, -1),
    (1, 0, -1),
    (-1, 0, -1),
    (0, 1, -1),
    (0, -1, -1),
    (0, 0, 0),
    (1, 0, 0),
    (-1, 0, 0),
    (0, 1, 0),
    (0, -1, 0),
    (1, 1, 0),
    (-1, -1, 0),
    (1, -1, 0),
    (-1, 1, 0),
]
flow_weight = [
    1.0 / 18,
    1.0 / 36,
    1.0 / 36,
    1.0 / 36,
    1.0 / 36,
    1.0 / 18,
    1.0 / 36,
    1.0 / 36,
    1.0 / 36,
    1.0 / 36,
    1.0 / 3,
    1.0 / 18,
    1.0 / 18,
    1.0 / 18,
    1.0 / 18,
    1.0 / 36,
    1.0 / 36,
    1.0 / 36,
    1.0 / 36,
]
acid_vel = [(0, 0, 1), (0, 0, -1), (0, 0, 0), (1, 0, 0), (-1, 0, 0), (0, 1, 0), (0, -1, 0)]
acid_weight = [0.125, 0.125, 0.25, 0.125, 0.125, 0.125, 0.125]
relax_flow = 1.25
relax_acid = 0.8
body_force = 0.001
react_rate = 0.1
dissolve_rate = 0.5

NF = len(flow_vel)
NG = len(acid_vel)


def roll_xy(a, cx, cy):
    if cx:
        a = pltpu.roll(a, cx % a.shape[0], 0)
    if cy:
        a = pltpu.roll(a, cy % a.shape[1], 1)
    return a


def face_sum(ref, i):
    mid = ref[i]
    total = ref[i - 1] + ref[i + 1]
    total = total + (roll_xy(mid, 1, 0) + roll_xy(mid, -1, 0))
    return total + (roll_xy(mid, 0, 1) + roll_xy(mid, 0, -1))


def edge_state(sx, gx, mx, cx, sm, cf, i):
    conc = gx[0, i]
    for j in range(1, NG):
        conc = conc + gx[j, i]
    cx[i] = conc
    solid = sx[i] > 0.5
    sm[i] = jnp.where(solid, mx[i], 0.0)
    cf[i] = jnp.where(solid, 0.0, conc)


def collide_plane(fx, gx, sx, cx, sm, fs, gs, i):
    solid = sx[i] > 0.5
    f = [fx[q, i] for q in range(NF)]
    density = f[0]
    for q in range(1, NF):
        density = density + f[q]
    moments = []
    for axis in range(3):
        total = None
        for q, vel in enumerate(flow_vel):
            if vel[axis] == 0:
                continue
            term = f[q] if vel[axis] > 0 else -f[q]
            total = term if total is None else total + term
        moments.append(total)
    inv = 1.0 / density
    comps = [m * inv for m in moments]
    base = 1.0 - 1.5 * (comps[0] * comps[0] + comps[1] * comps[1] + comps[2] * comps[2])
    keep = 1.0 - 1.0 / relax_flow
    scaled = {}
    for w in set(flow_weight):
        scaled[w] = (w / relax_flow) * density

    def along(vel):
        total = None
        for axis in range(3):
            if vel[axis] == 0:
                continue
            term = comps[axis] if vel[axis] > 0 else -comps[axis]
            total = term if total is None else total + term
        return total

    done = set()
    for q, vel in enumerate(flow_vel):
        if q in done:
            continue
        opp = flow_vel.index(tuple(-c for c in vel))
        done |= {q, opp}
        weight = scaled[flow_weight[q]]
        if opp == q:
            fs[q, i] = jnp.where(solid, f[q], keep * f[q] + weight * base)
            continue
        cu = along(vel)
        even = base + 4.5 * (cu * cu)
        odd = 3.0 * cu
        if vel[2]:
            odd = odd + 3.0 * body_force * relax_flow * vel[2]
        for member, poly in ((q, even + odd), (opp, even - odd)):
            fs[member, i] = jnp.where(solid, f[member], keep * f[member] + weight * poly)
    conc = cx[i]
    sink = (react_rate * conc) * face_sum(sm, i)
    rate = 1.0 / relax_acid
    shared = rate * conc - sink
    slope = (4.0 * rate) * conc
    done = set()
    for j, vel in enumerate(acid_vel):
        if j in done:
            continue
        opp = acid_vel.index(tuple(-c for c in vel))
        done |= {j, opp}
        if opp == j:
            parts = ((j, shared),)
        else:
            cu = slope * along(vel)
            parts = ((j, shared + cu), (opp, shared - cu))
        for member, inner in parts:
            g = gx[member, i]
            relaxed = acid_weight[member] * inner - (rate - 1.0) * g
            gs[member, i] = jnp.where(solid, g, relaxed)


def dissolve_plane(sx, mx_src, cf, mx_dst, i):
    solid = sx[i] > 0.5
    mineral = mx_src[i]
    loss = (dissolve_rate * react_rate) * mineral * face_sum(cf, i)
    mx_dst[i] = jnp.where(solid, mineral - loss, mineral)


SHIFTS = [(cx, cy) for cx in (-1, 0, 1) for cy in (-1, 0, 1) if cx or cy]


def shift_masks(sx, bm, i):
    for c, (cx, cy) in enumerate(SHIFTS):
        bm[c, i] = roll_xy(sx[i], cx, cy)


def stream_plane(fs, gs, sx, fdst, gdst, i, bm=None):
    solid = sx[i] > 0.5
    masks = {}
    for q, vel in enumerate(flow_vel):
        cx, cy, cz = vel
        if vel == (0, 0, 0):
            fdst[q, i] = fs[q, i]
            continue
        opp = flow_vel.index((-cx, -cy, -cz))
        src = i - cz
        pulled = roll_xy(fs[q, src], cx, cy)
        if bm is None or (cx, cy) == (0, 0):
            blocked = roll_xy(sx[src], cx, cy) > 0.5
        else:
            blocked = bm[SHIFTS.index((cx, cy)), src] > 0.5
        masks[vel] = blocked
        arrived = jnp.where(blocked, fs[opp, i], pulled)
        fdst[q, i] = jnp.where(solid, fs[q, i], arrived)
    for j, vel in enumerate(acid_vel):
        cx, cy, cz = vel
        if vel == (0, 0, 0):
            gdst[j, i] = gs[j, i]
            continue
        opp = acid_vel.index((-cx, -cy, -cz))
        pulled = roll_xy(gs[j, i - cz], cx, cy)
        arrived = jnp.where(masks[vel], gs[opp, i], pulled)
        gdst[j, i] = jnp.where(solid, gs[j, i], arrived)


def loop(lo, hi, fn):
    def body(i, carry):
        fn(i)
        return carry

    lax.fori_loop(lo, hi, body, 0)


UP_Q = [q for q, vel in enumerate(flow_vel) if vel[2] == 1]
DOWN_Q = [q for q, vel in enumerate(flow_vel) if vel[2] == -1]
UP_J = acid_vel.index((0, 0, 1))
DOWN_J = acid_vel.index((0, 0, -1))
NFLUX = 3 + 2 * (len(UP_Q) + 1) + 2


def flux_kernel(pop, sol, mnr, sld, up, down, fs, gs, f1, g1, m1, sx, cx, sm, cf):
    planes = sld.shape[0]
    hi, lo = planes - HALO - 1, HALO
    sx[...] = sld[...].astype(jnp.float32)
    loop(lo - 2, hi + 3, lambda i: edge_state(sx, sol, mnr, cx, sm, cf, i))

    def step1(i):
        dissolve_plane(sx, mnr, cf, m1, i)
        collide_plane(pop, sol, sx, cx, sm, fs, gs, i)

    loop(lo - 1, hi + 2, step1)
    for dst, i, qs, j in ((up, hi, UP_Q, UP_J), (down, lo, DOWN_Q, DOWN_J)):
        dst[0] = sx[i]
        dst[1] = sm[i]
        dst[2] = cf[i]
        for n, q in enumerate(qs):
            dst[3 + n] = fs[q, i]
        dst[3 + len(qs)] = gs[j, i]
    loop(lo, hi + 1, lambda i: stream_plane(fs, gs, sx, f1, g1, i))
    for i in range(lo - 1, hi + 2):
        sm[i] = jnp.where(sx[i] > 0.5, m1[i], 0.0)
    for i in range(lo, hi + 1):
        conc = g1[0, i]
        for j in range(1, NG):
            conc = conc + g1[j, i]
        cx[i] = conc
        cf[i] = jnp.where(sx[i] > 0.5, 0.0, conc)
    loop(lo, hi + 1, lambda i: collide_plane(f1, g1, sx, cx, sm, fs, gs, i))
    base = 4 + len(UP_Q)
    for dst, i, qs, j in ((up, hi, UP_Q, UP_J), (down, lo, DOWN_Q, DOWN_J)):
        dst[base] = sm[i]
        dst[base + 1] = cf[i]
        for n, q in enumerate(qs):
            dst[base + 2 + n] = fs[q, i]
        dst[base + 2 + len(qs)] = gs[j, i]


def set_bounds(flo, fhi, sm, cf, fs, gs, last, base):
    sm[0] = flo[base]
    cf[0] = flo[base + 1]
    sm[last] = fhi[base]
    cf[last] = fhi[base + 1]

    def posts():
        for n, q in enumerate(UP_Q):
            fs[q, 0] = flo[base + 2 + n]
        gs[UP_J, 0] = flo[base + 2 + len(UP_Q)]
        for n, q in enumerate(DOWN_Q):
            fs[q, last] = fhi[base + 2 + n]
        gs[DOWN_J, last] = fhi[base + 2 + len(DOWN_Q)]

    return posts


def main_kernel(
    mv, pop, sol, mnr, sld, hlo, hhi, flo, fhi,
    out_f, out_g, out_m, out_s,
    fx, gx, fs, gs, mx, m1, sx, si, cx, sm, cf, zf, zi, bm, sem, osem, zsem,
):
    planes = sld.shape[0]
    cap = out_s.shape[0]
    last = planes + 2 * HALO + 1
    own = HALO + 1
    top = own + planes
    fill = [
        (pop, fx.at[:, own:top]),
        (sol, gx.at[:, own:top]),
        (mnr, mx.at[own:top]),
        (hlo.at[0:NF], fx.at[:, 1:own]),
        (hlo.at[NF:NF + NG], gx.at[:, 1:own]),
        (hlo.at[NF + NG], mx.at[1:own]),
        (hlo.at[NF + NG + 1], sx.at[1:own]),
        (hhi.at[0:NF], fx.at[:, top:last]),
        (hhi.at[NF:NF + NG], gx.at[:, top:last]),
        (hhi.at[NF + NG], mx.at[top:last]),
        (hhi.at[NF + NG + 1], sx.at[top:last]),
    ]
    copies = [pltpu.make_async_copy(s, d, sem.at[k]) for k, (s, d) in enumerate(fill)]
    for c in copies:
        c.start()
    sx[own:top] = sld[...].astype(jnp.float32)
    si[own:top] = sld[...]
    sx[0] = flo[0]
    sx[last] = fhi[0]
    zf[...] = jnp.zeros(zf.shape, zf.dtype)
    zi[...] = jnp.zeros(zi.shape, zi.dtype)
    for c in copies:
        c.wait()
    si[1:own] = (sx[1:own] > 0.5).astype(jnp.int32)
    si[top:last] = (sx[top:last] > 0.5).astype(jnp.int32)

    from_low, send_low, send_high, from_high = mv[0], mv[1], mv[2], mv[3]
    valid_end = from_low + planes - send_low - send_high + from_high

    def plane_valid(i):
        p = i - own
        low = (p >= -from_low) & (p < 0)
        kept = (p >= send_low) & (p < planes - send_high)
        high = (p >= planes) & (p < planes + from_high)
        return low | kept | high

    def plane_copies(i):
        p = i - own
        s = p + from_low - jnp.where(p >= send_low, send_low, 0) - jnp.where(p >= planes, send_high, 0)
        s = jnp.clip(s, 0, cap - 1)
        srcs = (fx.at[:, i], gx.at[:, i], mx.at[i], si.at[i])
        dsts = (out_f.at[:, s], out_g.at[:, s], out_m.at[s], out_s.at[s])
        return [pltpu.make_async_copy(x, y, osem.at[i, k]) for k, (x, y) in enumerate(zip(srcs, dsts))]

    def zero_copies(s):
        srcs = (zf, zf.at[0:NG], zf.at[0], zi)
        dsts = (out_f.at[:, s], out_g.at[:, s], out_m.at[s], out_s.at[s])
        return [pltpu.make_async_copy(x, y, zsem.at[s, k]) for k, (x, y) in enumerate(zip(srcs, dsts))]

    for s in range(cap):
        @pl.when(s >= valid_end)
        def _():
            for c in zero_copies(s):
                c.start()

    loop(0, last + 1, lambda i: shift_masks(sx, bm, i))

    posts = set_bounds(flo, fhi, sm, cf, fs, gs, last, 1)
    loop(1, last, lambda i: edge_state(sx, gx, mx, cx, sm, cf, i))

    def step1(i):
        dissolve_plane(sx, mx, cf, m1, i)
        collide_plane(fx, gx, sx, cx, sm, fs, gs, i)

    loop(1, last, step1)
    posts()
    loop(1, last, lambda i: stream_plane(fs, gs, sx, fx, gx, i, bm))

    posts = set_bounds(flo, fhi, sm, cf, fs, gs, last, 4 + len(UP_Q))
    loop(1, last, lambda i: edge_state(sx, gx, m1, cx, sm, cf, i))

    def step2(i):
        dissolve_plane(sx, m1, cf, mx, i)
        collide_plane(fx, gx, sx, cx, sm, fs, gs, i)

    loop(1, last, step2)
    posts()

    def send_plane(i):
        @pl.when(plane_valid(i))
        def _():
            for c in plane_copies(i):
                c.start()

    def final(i):
        stream_plane(fs, gs, sx, fx, gx, i, bm)

        @pl.when(i > 1)
        def _():
            send_plane(i - 1)

    loop(1, last, final)
    send_plane(last - 1)
    for i in range(1, last):
        @pl.when(plane_valid(i))
        def _():
            for c in plane_copies(i):
                c.wait()
    for s in range(cap):
        @pl.when(s >= valid_end)
        def _():
            for c in zero_copies(s):
                c.wait()


def edge_kernel(pop, sol, mnr, sld, top_out, bottom_out, sem):
    planes = sld.shape[0]
    copies = []
    for n, (lo, out) in enumerate(((planes - HALO, top_out), (0, bottom_out))):
        parts = [
            (pop.at[:, lo:lo + HALO], out.at[0:NF]),
            (sol.at[:, lo:lo + HALO], out.at[NF:NF + NG]),
            (mnr.at[lo:lo + HALO], out.at[NF + NG]),
        ]
        copies += [pltpu.make_async_copy(s, d, sem.at[n, k]) for k, (s, d) in enumerate(parts)]
    for c in copies:
        c.start()
    top_out[NF + NG + 1] = sld[planes - HALO:planes].astype(jnp.float32)
    bottom_out[NF + NG + 1] = sld[0:HALO].astype(jnp.float32)
    for c in copies:
        c.wait()


def shards(populations, solute, mineral, solid, plane_moves):
    planes = populations.shape[1]
    cap = planes + 2 * MOVE_MOST
    ext = planes + 2 * HALO + 2
    count = lax.axis_size("blk")
    forward = [(i, (i + 1) % count) for i in range(count)]
    backward = [(i, (i - 1) % count) for i in range(count)]

    plane = populations.shape[2:]
    f32 = jnp.float32
    any_spec = pl.BlockSpec(memory_space=pl.ANY)
    vmem = pl.BlockSpec(memory_space=pltpu.VMEM)
    smem = pl.BlockSpec(memory_space=pltpu.SMEM)

    top_edge, bottom_edge = pl.pallas_call(
        edge_kernel,
        out_shape=(
            jax.ShapeDtypeStruct((NF + NG + 2, HALO) + plane, f32),
            jax.ShapeDtypeStruct((NF + NG + 2, HALO) + plane, f32),
        ),
        in_specs=[any_spec, any_spec, any_spec, vmem],
        out_specs=[vmem, vmem],
        scratch_shapes=[pltpu.SemaphoreType.DMA((2, 3))],
    )(populations, solute, mineral, solid)
    halo_lo = lax.ppermute(top_edge, "blk", forward)
    halo_hi = lax.ppermute(bottom_edge, "blk", backward)

    up, down = pl.pallas_call(
        flux_kernel,
        out_shape=(
            jax.ShapeDtypeStruct((NFLUX,) + plane, f32),
            jax.ShapeDtypeStruct((NFLUX,) + plane, f32),
        ),
        in_specs=[vmem] * 4,
        out_specs=[vmem] * 2,
        scratch_shapes=[
            pltpu.VMEM((NF, planes) + plane, f32),
            pltpu.VMEM((NG, planes) + plane, f32),
            pltpu.VMEM((NF, planes) + plane, f32),
            pltpu.VMEM((NG, planes) + plane, f32),
        ]
        + [pltpu.VMEM((planes,) + plane, f32)] * 5,
    )(populations, solute, mineral, solid)
    flux_lo = lax.ppermute(up, "blk", forward)
    flux_hi = lax.ppermute(down, "blk", backward)

    me = lax.axis_index("blk")
    from_low = plane_moves[jnp.mod(me - 1, count), 1]
    send_low = plane_moves[me, 0]
    send_high = plane_moves[me, 1]
    from_high = plane_moves[jnp.mod(me + 1, count), 0]
    mv = jnp.stack([from_low, send_low, send_high, from_high]).astype(jnp.int32)

    return pl.pallas_call(
        main_kernel,
        out_shape=(
            jax.ShapeDtypeStruct((NF, cap) + plane, f32),
            jax.ShapeDtypeStruct((NG, cap) + plane, f32),
            jax.ShapeDtypeStruct((cap,) + plane, f32),
            jax.ShapeDtypeStruct((cap,) + plane, jnp.int32),
        ),
        in_specs=[smem, any_spec, any_spec, any_spec, vmem, any_spec, any_spec, vmem, vmem],
        out_specs=[any_spec] * 4,
        scratch_shapes=[
            pltpu.VMEM((NF, ext) + plane, f32),
            pltpu.VMEM((NG, ext) + plane, f32),
            pltpu.VMEM((NF, ext) + plane, f32),
            pltpu.VMEM((NG, ext) + plane, f32),
            pltpu.VMEM((ext,) + plane, f32),
            pltpu.VMEM((ext,) + plane, f32),
            pltpu.VMEM((ext,) + plane, f32),
            pltpu.VMEM((ext,) + plane, jnp.int32),
            pltpu.VMEM((ext,) + plane, f32),
            pltpu.VMEM((ext,) + plane, f32),
            pltpu.VMEM((ext,) + plane, f32),
            pltpu.VMEM((NF,) + plane, f32),
            pltpu.VMEM(plane, jnp.int32),
            pltpu.VMEM((len(SHIFTS), ext) + plane, f32),
            pltpu.SemaphoreType.DMA((11,)),
            pltpu.SemaphoreType.DMA((ext, 4)),
            pltpu.SemaphoreType.DMA((cap, 4)),
        ],
        compiler_params=pltpu.CompilerParams(vmem_limit_bytes=50 * 1024 * 1024),
    )(mv, populations, solute, mineral, solid, halo_lo, halo_hi, flux_lo, flux_hi)


def solution(mesh):
    return jax.shard_map(
        shards,
        mesh=mesh,
        in_specs=(
            P(None, "blk", None, None),
            P(None, "blk", None, None),
            P("blk", None, None),
            P("blk", None, None),
            P(),
        ),
        out_specs=(
            P(None, "blk", None, None),
            P(None, "blk", None, None),
            P("blk", None, None),
            P("blk", None, None),
        ),
        check_vma=False,
    )
```

```python
import functools

import jax
import jax.numpy as jnp
from jax import lax
from jax.experimental import pallas as pl
from jax.experimental.pallas import tpu as pltpu
from jax.sharding import PartitionSpec as P

MOVE_MOST = 3
HALO = 3

flow_vel = [
    (0, 0, 1),
    (1, 0, 1),
    (-1, 0, 1),
    (0, 1, 1),
    (0, -1, 1),
    (0, 0, -1),
    (1, 0, -1),
    (-1, 0, -1),
    (0, 1, -1),
    (0, -1, -1),
    (0, 0, 0),
    (1, 0, 0),
    (-1, 0, 0),
    (0, 1, 0),
    (0, -1, 0),
    (1, 1, 0),
    (-1, -1, 0),
    (1, -1, 0),
    (-1, 1, 0),
]
flow_weight = [
    1.0 / 18,
    1.0 / 36,
    1.0 / 36,
    1.0 / 36,
    1.0 / 36,
    1.0 / 18,
    1.0 / 36,
    1.0 / 36,
    1.0 / 36,
    1.0 / 36,
    1.0 / 3,
    1.0 / 18,
    1.0 / 18,
    1.0 / 18,
    1.0 / 18,
    1.0 / 36,
    1.0 / 36,
    1.0 / 36,
    1.0 / 36,
]
acid_vel = [(0, 0, 1), (0, 0, -1), (0, 0, 0), (1, 0, 0), (-1, 0, 0), (0, 1, 0), (0, -1, 0)]
acid_weight = [0.125, 0.125, 0.25, 0.125, 0.125, 0.125, 0.125]
relax_flow = 1.25
relax_acid = 0.8
body_force = 0.001
react_rate = 0.1
dissolve_rate = 0.5

NF = len(flow_vel)
NG = len(acid_vel)


def roll_xy(a, cx, cy):
    if cx:
        a = pltpu.roll(a, cx % a.shape[0], 0)
    if cy:
        a = pltpu.roll(a, cy % a.shape[1], 1)
    return a


def face_sum(ref, i):
    mid = ref[i]
    total = ref[i - 1] + ref[i + 1]
    total = total + (roll_xy(mid, 1, 0) + roll_xy(mid, -1, 0))
    return total + (roll_xy(mid, 0, 1) + roll_xy(mid, 0, -1))


def edge_state(sx, gx, mx, cx, sm, cf, i):
    conc = gx[0, i]
    for j in range(1, NG):
        conc = conc + gx[j, i]
    cx[i] = conc
    solid = sx[i] > 0.5
    sm[i] = jnp.where(solid, mx[i], 0.0)
    cf[i] = jnp.where(solid, 0.0, conc)


def collide_plane(fx, gx, sx, cx, sm, fs, gs, i):
    solid = sx[i] > 0.5
    f = [fx[q, i] for q in range(NF)]
    density = f[0]
    for q in range(1, NF):
        density = density + f[q]
    moments = []
    for axis in range(3):
        total = None
        for q, vel in enumerate(flow_vel):
            if vel[axis] == 0:
                continue
            term = f[q] if vel[axis] > 0 else -f[q]
            total = term if total is None else total + term
        moments.append(total)
    inv = 1.0 / density
    comps = [m * inv for m in moments]
    base = 1.0 - 1.5 * (comps[0] * comps[0] + comps[1] * comps[1] + comps[2] * comps[2])
    keep = 1.0 - 1.0 / relax_flow
    scaled = {}
    for w in set(flow_weight):
        scaled[w] = (w / relax_flow) * density

    def along(vel):
        total = None
        for axis in range(3):
            if vel[axis] == 0:
                continue
            term = comps[axis] if vel[axis] > 0 else -comps[axis]
            total = term if total is None else total + term
        return total

    done = set()
    for q, vel in enumerate(flow_vel):
        if q in done:
            continue
        opp = flow_vel.index(tuple(-c for c in vel))
        done |= {q, opp}
        weight = scaled[flow_weight[q]]
        if opp == q:
            fs[q, i] = jnp.where(solid, f[q], keep * f[q] + weight * base)
            continue
        cu = along(vel)
        even = base + 4.5 * (cu * cu)
        odd = 3.0 * cu
        if vel[2]:
            odd = odd + 3.0 * body_force * relax_flow * vel[2]
        for member, poly in ((q, even + odd), (opp, even - odd)):
            fs[member, i] = jnp.where(solid, f[member], keep * f[member] + weight * poly)
    conc = cx[i]
    sink = (react_rate * conc) * face_sum(sm, i)
    rate = 1.0 / relax_acid
    shared = rate * conc - sink
    slope = (4.0 * rate) * conc
    done = set()
    for j, vel in enumerate(acid_vel):
        if j in done:
            continue
        opp = acid_vel.index(tuple(-c for c in vel))
        done |= {j, opp}
        if opp == j:
            parts = ((j, shared),)
        else:
            cu = slope * along(vel)
            parts = ((j, shared + cu), (opp, shared - cu))
        for member, inner in parts:
            g = gx[member, i]
            relaxed = acid_weight[member] * inner - (rate - 1.0) * g
            gs[member, i] = jnp.where(solid, g, relaxed)


def dissolve_plane(sx, mx_src, cf, mx_dst, i):
    solid = sx[i] > 0.5
    mineral = mx_src[i]
    loss = (dissolve_rate * react_rate) * mineral * face_sum(cf, i)
    mx_dst[i] = jnp.where(solid, mineral - loss, mineral)


SHIFTS = [(cx, cy) for cx in (-1, 0, 1) for cy in (-1, 0, 1) if cx or cy]


def shift_masks(sx, bm, i):
    for c, (cx, cy) in enumerate(SHIFTS):
        bm[c, i] = roll_xy(sx[i], cx, cy)


def stream_plane(fs, gs, sx, fdst, gdst, i, bm=None):
    solid = sx[i] > 0.5
    masks = {}
    for q, vel in enumerate(flow_vel):
        cx, cy, cz = vel
        if vel == (0, 0, 0):
            fdst[q, i] = fs[q, i]
            continue
        opp = flow_vel.index((-cx, -cy, -cz))
        src = i - cz
        pulled = roll_xy(fs[q, src], cx, cy)
        if bm is None or (cx, cy) == (0, 0):
            blocked = roll_xy(sx[src], cx, cy) > 0.5
        else:
            blocked = bm[SHIFTS.index((cx, cy)), src] > 0.5
        masks[vel] = blocked
        arrived = jnp.where(blocked, fs[opp, i], pulled)
        fdst[q, i] = jnp.where(solid, fs[q, i], arrived)
    for j, vel in enumerate(acid_vel):
        cx, cy, cz = vel
        if vel == (0, 0, 0):
            gdst[j, i] = gs[j, i]
            continue
        opp = acid_vel.index((-cx, -cy, -cz))
        pulled = roll_xy(gs[j, i - cz], cx, cy)
        arrived = jnp.where(masks[vel], gs[opp, i], pulled)
        gdst[j, i] = jnp.where(solid, gs[j, i], arrived)


def loop(lo, hi, fn):
    def body(i, carry):
        fn(i)
        return carry

    lax.fori_loop(lo, hi, body, 0)


UP_Q = [q for q, vel in enumerate(flow_vel) if vel[2] == 1]
DOWN_Q = [q for q, vel in enumerate(flow_vel) if vel[2] == -1]
UP_J = acid_vel.index((0, 0, 1))
DOWN_J = acid_vel.index((0, 0, -1))
NFLUX = 3 + 2 * (len(UP_Q) + 1) + 2


def flux_kernel(pop, sol, mnr, sld, up, down, fs, gs, f1, g1, m1, sx, cx, sm, cf):
    planes = sld.shape[0]
    hi, lo = planes - HALO - 1, HALO
    sx[...] = sld[...].astype(jnp.float32)
    loop(lo - 2, hi + 3, lambda i: edge_state(sx, sol, mnr, cx, sm, cf, i))

    def step1(i):
        dissolve_plane(sx, mnr, cf, m1, i)
        collide_plane(pop, sol, sx, cx, sm, fs, gs, i)

    loop(lo - 1, hi + 2, step1)
    for dst, i, qs, j in ((up, hi, UP_Q, UP_J), (down, lo, DOWN_Q, DOWN_J)):
        dst[0] = sx[i]
        dst[1] = sm[i]
        dst[2] = cf[i]
        for n, q in enumerate(qs):
            dst[3 + n] = fs[q, i]
        dst[3 + len(qs)] = gs[j, i]
    loop(lo, hi + 1, lambda i: stream_plane(fs, gs, sx, f1, g1, i))
    for i in range(lo - 1, hi + 2):
        sm[i] = jnp.where(sx[i] > 0.5, m1[i], 0.0)
    for i in range(lo, hi + 1):
        conc = g1[0, i]
        for j in range(1, NG):
            conc = conc + g1[j, i]
        cx[i] = conc
        cf[i] = jnp.where(sx[i] > 0.5, 0.0, conc)
    loop(lo, hi + 1, lambda i: collide_plane(f1, g1, sx, cx, sm, fs, gs, i))
    base = 4 + len(UP_Q)
    for dst, i, qs, j in ((up, hi, UP_Q, UP_J), (down, lo, DOWN_Q, DOWN_J)):
        dst[base] = sm[i]
        dst[base + 1] = cf[i]
        for n, q in enumerate(qs):
            dst[base + 2 + n] = fs[q, i]
        dst[base + 2 + len(qs)] = gs[j, i]
    up[NFLUX:NFLUX + HALO] = sx[planes - HALO:planes]
    down[NFLUX:NFLUX + HALO] = sx[0:HALO]


def set_bounds(flo, fhi, sm, cf, fs, gs, last, base):
    sm[0] = flo[base]
    cf[0] = flo[base + 1]
    sm[last] = fhi[base]
    cf[last] = fhi[base + 1]

    def posts():
        for n, q in enumerate(UP_Q):
            fs[q, 0] = flo[base + 2 + n]
        gs[UP_J, 0] = flo[base + 2 + len(UP_Q)]
        for n, q in enumerate(DOWN_Q):
            fs[q, last] = fhi[base + 2 + n]
        gs[DOWN_J, last] = fhi[base + 2 + len(DOWN_Q)]

    return posts


def main_kernel(
    mv, pop, sol, mnr, sld, hlo, hhi, flo, fhi,
    out_f, out_g, out_m, out_s,
    fx, gx, fs, gs, mx, m1, sx, si, cx, sm, cf, zf, zi, bm, sem, osem, zsem,
):
    planes = sld.shape[0]
    cap = out_s.shape[0]
    last = planes + 2 * HALO + 1
    own = HALO + 1
    top = own + planes
    fill = [
        (pop, fx.at[:, own:top]),
        (sol, gx.at[:, own:top]),
        (mnr, mx.at[own:top]),
        (hlo.at[0:NF], fx.at[:, 1:own]),
        (hlo.at[NF:NF + NG], gx.at[:, 1:own]),
        (hlo.at[NF + NG], mx.at[1:own]),
        (hhi.at[0:NF], fx.at[:, top:last]),
        (hhi.at[NF:NF + NG], gx.at[:, top:last]),
        (hhi.at[NF + NG], mx.at[top:last]),
    ]
    copies = [pltpu.make_async_copy(s, d, sem.at[k]) for k, (s, d) in enumerate(fill)]
    for c in copies:
        c.start()
    sx[own:top] = sld[...].astype(jnp.float32)
    si[own:top] = sld[...]
    sx[0] = flo[0]
    sx[last] = fhi[0]
    sx[1:own] = flo[NFLUX:NFLUX + HALO]
    sx[top:last] = fhi[NFLUX:NFLUX + HALO]
    zf[...] = jnp.zeros(zf.shape, zf.dtype)
    zi[...] = jnp.zeros(zi.shape, zi.dtype)
    for c in copies:
        c.wait()
    si[1:own] = (sx[1:own] > 0.5).astype(jnp.int32)
    si[top:last] = (sx[top:last] > 0.5).astype(jnp.int32)

    from_low, send_low, send_high, from_high = mv[0], mv[1], mv[2], mv[3]
    valid_end = from_low + planes - send_low - send_high + from_high

    def plane_valid(i):
        p = i - own
        low = (p >= -from_low) & (p < 0)
        kept = (p >= send_low) & (p < planes - send_high)
        high = (p >= planes) & (p < planes + from_high)
        return low | kept | high

    def plane_copies(i):
        p = i - own
        s = p + from_low - jnp.where(p >= send_low, send_low, 0) - jnp.where(p >= planes, send_high, 0)
        s = jnp.clip(s, 0, cap - 1)
        srcs = (fx.at[:, i], gx.at[:, i], mx.at[i], si.at[i])
        dsts = (out_f.at[:, s], out_g.at[:, s], out_m.at[s], out_s.at[s])
        return [pltpu.make_async_copy(x, y, osem.at[i, k]) for k, (x, y) in enumerate(zip(srcs, dsts))]

    def zero_copies(s):
        srcs = (zf, zf.at[0:NG], zf.at[0], zi)
        dsts = (out_f.at[:, s], out_g.at[:, s], out_m.at[s], out_s.at[s])
        return [pltpu.make_async_copy(x, y, zsem.at[s, k]) for k, (x, y) in enumerate(zip(srcs, dsts))]

    for s in range(cap):
        @pl.when(s >= valid_end)
        def _():
            for c in zero_copies(s):
                c.start()

    loop(0, last + 1, lambda i: shift_masks(sx, bm, i))

    posts = set_bounds(flo, fhi, sm, cf, fs, gs, last, 1)
    loop(1, last, lambda i: edge_state(sx, gx, mx, cx, sm, cf, i))

    def step1(i):
        dissolve_plane(sx, mx, cf, m1, i)
        collide_plane(fx, gx, sx, cx, sm, fs, gs, i)

    loop(1, last, step1)
    posts()
    loop(1, last, lambda i: stream_plane(fs, gs, sx, fx, gx, i, bm))

    posts = set_bounds(flo, fhi, sm, cf, fs, gs, last, 4 + len(UP_Q))
    loop(1, last, lambda i: edge_state(sx, gx, m1, cx, sm, cf, i))

    def step2(i):
        dissolve_plane(sx, m1, cf, mx, i)
        collide_plane(fx, gx, sx, cx, sm, fs, gs, i)

    loop(1, last, step2)
    posts()

    def send_plane(i):
        @pl.when(plane_valid(i))
        def _():
            for c in plane_copies(i):
                c.start()

    def final(i):
        stream_plane(fs, gs, sx, fx, gx, i, bm)

        @pl.when(i > 1)
        def _():
            send_plane(i - 1)

    loop(1, last, final)
    send_plane(last - 1)
    for i in range(1, last):
        @pl.when(plane_valid(i))
        def _():
            for c in plane_copies(i):
                c.wait()
    for s in range(cap):
        @pl.when(s >= valid_end)
        def _():
            for c in zero_copies(s):
                c.wait()


def edge_kernel(lo, pop, sol, mnr, out, sem):
    parts = [
        (pop.at[:, lo:lo + HALO], out.at[0:NF]),
        (sol.at[:, lo:lo + HALO], out.at[NF:NF + NG]),
        (mnr.at[lo:lo + HALO], out.at[NF + NG]),
    ]
    copies = [pltpu.make_async_copy(s, d, sem.at[k]) for k, (s, d) in enumerate(parts)]
    for c in copies:
        c.start()
    for c in copies:
        c.wait()


def shards(populations, solute, mineral, solid, plane_moves):
    planes = populations.shape[1]
    cap = planes + 2 * MOVE_MOST
    ext = planes + 2 * HALO + 2
    count = lax.axis_size("blk")
    forward = [(i, (i + 1) % count) for i in range(count)]
    backward = [(i, (i - 1) % count) for i in range(count)]

    plane = populations.shape[2:]
    f32 = jnp.float32
    any_spec = pl.BlockSpec(memory_space=pl.ANY)
    vmem = pl.BlockSpec(memory_space=pltpu.VMEM)
    smem = pl.BlockSpec(memory_space=pltpu.SMEM)

    def edge(lo):
        return pl.pallas_call(
            functools.partial(edge_kernel, lo),
            out_shape=jax.ShapeDtypeStruct((NF + NG + 1, HALO) + plane, f32),
            in_specs=[any_spec, any_spec, any_spec],
            out_specs=any_spec,
            scratch_shapes=[pltpu.SemaphoreType.DMA((3,))],
        )(populations, solute, mineral)

    halo_lo = lax.ppermute(edge(planes - HALO), "blk", forward)
    halo_hi = lax.ppermute(edge(0), "blk", backward)

    up, down = pl.pallas_call(
        flux_kernel,
        out_shape=(
            jax.ShapeDtypeStruct((NFLUX + HALO,) + plane, f32),
            jax.ShapeDtypeStruct((NFLUX + HALO,) + plane, f32),
        ),
        in_specs=[vmem] * 4,
        out_specs=[vmem] * 2,
        scratch_shapes=[
            pltpu.VMEM((NF, planes) + plane, f32),
            pltpu.VMEM((NG, planes) + plane, f32),
            pltpu.VMEM((NF, planes) + plane, f32),
            pltpu.VMEM((NG, planes) + plane, f32),
        ]
        + [pltpu.VMEM((planes,) + plane, f32)] * 5,
    )(populations, solute, mineral, solid)
    flux_lo = lax.ppermute(up, "blk", forward)
    flux_hi = lax.ppermute(down, "blk", backward)

    me = lax.axis_index("blk")
    from_low = plane_moves[jnp.mod(me - 1, count), 1]
    send_low = plane_moves[me, 0]
    send_high = plane_moves[me, 1]
    from_high = plane_moves[jnp.mod(me + 1, count), 0]
    mv = jnp.stack([from_low, send_low, send_high, from_high]).astype(jnp.int32)

    return pl.pallas_call(
        main_kernel,
        out_shape=(
            jax.ShapeDtypeStruct((NF, cap) + plane, f32),
            jax.ShapeDtypeStruct((NG, cap) + plane, f32),
            jax.ShapeDtypeStruct((cap,) + plane, f32),
            jax.ShapeDtypeStruct((cap,) + plane, jnp.int32),
        ),
        in_specs=[smem, any_spec, any_spec, any_spec, vmem, any_spec, any_spec, vmem, vmem],
        out_specs=[any_spec] * 4,
        scratch_shapes=[
            pltpu.VMEM((NF, ext) + plane, f32),
            pltpu.VMEM((NG, ext) + plane, f32),
            pltpu.VMEM((NF, ext) + plane, f32),
            pltpu.VMEM((NG, ext) + plane, f32),
            pltpu.VMEM((ext,) + plane, f32),
            pltpu.VMEM((ext,) + plane, f32),
            pltpu.VMEM((ext,) + plane, f32),
            pltpu.VMEM((ext,) + plane, jnp.int32),
            pltpu.VMEM((ext,) + plane, f32),
            pltpu.VMEM((ext,) + plane, f32),
            pltpu.VMEM((ext,) + plane, f32),
            pltpu.VMEM((NF,) + plane, f32),
            pltpu.VMEM(plane, jnp.int32),
            pltpu.VMEM((len(SHIFTS), ext) + plane, f32),
            pltpu.SemaphoreType.DMA((9,)),
            pltpu.SemaphoreType.DMA((ext, 4)),
            pltpu.SemaphoreType.DMA((cap, 4)),
        ],
        compiler_params=pltpu.CompilerParams(vmem_limit_bytes=50 * 1024 * 1024),
    )(mv, populations, solute, mineral, solid, halo_lo, halo_hi, flux_lo, flux_hi)


def solution(mesh):
    return jax.shard_map(
        shards,
        mesh=mesh,
        in_specs=(
            P(None, "blk", None, None),
            P(None, "blk", None, None),
            P("blk", None, None),
            P("blk", None, None),
            P(),
        ),
        out_specs=(
            P(None, "blk", None, None),
            P(None, "blk", None, None),
            P("blk", None, None),
            P("blk", None, None),
        ),
        check_vma=False,
    )
```

```python
import functools

import jax
import jax.numpy as jnp
from jax import lax
from jax.experimental import pallas as pl
from jax.experimental.pallas import tpu as pltpu
from jax.sharding import PartitionSpec as P

MOVE_MOST = 3
HALO = 3

flow_vel = [
    (0, 0, 1),
    (1, 0, 1),
    (-1, 0, 1),
    (0, 1, 1),
    (0, -1, 1),
    (0, 0, -1),
    (1, 0, -1),
    (-1, 0, -1),
    (0, 1, -1),
    (0, -1, -1),
    (0, 0, 0),
    (1, 0, 0),
    (-1, 0, 0),
    (0, 1, 0),
    (0, -1, 0),
    (1, 1, 0),
    (-1, -1, 0),
    (1, -1, 0),
    (-1, 1, 0),
]
flow_weight = [
    1.0 / 18,
    1.0 / 36,
    1.0 / 36,
    1.0 / 36,
    1.0 / 36,
    1.0 / 18,
    1.0 / 36,
    1.0 / 36,
    1.0 / 36,
    1.0 / 36,
    1.0 / 3,
    1.0 / 18,
    1.0 / 18,
    1.0 / 18,
    1.0 / 18,
    1.0 / 36,
    1.0 / 36,
    1.0 / 36,
    1.0 / 36,
]
acid_vel = [(0, 0, 1), (0, 0, -1), (0, 0, 0), (1, 0, 0), (-1, 0, 0), (0, 1, 0), (0, -1, 0)]
acid_weight = [0.125, 0.125, 0.25, 0.125, 0.125, 0.125, 0.125]
relax_flow = 1.25
relax_acid = 0.8
body_force = 0.001
react_rate = 0.1
dissolve_rate = 0.5

NF = len(flow_vel)
NG = len(acid_vel)


def roll_xy(a, cx, cy):
    if cx:
        a = pltpu.roll(a, cx % a.shape[0], 0)
    if cy:
        a = pltpu.roll(a, cy % a.shape[1], 1)
    return a


def face_sum(ref, i):
    mid = ref[i]
    total = ref[i - 1] + ref[i + 1]
    total = total + (roll_xy(mid, 1, 0) + roll_xy(mid, -1, 0))
    return total + (roll_xy(mid, 0, 1) + roll_xy(mid, 0, -1))


def edge_state(sx, gx, mx, cx, sm, cf, i):
    conc = gx[0, i]
    for j in range(1, NG):
        conc = conc + gx[j, i]
    cx[i] = conc
    solid = sx[i] > 0.5
    sm[i] = jnp.where(solid, mx[i], 0.0)
    cf[i] = jnp.where(solid, 0.0, conc)


def collide_plane(fx, gx, sx, cx, sm, fs, gs, i):
    solid = sx[i] > 0.5
    f = [fx[q, i] for q in range(NF)]
    density = f[0]
    for q in range(1, NF):
        density = density + f[q]
    moments = []
    for axis in range(3):
        total = None
        for q, vel in enumerate(flow_vel):
            if vel[axis] == 0:
                continue
            term = f[q] if vel[axis] > 0 else -f[q]
            total = term if total is None else total + term
        moments.append(total)
    inv = 1.0 / density
    comps = [m * inv for m in moments]
    base = 1.0 - 1.5 * (comps[0] * comps[0] + comps[1] * comps[1] + comps[2] * comps[2])
    keep = 1.0 - 1.0 / relax_flow
    scaled = {}
    for w in set(flow_weight):
        scaled[w] = (w / relax_flow) * density

    def along(vel):
        total = None
        for axis in range(3):
            if vel[axis] == 0:
                continue
            term = comps[axis] if vel[axis] > 0 else -comps[axis]
            total = term if total is None else total + term
        return total

    done = set()
    for q, vel in enumerate(flow_vel):
        if q in done:
            continue
        opp = flow_vel.index(tuple(-c for c in vel))
        done |= {q, opp}
        weight = scaled[flow_weight[q]]
        if opp == q:
            fs[q, i] = jnp.where(solid, f[q], keep * f[q] + weight * base)
            continue
        cu = along(vel)
        even = base + 4.5 * (cu * cu)
        odd = 3.0 * cu
        if vel[2]:
            odd = odd + 3.0 * body_force * relax_flow * vel[2]
        for member, poly in ((q, even + odd), (opp, even - odd)):
            fs[member, i] = jnp.where(solid, f[member], keep * f[member] + weight * poly)
    conc = cx[i]
    sink = (react_rate * conc) * face_sum(sm, i)
    rate = 1.0 / relax_acid
    shared = rate * conc - sink
    slope = (4.0 * rate) * conc
    done = set()
    for j, vel in enumerate(acid_vel):
        if j in done:
            continue
        opp = acid_vel.index(tuple(-c for c in vel))
        done |= {j, opp}
        if opp == j:
            parts = ((j, shared),)
        else:
            cu = slope * along(vel)
            parts = ((j, shared + cu), (opp, shared - cu))
        for member, inner in parts:
            g = gx[member, i]
            relaxed = acid_weight[member] * inner - (rate - 1.0) * g
            gs[member, i] = jnp.where(solid, g, relaxed)


def dissolve_plane(sx, mx_src, cf, mx_dst, i):
    solid = sx[i] > 0.5
    mineral = mx_src[i]
    loss = (dissolve_rate * react_rate) * mineral * face_sum(cf, i)
    mx_dst[i] = jnp.where(solid, mineral - loss, mineral)


SHIFTS = [(cx, cy) for cx in (-1, 0, 1) for cy in (-1, 0, 1) if cx or cy]


def shift_masks(sx, bm, i):
    for c, (cx, cy) in enumerate(SHIFTS):
        bm[c, i] = roll_xy(sx[i], cx, cy)


def stream_plane(fs, gs, sx, fdst, gdst, i, bm=None):
    solid = sx[i] > 0.5
    masks = {}
    for q, vel in enumerate(flow_vel):
        cx, cy, cz = vel
        if vel == (0, 0, 0):
            fdst[q, i] = fs[q, i]
            continue
        opp = flow_vel.index((-cx, -cy, -cz))
        src = i - cz
        pulled = roll_xy(fs[q, src], cx, cy)
        if bm is None or (cx, cy) == (0, 0):
            blocked = roll_xy(sx[src], cx, cy) > 0.5
        else:
            blocked = bm[SHIFTS.index((cx, cy)), src] > 0.5
        masks[vel] = blocked
        arrived = jnp.where(blocked, fs[opp, i], pulled)
        fdst[q, i] = jnp.where(solid, fs[q, i], arrived)
    for j, vel in enumerate(acid_vel):
        cx, cy, cz = vel
        if vel == (0, 0, 0):
            gdst[j, i] = gs[j, i]
            continue
        opp = acid_vel.index((-cx, -cy, -cz))
        pulled = roll_xy(gs[j, i - cz], cx, cy)
        arrived = jnp.where(masks[vel], gs[opp, i], pulled)
        gdst[j, i] = jnp.where(solid, gs[j, i], arrived)


def loop(lo, hi, fn):
    def body(i, carry):
        fn(i)
        return carry

    lax.fori_loop(lo, hi, body, 0, unroll=2 if hi - lo > 4 else 1)


UP_Q = [q for q, vel in enumerate(flow_vel) if vel[2] == 1]
DOWN_Q = [q for q, vel in enumerate(flow_vel) if vel[2] == -1]
UP_J = acid_vel.index((0, 0, 1))
DOWN_J = acid_vel.index((0, 0, -1))
NFLUX = 3 + 2 * (len(UP_Q) + 1) + 2


def flux_kernel(pop, sol, mnr, sld, up, down, fs, gs, f1, g1, m1, sx, cx, sm, cf):
    planes = sld.shape[0]
    hi, lo = planes - HALO - 1, HALO
    sx[...] = sld[...].astype(jnp.float32)
    loop(lo - 2, hi + 3, lambda i: edge_state(sx, sol, mnr, cx, sm, cf, i))

    def step1(i):
        dissolve_plane(sx, mnr, cf, m1, i)
        collide_plane(pop, sol, sx, cx, sm, fs, gs, i)

    loop(lo - 1, hi + 2, step1)
    for dst, i, qs, j in ((up, hi, UP_Q, UP_J), (down, lo, DOWN_Q, DOWN_J)):
        dst[0] = sx[i]
        dst[1] = sm[i]
        dst[2] = cf[i]
        for n, q in enumerate(qs):
            dst[3 + n] = fs[q, i]
        dst[3 + len(qs)] = gs[j, i]
    loop(lo, hi + 1, lambda i: stream_plane(fs, gs, sx, f1, g1, i))
    for i in range(lo - 1, hi + 2):
        sm[i] = jnp.where(sx[i] > 0.5, m1[i], 0.0)
    for i in range(lo, hi + 1):
        conc = g1[0, i]
        for j in range(1, NG):
            conc = conc + g1[j, i]
        cx[i] = conc
        cf[i] = jnp.where(sx[i] > 0.5, 0.0, conc)
    loop(lo, hi + 1, lambda i: collide_plane(f1, g1, sx, cx, sm, fs, gs, i))
    base = 4 + len(UP_Q)
    for dst, i, qs, j in ((up, hi, UP_Q, UP_J), (down, lo, DOWN_Q, DOWN_J)):
        dst[base] = sm[i]
        dst[base + 1] = cf[i]
        for n, q in enumerate(qs):
            dst[base + 2 + n] = fs[q, i]
        dst[base + 2 + len(qs)] = gs[j, i]


def set_bounds(flo, fhi, sm, cf, fs, gs, last, base):
    sm[0] = flo[base]
    cf[0] = flo[base + 1]
    sm[last] = fhi[base]
    cf[last] = fhi[base + 1]

    def posts():
        for n, q in enumerate(UP_Q):
            fs[q, 0] = flo[base + 2 + n]
        gs[UP_J, 0] = flo[base + 2 + len(UP_Q)]
        for n, q in enumerate(DOWN_Q):
            fs[q, last] = fhi[base + 2 + n]
        gs[DOWN_J, last] = fhi[base + 2 + len(DOWN_Q)]

    return posts


def main_kernel(
    mv, pop, sol, mnr, sld, hlo, hhi, flo, fhi,
    out_f, out_g, out_m, out_s,
    fx, gx, fs, gs, mx, m1, sx, si, cx, sm, cf, zf, zi, bm, sem, osem, zsem,
):
    planes = sld.shape[0]
    cap = out_s.shape[0]
    last = planes + 2 * HALO + 1
    own = HALO + 1
    top = own + planes
    fill = [
        (pop, fx.at[:, own:top]),
        (sol, gx.at[:, own:top]),
        (mnr, mx.at[own:top]),
        (hlo.at[0:NF], fx.at[:, 1:own]),
        (hlo.at[NF:NF + NG], gx.at[:, 1:own]),
        (hlo.at[NF + NG], mx.at[1:own]),
        (hlo.at[NF + NG + 1], sx.at[1:own]),
        (hhi.at[0:NF], fx.at[:, top:last]),
        (hhi.at[NF:NF + NG], gx.at[:, top:last]),
        (hhi.at[NF + NG], mx.at[top:last]),
        (hhi.at[NF + NG + 1], sx.at[top:last]),
    ]
    copies = [pltpu.make_async_copy(s, d, sem.at[k]) for k, (s, d) in enumerate(fill)]
    for c in copies:
        c.start()
    sx[own:top] = sld[...].astype(jnp.float32)
    si[own:top] = sld[...]
    sx[0] = flo[0]
    sx[last] = fhi[0]
    zf[...] = jnp.zeros(zf.shape, zf.dtype)
    zi[...] = jnp.zeros(zi.shape, zi.dtype)
    for c in copies[1:]:
        c.wait()
    si[1:own] = (sx[1:own] > 0.5).astype(jnp.int32)
    si[top:last] = (sx[top:last] > 0.5).astype(jnp.int32)

    from_low, send_low, send_high, from_high = mv[0], mv[1], mv[2], mv[3]
    valid_end = from_low + planes - send_low - send_high + from_high

    def plane_valid(i):
        p = i - own
        low = (p >= -from_low) & (p < 0)
        kept = (p >= send_low) & (p < planes - send_high)
        high = (p >= planes) & (p < planes + from_high)
        return low | kept | high

    def plane_copies(i):
        p = i - own
        s = p + from_low - jnp.where(p >= send_low, send_low, 0) - jnp.where(p >= planes, send_high, 0)
        s = jnp.clip(s, 0, cap - 1)
        srcs = (fx.at[:, i], gx.at[:, i], mx.at[i], si.at[i])
        dsts = (out_f.at[:, s], out_g.at[:, s], out_m.at[s], out_s.at[s])
        return [pltpu.make_async_copy(x, y, osem.at[i, k]) for k, (x, y) in enumerate(zip(srcs, dsts))]

    def zero_copies(s):
        srcs = (zf, zf.at[0:NG], zf.at[0], zi)
        dsts = (out_f.at[:, s], out_g.at[:, s], out_m.at[s], out_s.at[s])
        return [pltpu.make_async_copy(x, y, zsem.at[s, k]) for k, (x, y) in enumerate(zip(srcs, dsts))]

    for s in range(cap):
        @pl.when(s >= valid_end)
        def _():
            for c in zero_copies(s):
                c.start()

    loop(0, last + 1, lambda i: shift_masks(sx, bm, i))

    posts = set_bounds(flo, fhi, sm, cf, fs, gs, last, 1)
    loop(1, last, lambda i: edge_state(sx, gx, mx, cx, sm, cf, i))
    copies[0].wait()

    def step1(i):
        dissolve_plane(sx, mx, cf, m1, i)
        collide_plane(fx, gx, sx, cx, sm, fs, gs, i)

    loop(1, last, step1)
    posts()
    loop(1, last, lambda i: stream_plane(fs, gs, sx, fx, gx, i, bm))

    posts = set_bounds(flo, fhi, sm, cf, fs, gs, last, 4 + len(UP_Q))
    loop(1, last, lambda i: edge_state(sx, gx, m1, cx, sm, cf, i))

    def step2(i):
        dissolve_plane(sx, m1, cf, mx, i)
        collide_plane(fx, gx, sx, cx, sm, fs, gs, i)

    loop(1, last, step2)
    posts()

    def send_plane(i):
        @pl.when(plane_valid(i))
        def _():
            for c in plane_copies(i):
                c.start()

    def final(i):
        stream_plane(fs, gs, sx, fx, gx, i, bm)

        @pl.when(i > 1)
        def _():
            send_plane(i - 1)

    loop(1, last, final)
    send_plane(last - 1)
    for i in range(1, last):
        @pl.when(plane_valid(i))
        def _():
            for c in plane_copies(i):
                c.wait()
    for s in range(cap):
        @pl.when(s >= valid_end)
        def _():
            for c in zero_copies(s):
                c.wait()


def edge_kernel(lo, pop, sol, mnr, sld, out, sem):
    parts = [
        (pop.at[:, lo:lo + HALO], out.at[0:NF]),
        (sol.at[:, lo:lo + HALO], out.at[NF:NF + NG]),
        (mnr.at[lo:lo + HALO], out.at[NF + NG]),
    ]
    copies = [pltpu.make_async_copy(s, d, sem.at[k]) for k, (s, d) in enumerate(parts)]
    for c in copies:
        c.start()
    out[NF + NG + 1] = sld[lo:lo + HALO].astype(jnp.float32)
    for c in copies:
        c.wait()


def shards(populations, solute, mineral, solid, plane_moves):
    planes = populations.shape[1]
    cap = planes + 2 * MOVE_MOST
    ext = planes + 2 * HALO + 2
    count = lax.axis_size("blk")
    forward = [(i, (i + 1) % count) for i in range(count)]
    backward = [(i, (i - 1) % count) for i in range(count)]

    plane = populations.shape[2:]
    f32 = jnp.float32
    any_spec = pl.BlockSpec(memory_space=pl.ANY)
    vmem = pl.BlockSpec(memory_space=pltpu.VMEM)
    smem = pl.BlockSpec(memory_space=pltpu.SMEM)

    def edge(lo):
        return pl.pallas_call(
            functools.partial(edge_kernel, lo),
            out_shape=jax.ShapeDtypeStruct((NF + NG + 2, HALO) + plane, f32),
            in_specs=[any_spec, any_spec, any_spec, vmem],
            out_specs=vmem,
            scratch_shapes=[pltpu.SemaphoreType.DMA((3,))],
        )(populations, solute, mineral, solid)

    halo_lo = lax.ppermute(edge(planes - HALO), "blk", forward)
    halo_hi = lax.ppermute(edge(0), "blk", backward)

    up, down = pl.pallas_call(
        flux_kernel,
        out_shape=(
            jax.ShapeDtypeStruct((NFLUX,) + plane, f32),
            jax.ShapeDtypeStruct((NFLUX,) + plane, f32),
        ),
        in_specs=[vmem] * 4,
        out_specs=[vmem] * 2,
        scratch_shapes=[
            pltpu.VMEM((NF, planes) + plane, f32),
            pltpu.VMEM((NG, planes) + plane, f32),
            pltpu.VMEM((NF, planes) + plane, f32),
            pltpu.VMEM((NG, planes) + plane, f32),
        ]
        + [pltpu.VMEM((planes,) + plane, f32)] * 5,
    )(populations, solute, mineral, solid)
    flux_lo = lax.ppermute(up, "blk", forward)
    flux_hi = lax.ppermute(down, "blk", backward)

    me = lax.axis_index("blk")
    from_low = plane_moves[jnp.mod(me - 1, count), 1]
    send_low = plane_moves[me, 0]
    send_high = plane_moves[me, 1]
    from_high = plane_moves[jnp.mod(me + 1, count), 0]
    mv = jnp.stack([from_low, send_low, send_high, from_high]).astype(jnp.int32)

    return pl.pallas_call(
        main_kernel,
        out_shape=(
            jax.ShapeDtypeStruct((NF, cap) + plane, f32),
            jax.ShapeDtypeStruct((NG, cap) + plane, f32),
            jax.ShapeDtypeStruct((cap,) + plane, f32),
            jax.ShapeDtypeStruct((cap,) + plane, jnp.int32),
        ),
        in_specs=[smem, any_spec, any_spec, any_spec, vmem, any_spec, any_spec, vmem, vmem],
        out_specs=[any_spec] * 4,
        scratch_shapes=[
            pltpu.VMEM((NF, ext) + plane, f32),
            pltpu.VMEM((NG, ext) + plane, f32),
            pltpu.VMEM((NF, ext) + plane, f32),
            pltpu.VMEM((NG, ext) + plane, f32),
            pltpu.VMEM((ext,) + plane, f32),
            pltpu.VMEM((ext,) + plane, f32),
            pltpu.VMEM((ext,) + plane, f32),
            pltpu.VMEM((ext,) + plane, jnp.int32),
            pltpu.VMEM((ext,) + plane, f32),
            pltpu.VMEM((ext,) + plane, f32),
            pltpu.VMEM((ext,) + plane, f32),
            pltpu.VMEM((NF,) + plane, f32),
            pltpu.VMEM(plane, jnp.int32),
            pltpu.VMEM((len(SHIFTS), ext) + plane, f32),
            pltpu.SemaphoreType.DMA((11,)),
            pltpu.SemaphoreType.DMA((ext, 4)),
            pltpu.SemaphoreType.DMA((cap, 4)),
        ],
        compiler_params=pltpu.CompilerParams(vmem_limit_bytes=50 * 1024 * 1024),
    )(mv, populations, solute, mineral, solid, halo_lo, halo_hi, flux_lo, flux_hi)


def solution(mesh):
    return jax.shard_map(
        shards,
        mesh=mesh,
        in_specs=(
            P(None, "blk", None, None),
            P(None, "blk", None, None),
            P("blk", None, None),
            P("blk", None, None),
            P(),
        ),
        out_specs=(
            P(None, "blk", None, None),
            P(None, "blk", None, None),
            P("blk", None, None),
            P("blk", None, None),
        ),
        check_vma=False,
    )
```

```python
import functools

import jax
import jax.numpy as jnp
from jax import lax
from jax.experimental import pallas as pl
from jax.experimental.pallas import tpu as pltpu
from jax.sharding import PartitionSpec as P

MOVE_MOST = 3
HALO = 3

flow_vel = [
    (0, 0, 1),
    (1, 0, 1),
    (-1, 0, 1),
    (0, 1, 1),
    (0, -1, 1),
    (0, 0, -1),
    (1, 0, -1),
    (-1, 0, -1),
    (0, 1, -1),
    (0, -1, -1),
    (0, 0, 0),
    (1, 0, 0),
    (-1, 0, 0),
    (0, 1, 0),
    (0, -1, 0),
    (1, 1, 0),
    (-1, -1, 0),
    (1, -1, 0),
    (-1, 1, 0),
]
flow_weight = [
    1.0 / 18,
    1.0 / 36,
    1.0 / 36,
    1.0 / 36,
    1.0 / 36,
    1.0 / 18,
    1.0 / 36,
    1.0 / 36,
    1.0 / 36,
    1.0 / 36,
    1.0 / 3,
    1.0 / 18,
    1.0 / 18,
    1.0 / 18,
    1.0 / 18,
    1.0 / 36,
    1.0 / 36,
    1.0 / 36,
    1.0 / 36,
]
acid_vel = [(0, 0, 1), (0, 0, -1), (0, 0, 0), (1, 0, 0), (-1, 0, 0), (0, 1, 0), (0, -1, 0)]
acid_weight = [0.125, 0.125, 0.25, 0.125, 0.125, 0.125, 0.125]
relax_flow = 1.25
relax_acid = 0.8
body_force = 0.001
react_rate = 0.1
dissolve_rate = 0.5

NF = len(flow_vel)
NG = len(acid_vel)


def roll_xy(a, cx, cy):
    if cx:
        a = pltpu.roll(a, cx % a.shape[0], 0)
    if cy:
        a = pltpu.roll(a, cy % a.shape[1], 1)
    return a


def face_sum(ref, i):
    mid = ref[i]
    total = ref[i - 1] + ref[i + 1]
    total = total + (roll_xy(mid, 1, 0) + roll_xy(mid, -1, 0))
    return total + (roll_xy(mid, 0, 1) + roll_xy(mid, 0, -1))


def edge_state(sx, gx, mx, cx, sm, cf, i):
    conc = gx[0, i]
    for j in range(1, NG):
        conc = conc + gx[j, i]
    cx[i] = conc
    solid = sx[i] > 0.5
    sm[i] = jnp.where(solid, mx[i], 0.0)
    cf[i] = jnp.where(solid, 0.0, conc)


def collide_plane(fx, gx, sx, cx, sm, fs, gs, i):
    solid = sx[i] > 0.5
    f = [fx[q, i] for q in range(NF)]
    density = f[0]
    for q in range(1, NF):
        density = density + f[q]
    moments = []
    for axis in range(3):
        total = None
        for q, vel in enumerate(flow_vel):
            if vel[axis] == 0:
                continue
            term = f[q] if vel[axis] > 0 else -f[q]
            total = term if total is None else total + term
        moments.append(total)
    inv = 1.0 / density
    comps = [m * inv for m in moments]
    base = 1.0 - 1.5 * (comps[0] * comps[0] + comps[1] * comps[1] + comps[2] * comps[2])
    keep = 1.0 - 1.0 / relax_flow
    scaled = {}
    for w in set(flow_weight):
        scaled[w] = (w / relax_flow) * density

    def along(vel):
        total = None
        for axis in range(3):
            if vel[axis] == 0:
                continue
            term = comps[axis] if vel[axis] > 0 else -comps[axis]
            total = term if total is None else total + term
        return total

    done = set()
    for q, vel in enumerate(flow_vel):
        if q in done:
            continue
        opp = flow_vel.index(tuple(-c for c in vel))
        done |= {q, opp}
        weight = scaled[flow_weight[q]]
        if opp == q:
            fs[q, i] = jnp.where(solid, f[q], keep * f[q] + weight * base)
            continue
        cu = along(vel)
        even = base + 4.5 * (cu * cu)
        odd = 3.0 * cu
        if vel[2]:
            odd = odd + 3.0 * body_force * relax_flow * vel[2]
        for member, poly in ((q, even + odd), (opp, even - odd)):
            fs[member, i] = jnp.where(solid, f[member], keep * f[member] + weight * poly)
    conc = cx[i]
    sink = (react_rate * conc) * face_sum(sm, i)
    rate = 1.0 / relax_acid
    shared = rate * conc - sink
    slope = (4.0 * rate) * conc
    done = set()
    for j, vel in enumerate(acid_vel):
        if j in done:
            continue
        opp = acid_vel.index(tuple(-c for c in vel))
        done |= {j, opp}
        if opp == j:
            parts = ((j, shared),)
        else:
            cu = slope * along(vel)
            parts = ((j, shared + cu), (opp, shared - cu))
        for member, inner in parts:
            g = gx[member, i]
            relaxed = acid_weight[member] * inner - (rate - 1.0) * g
            gs[member, i] = jnp.where(solid, g, relaxed)


def dissolve_plane(sx, mx_src, cf, mx_dst, i):
    solid = sx[i] > 0.5
    mineral = mx_src[i]
    loss = (dissolve_rate * react_rate) * mineral * face_sum(cf, i)
    mx_dst[i] = jnp.where(solid, mineral - loss, mineral)


SHIFTS = [(cx, cy) for cx in (-1, 0, 1) for cy in (-1, 0, 1) if cx or cy]


def shift_masks(sx, bm, i):
    for c, (cx, cy) in enumerate(SHIFTS):
        bm[c, i] = roll_xy(sx[i], cx, cy)


def stream_plane(fs, gs, sx, fdst, gdst, i, bm=None):
    solid = sx[i] > 0.5
    masks = {}
    for q, vel in enumerate(flow_vel):
        cx, cy, cz = vel
        if vel == (0, 0, 0):
            fdst[q, i] = fs[q, i]
            continue
        opp = flow_vel.index((-cx, -cy, -cz))
        src = i - cz
        pulled = roll_xy(fs[q, src], cx, cy)
        if bm is None or (cx, cy) == (0, 0):
            blocked = roll_xy(sx[src], cx, cy) > 0.5
        else:
            blocked = bm[SHIFTS.index((cx, cy)), src] > 0.5
        masks[vel] = blocked
        arrived = jnp.where(blocked, fs[opp, i], pulled)
        fdst[q, i] = jnp.where(solid, fs[q, i], arrived)
    for j, vel in enumerate(acid_vel):
        cx, cy, cz = vel
        if vel == (0, 0, 0):
            gdst[j, i] = gs[j, i]
            continue
        opp = acid_vel.index((-cx, -cy, -cz))
        pulled = roll_xy(gs[j, i - cz], cx, cy)
        arrived = jnp.where(masks[vel], gs[opp, i], pulled)
        gdst[j, i] = jnp.where(solid, gs[j, i], arrived)


def loop(lo, hi, fn):
    def body(i, carry):
        fn(i)
        return carry

    lax.fori_loop(lo, hi, body, 0, unroll=4 if hi - lo > 8 else (2 if hi - lo > 4 else 1))


UP_Q = [q for q, vel in enumerate(flow_vel) if vel[2] == 1]
DOWN_Q = [q for q, vel in enumerate(flow_vel) if vel[2] == -1]
UP_J = acid_vel.index((0, 0, 1))
DOWN_J = acid_vel.index((0, 0, -1))
NFLUX = 3 + 2 * (len(UP_Q) + 1) + 2


def flux_kernel(pop, sol, mnr, sld, up, down, fs, gs, f1, g1, m1, sx, cx, sm, cf):
    planes = sld.shape[0]
    hi, lo = planes - HALO - 1, HALO
    sx[...] = sld[...].astype(jnp.float32)
    loop(lo - 2, hi + 3, lambda i: edge_state(sx, sol, mnr, cx, sm, cf, i))

    def step1(i):
        dissolve_plane(sx, mnr, cf, m1, i)
        collide_plane(pop, sol, sx, cx, sm, fs, gs, i)

    loop(lo - 1, hi + 2, step1)
    for dst, i, qs, j in ((up, hi, UP_Q, UP_J), (down, lo, DOWN_Q, DOWN_J)):
        dst[0] = sx[i]
        dst[1] = sm[i]
        dst[2] = cf[i]
        for n, q in enumerate(qs):
            dst[3 + n] = fs[q, i]
        dst[3 + len(qs)] = gs[j, i]
    loop(lo, hi + 1, lambda i: stream_plane(fs, gs, sx, f1, g1, i))
    for i in range(lo - 1, hi + 2):
        sm[i] = jnp.where(sx[i] > 0.5, m1[i], 0.0)
    for i in range(lo, hi + 1):
        conc = g1[0, i]
        for j in range(1, NG):
            conc = conc + g1[j, i]
        cx[i] = conc
        cf[i] = jnp.where(sx[i] > 0.5, 0.0, conc)
    loop(lo, hi + 1, lambda i: collide_plane(f1, g1, sx, cx, sm, fs, gs, i))
    base = 4 + len(UP_Q)
    for dst, i, qs, j in ((up, hi, UP_Q, UP_J), (down, lo, DOWN_Q, DOWN_J)):
        dst[base] = sm[i]
        dst[base + 1] = cf[i]
        for n, q in enumerate(qs):
            dst[base + 2 + n] = fs[q, i]
        dst[base + 2 + len(qs)] = gs[j, i]


def set_bounds(flo, fhi, sm, cf, fs, gs, last, base):
    sm[0] = flo[base]
    cf[0] = flo[base + 1]
    sm[last] = fhi[base]
    cf[last] = fhi[base + 1]

    def posts():
        for n, q in enumerate(UP_Q):
            fs[q, 0] = flo[base + 2 + n]
        gs[UP_J, 0] = flo[base + 2 + len(UP_Q)]
        for n, q in enumerate(DOWN_Q):
            fs[q, last] = fhi[base + 2 + n]
        gs[DOWN_J, last] = fhi[base + 2 + len(DOWN_Q)]

    return posts


def main_kernel(
    mv, pop, sol, mnr, sld, hlo, hhi, flo, fhi,
    out_f, out_g, out_m, out_s,
    fx, gx, fs, gs, mx, m1, sx, si, cx, sm, cf, zf, zi, bm, sem, osem, zsem,
):
    planes = sld.shape[0]
    cap = out_s.shape[0]
    last = planes + 2 * HALO + 1
    own = HALO + 1
    top = own + planes
    fill = [
        (pop, fx.at[:, own:top]),
        (sol, gx.at[:, own:top]),
        (mnr, mx.at[own:top]),
        (hlo.at[0:NF], fx.at[:, 1:own]),
        (hlo.at[NF:NF + NG], gx.at[:, 1:own]),
        (hlo.at[NF + NG], mx.at[1:own]),
        (hlo.at[NF + NG + 1], sx.at[1:own]),
        (hhi.at[0:NF], fx.at[:, top:last]),
        (hhi.at[NF:NF + NG], gx.at[:, top:last]),
        (hhi.at[NF + NG], mx.at[top:last]),
        (hhi.at[NF + NG + 1], sx.at[top:last]),
    ]
    copies = [pltpu.make_async_copy(s, d, sem.at[k]) for k, (s, d) in enumerate(fill)]
    for c in copies:
        c.start()
    sx[own:top] = sld[...].astype(jnp.float32)
    si[own:top] = sld[...]
    sx[0] = flo[0]
    sx[last] = fhi[0]
    zf[...] = jnp.zeros(zf.shape, zf.dtype)
    zi[...] = jnp.zeros(zi.shape, zi.dtype)
    for c in copies[1:]:
        c.wait()
    si[1:own] = (sx[1:own] > 0.5).astype(jnp.int32)
    si[top:last] = (sx[top:last] > 0.5).astype(jnp.int32)

    from_low, send_low, send_high, from_high = mv[0], mv[1], mv[2], mv[3]
    valid_end = from_low + planes - send_low - send_high + from_high

    def plane_valid(i):
        p = i - own
        low = (p >= -from_low) & (p < 0)
        kept = (p >= send_low) & (p < planes - send_high)
        high = (p >= planes) & (p < planes + from_high)
        return low | kept | high

    def plane_copies(i):
        p = i - own
        s = p + from_low - jnp.where(p >= send_low, send_low, 0) - jnp.where(p >= planes, send_high, 0)
        s = jnp.clip(s, 0, cap - 1)
        srcs = (fx.at[:, i], gx.at[:, i], mx.at[i], si.at[i])
        dsts = (out_f.at[:, s], out_g.at[:, s], out_m.at[s], out_s.at[s])
        return [pltpu.make_async_copy(x, y, osem.at[i, k]) for k, (x, y) in enumerate(zip(srcs, dsts))]

    def zero_copies(s):
        srcs = (zf, zf.at[0:NG], zf.at[0], zi)
        dsts = (out_f.at[:, s], out_g.at[:, s], out_m.at[s], out_s.at[s])
        return [pltpu.make_async_copy(x, y, zsem.at[s, k]) for k, (x, y) in enumerate(zip(srcs, dsts))]

    for s in range(cap):
        @pl.when(s >= valid_end)
        def _():
            for c in zero_copies(s):
                c.start()

    loop(0, last + 1, lambda i: shift_masks(sx, bm, i))

    posts = set_bounds(flo, fhi, sm, cf, fs, gs, last, 1)
    loop(1, last, lambda i: edge_state(sx, gx, mx, cx, sm, cf, i))
    copies[0].wait()

    def step1(i):
        dissolve_plane(sx, mx, cf, m1, i)
        collide_plane(fx, gx, sx, cx, sm, fs, gs, i)

    loop(1, last, step1)
    posts()
    loop(1, last, lambda i: stream_plane(fs, gs, sx, fx, gx, i, bm))

    posts = set_bounds(flo, fhi, sm, cf, fs, gs, last, 4 + len(UP_Q))
    loop(1, last, lambda i: edge_state(sx, gx, m1, cx, sm, cf, i))

    def step2(i):
        dissolve_plane(sx, m1, cf, mx, i)
        collide_plane(fx, gx, sx, cx, sm, fs, gs, i)

    loop(1, last, step2)
    posts()

    def send_plane(i):
        @pl.when(plane_valid(i))
        def _():
            for c in plane_copies(i):
                c.start()

    def final(i):
        stream_plane(fs, gs, sx, fx, gx, i, bm)

        @pl.when(i > 1)
        def _():
            send_plane(i - 1)

    loop(1, last, final)
    send_plane(last - 1)
    for i in range(1, last):
        @pl.when(plane_valid(i))
        def _():
            for c in plane_copies(i):
                c.wait()
    for s in range(cap):
        @pl.when(s >= valid_end)
        def _():
            for c in zero_copies(s):
                c.wait()


def edge_kernel(lo, pop, sol, mnr, sld, out, sem):
    parts = [
        (pop.at[:, lo:lo + HALO], out.at[0:NF]),
        (sol.at[:, lo:lo + HALO], out.at[NF:NF + NG]),
        (mnr.at[lo:lo + HALO], out.at[NF + NG]),
    ]
    copies = [pltpu.make_async_copy(s, d, sem.at[k]) for k, (s, d) in enumerate(parts)]
    for c in copies:
        c.start()
    out[NF + NG + 1] = sld[lo:lo + HALO].astype(jnp.float32)
    for c in copies:
        c.wait()


def shards(populations, solute, mineral, solid, plane_moves):
    planes = populations.shape[1]
    cap = planes + 2 * MOVE_MOST
    ext = planes + 2 * HALO + 2
    count = lax.axis_size("blk")
    forward = [(i, (i + 1) % count) for i in range(count)]
    backward = [(i, (i - 1) % count) for i in range(count)]

    plane = populations.shape[2:]
    f32 = jnp.float32
    any_spec = pl.BlockSpec(memory_space=pl.ANY)
    vmem = pl.BlockSpec(memory_space=pltpu.VMEM)
    smem = pl.BlockSpec(memory_space=pltpu.SMEM)

    def edge(lo):
        return pl.pallas_call(
            functools.partial(edge_kernel, lo),
            out_shape=jax.ShapeDtypeStruct((NF + NG + 2, HALO) + plane, f32),
            in_specs=[any_spec, any_spec, any_spec, vmem],
            out_specs=vmem,
            scratch_shapes=[pltpu.SemaphoreType.DMA((3,))],
        )(populations, solute, mineral, solid)

    halo_lo = lax.ppermute(edge(planes - HALO), "blk", forward)
    halo_hi = lax.ppermute(edge(0), "blk", backward)

    up, down = pl.pallas_call(
        flux_kernel,
        out_shape=(
            jax.ShapeDtypeStruct((NFLUX,) + plane, f32),
            jax.ShapeDtypeStruct((NFLUX,) + plane, f32),
        ),
        in_specs=[vmem] * 4,
        out_specs=[vmem] * 2,
        scratch_shapes=[
            pltpu.VMEM((NF, planes) + plane, f32),
            pltpu.VMEM((NG, planes) + plane, f32),
            pltpu.VMEM((NF, planes) + plane, f32),
            pltpu.VMEM((NG, planes) + plane, f32),
        ]
        + [pltpu.VMEM((planes,) + plane, f32)] * 5,
    )(populations, solute, mineral, solid)
    flux_lo = lax.ppermute(up, "blk", forward)
    flux_hi = lax.ppermute(down, "blk", backward)

    me = lax.axis_index("blk")
    from_low = plane_moves[jnp.mod(me - 1, count), 1]
    send_low = plane_moves[me, 0]
    send_high = plane_moves[me, 1]
    from_high = plane_moves[jnp.mod(me + 1, count), 0]
    mv = jnp.stack([from_low, send_low, send_high, from_high]).astype(jnp.int32)

    return pl.pallas_call(
        main_kernel,
        out_shape=(
            jax.ShapeDtypeStruct((NF, cap) + plane, f32),
            jax.ShapeDtypeStruct((NG, cap) + plane, f32),
            jax.ShapeDtypeStruct((cap,) + plane, f32),
            jax.ShapeDtypeStruct((cap,) + plane, jnp.int32),
        ),
        in_specs=[smem, any_spec, any_spec, any_spec, vmem, any_spec, any_spec, vmem, vmem],
        out_specs=[any_spec] * 4,
        scratch_shapes=[
            pltpu.VMEM((NF, ext) + plane, f32),
            pltpu.VMEM((NG, ext) + plane, f32),
            pltpu.VMEM((NF, ext) + plane, f32),
            pltpu.VMEM((NG, ext) + plane, f32),
            pltpu.VMEM((ext,) + plane, f32),
            pltpu.VMEM((ext,) + plane, f32),
            pltpu.VMEM((ext,) + plane, f32),
            pltpu.VMEM((ext,) + plane, jnp.int32),
            pltpu.VMEM((ext,) + plane, f32),
            pltpu.VMEM((ext,) + plane, f32),
            pltpu.VMEM((ext,) + plane, f32),
            pltpu.VMEM((NF,) + plane, f32),
            pltpu.VMEM(plane, jnp.int32),
            pltpu.VMEM((len(SHIFTS), ext) + plane, f32),
            pltpu.SemaphoreType.DMA((11,)),
            pltpu.SemaphoreType.DMA((ext, 4)),
            pltpu.SemaphoreType.DMA((cap, 4)),
        ],
        compiler_params=pltpu.CompilerParams(vmem_limit_bytes=50 * 1024 * 1024),
    )(mv, populations, solute, mineral, solid, halo_lo, halo_hi, flux_lo, flux_hi)


def solution(mesh):
    return jax.shard_map(
        shards,
        mesh=mesh,
        in_specs=(
            P(None, "blk", None, None),
            P(None, "blk", None, None),
            P("blk", None, None),
            P("blk", None, None),
            P(),
        ),
        out_specs=(
            P(None, "blk", None, None),
            P(None, "blk", None, None),
            P("blk", None, None),
            P("blk", None, None),
        ),
        check_vma=False,
    )
```

```python
import functools

import jax
import jax.numpy as jnp
from jax import lax
from jax.experimental import pallas as pl
from jax.experimental.pallas import tpu as pltpu
from jax.sharding import PartitionSpec as P

MOVE_MOST = 3
HALO = 3

flow_vel = [
    (0, 0, 1),
    (1, 0, 1),
    (-1, 0, 1),
    (0, 1, 1),
    (0, -1, 1),
    (0, 0, -1),
    (1, 0, -1),
    (-1, 0, -1),
    (0, 1, -1),
    (0, -1, -1),
    (0, 0, 0),
    (1, 0, 0),
    (-1, 0, 0),
    (0, 1, 0),
    (0, -1, 0),
    (1, 1, 0),
    (-1, -1, 0),
    (1, -1, 0),
    (-1, 1, 0),
]
flow_weight = [
    1.0 / 18,
    1.0 / 36,
    1.0 / 36,
    1.0 / 36,
    1.0 / 36,
    1.0 / 18,
    1.0 / 36,
    1.0 / 36,
    1.0 / 36,
    1.0 / 36,
    1.0 / 3,
    1.0 / 18,
    1.0 / 18,
    1.0 / 18,
    1.0 / 18,
    1.0 / 36,
    1.0 / 36,
    1.0 / 36,
    1.0 / 36,
]
acid_vel = [(0, 0, 1), (0, 0, -1), (0, 0, 0), (1, 0, 0), (-1, 0, 0), (0, 1, 0), (0, -1, 0)]
acid_weight = [0.125, 0.125, 0.25, 0.125, 0.125, 0.125, 0.125]
relax_flow = 1.25
relax_acid = 0.8
body_force = 0.001
react_rate = 0.1
dissolve_rate = 0.5

NF = len(flow_vel)
NG = len(acid_vel)


def roll_xy(a, cx, cy):
    if cx:
        a = pltpu.roll(a, cx % a.shape[0], 0)
    if cy:
        a = pltpu.roll(a, cy % a.shape[1], 1)
    return a


def face_sum(ref, i):
    mid = ref[i]
    total = ref[i - 1] + ref[i + 1]
    total = total + (roll_xy(mid, 1, 0) + roll_xy(mid, -1, 0))
    return total + (roll_xy(mid, 0, 1) + roll_xy(mid, 0, -1))


def edge_state(sx, gx, mx, cx, sm, cf, i):
    conc = gx[0, i]
    for j in range(1, NG):
        conc = conc + gx[j, i]
    cx[i] = conc
    solid = sx[i] > 0.5
    sm[i] = jnp.where(solid, mx[i], 0.0)
    cf[i] = jnp.where(solid, 0.0, conc)


def collide_plane(fx, gx, sx, cx, sm, fs, gs, i):
    solid = sx[i] > 0.5
    f = [fx[q, i] for q in range(NF)]
    density = f[0]
    for q in range(1, NF):
        density = density + f[q]
    moments = []
    for axis in range(3):
        total = None
        for q, vel in enumerate(flow_vel):
            if vel[axis] == 0:
                continue
            term = f[q] if vel[axis] > 0 else -f[q]
            total = term if total is None else total + term
        moments.append(total)
    inv = 1.0 / density
    comps = [m * inv for m in moments]
    base = 1.0 - 1.5 * (comps[0] * comps[0] + comps[1] * comps[1] + comps[2] * comps[2])
    keep = 1.0 - 1.0 / relax_flow
    scaled = {}
    for w in set(flow_weight):
        scaled[w] = (w / relax_flow) * density

    def along(vel):
        total = None
        for axis in range(3):
            if vel[axis] == 0:
                continue
            term = comps[axis] if vel[axis] > 0 else -comps[axis]
            total = term if total is None else total + term
        return total

    done = set()
    for q, vel in enumerate(flow_vel):
        if q in done:
            continue
        opp = flow_vel.index(tuple(-c for c in vel))
        done |= {q, opp}
        weight = scaled[flow_weight[q]]
        if opp == q:
            fs[q, i] = jnp.where(solid, f[q], keep * f[q] + weight * base)
            continue
        cu = along(vel)
        even = base + 4.5 * (cu * cu)
        odd = 3.0 * cu
        if vel[2]:
            odd = odd + 3.0 * body_force * relax_flow * vel[2]
        for member, poly in ((q, even + odd), (opp, even - odd)):
            fs[member, i] = jnp.where(solid, f[member], keep * f[member] + weight * poly)
    conc = cx[i]
    sink = (react_rate * conc) * face_sum(sm, i)
    rate = 1.0 / relax_acid
    shared = rate * conc - sink
    slope = (4.0 * rate) * conc
    done = set()
    for j, vel in enumerate(acid_vel):
        if j in done:
            continue
        opp = acid_vel.index(tuple(-c for c in vel))
        done |= {j, opp}
        if opp == j:
            parts = ((j, shared),)
        else:
            cu = slope * along(vel)
            parts = ((j, shared + cu), (opp, shared - cu))
        for member, inner in parts:
            g = gx[member, i]
            relaxed = acid_weight[member] * inner - (rate - 1.0) * g
            gs[member, i] = jnp.where(solid, g, relaxed)


def dissolve_plane(sx, mx_src, cf, mx_dst, i):
    solid = sx[i] > 0.5
    mineral = mx_src[i]
    loss = (dissolve_rate * react_rate) * mineral * face_sum(cf, i)
    mx_dst[i] = jnp.where(solid, mineral - loss, mineral)


SHIFTS = [(cx, cy) for cx in (-1, 0, 1) for cy in (-1, 0, 1) if cx or cy]


def shift_masks(sx, bm, i):
    for c, (cx, cy) in enumerate(SHIFTS):
        bm[c, i] = roll_xy(sx[i], cx, cy)


def stream_plane(fs, gs, sx, fdst, gdst, i, bm=None):
    solid = sx[i] > 0.5
    masks = {}
    for q, vel in enumerate(flow_vel):
        cx, cy, cz = vel
        if vel == (0, 0, 0):
            fdst[q, i] = fs[q, i]
            continue
        opp = flow_vel.index((-cx, -cy, -cz))
        src = i - cz
        pulled = roll_xy(fs[q, src], cx, cy)
        if bm is None or (cx, cy) == (0, 0):
            blocked = roll_xy(sx[src], cx, cy) > 0.5
        else:
            blocked = bm[SHIFTS.index((cx, cy)), src] > 0.5
        masks[vel] = blocked
        arrived = jnp.where(blocked, fs[opp, i], pulled)
        fdst[q, i] = jnp.where(solid, fs[q, i], arrived)
    for j, vel in enumerate(acid_vel):
        cx, cy, cz = vel
        if vel == (0, 0, 0):
            gdst[j, i] = gs[j, i]
            continue
        opp = acid_vel.index((-cx, -cy, -cz))
        pulled = roll_xy(gs[j, i - cz], cx, cy)
        arrived = jnp.where(masks[vel], gs[opp, i], pulled)
        gdst[j, i] = jnp.where(solid, gs[j, i], arrived)


def loop(lo, hi, fn):
    def body(i, carry):
        fn(i)
        return carry

    lax.fori_loop(lo, hi, body, 0, unroll=2 if hi - lo > 4 else 1)


UP_Q = [q for q, vel in enumerate(flow_vel) if vel[2] == 1]
DOWN_Q = [q for q, vel in enumerate(flow_vel) if vel[2] == -1]
UP_J = acid_vel.index((0, 0, 1))
DOWN_J = acid_vel.index((0, 0, -1))
NFLUX = 3 + 2 * (len(UP_Q) + 1) + 2


def flux_kernel(pop, sol, mnr, sld, up, down, fs, gs, f1, g1, m1, sx, cx, sm, cf):
    planes = sld.shape[0]
    hi, lo = planes - HALO - 1, HALO
    sx[...] = sld[...].astype(jnp.float32)
    loop(lo - 2, hi + 3, lambda i: edge_state(sx, sol, mnr, cx, sm, cf, i))

    def step1(i):
        dissolve_plane(sx, mnr, cf, m1, i)
        collide_plane(pop, sol, sx, cx, sm, fs, gs, i)

    loop(lo - 1, hi + 2, step1)
    for dst, i, qs, j in ((up, hi, UP_Q, UP_J), (down, lo, DOWN_Q, DOWN_J)):
        dst[0] = sx[i]
        dst[1] = sm[i]
        dst[2] = cf[i]
        for n, q in enumerate(qs):
            dst[3 + n] = fs[q, i]
        dst[3 + len(qs)] = gs[j, i]
    loop(lo, hi + 1, lambda i: stream_plane(fs, gs, sx, f1, g1, i))
    for i in range(lo - 1, hi + 2):
        sm[i] = jnp.where(sx[i] > 0.5, m1[i], 0.0)
    for i in range(lo, hi + 1):
        conc = g1[0, i]
        for j in range(1, NG):
            conc = conc + g1[j, i]
        cx[i] = conc
        cf[i] = jnp.where(sx[i] > 0.5, 0.0, conc)
    loop(lo, hi + 1, lambda i: collide_plane(f1, g1, sx, cx, sm, fs, gs, i))
    base = 4 + len(UP_Q)
    for dst, i, qs, j in ((up, hi, UP_Q, UP_J), (down, lo, DOWN_Q, DOWN_J)):
        dst[base] = sm[i]
        dst[base + 1] = cf[i]
        for n, q in enumerate(qs):
            dst[base + 2 + n] = fs[q, i]
        dst[base + 2 + len(qs)] = gs[j, i]


def set_bounds(flo, fhi, sm, cf, fs, gs, last, base):
    sm[0] = flo[base]
    cf[0] = flo[base + 1]
    sm[last] = fhi[base]
    cf[last] = fhi[base + 1]

    def posts():
        for n, q in enumerate(UP_Q):
            fs[q, 0] = flo[base + 2 + n]
        gs[UP_J, 0] = flo[base + 2 + len(UP_Q)]
        for n, q in enumerate(DOWN_Q):
            fs[q, last] = fhi[base + 2 + n]
        gs[DOWN_J, last] = fhi[base + 2 + len(DOWN_Q)]

    return posts


def main_kernel(
    mv, pop, sol, mnr, sld, hlo, hhi, flo, fhi,
    out_f, out_g, out_m, out_s,
    fx, gx, fs, gs, mx, m1, sx, si, cx, sm, cf, zf, zi, bm, sem, osem, zsem,
):
    planes = sld.shape[0]
    cap = out_s.shape[0]
    last = planes + 2 * HALO + 1
    own = HALO + 1
    top = own + planes
    fill = [
        (pop, fx.at[:, own:top]),
        (sol, gx.at[:, own:top]),
        (mnr, mx.at[own:top]),
        (hlo.at[0:NF], fx.at[:, 1:own]),
        (hlo.at[NF:NF + NG], gx.at[:, 1:own]),
        (hlo.at[NF + NG], mx.at[1:own]),
        (hlo.at[NF + NG + 1], sx.at[1:own]),
        (hhi.at[0:NF], fx.at[:, top:last]),
        (hhi.at[NF:NF + NG], gx.at[:, top:last]),
        (hhi.at[NF + NG], mx.at[top:last]),
        (hhi.at[NF + NG + 1], sx.at[top:last]),
    ]
    copies = [pltpu.make_async_copy(s, d, sem.at[k]) for k, (s, d) in enumerate(fill)]
    for c in copies:
        c.start()
    sx[own:top] = sld[...].astype(jnp.float32)
    si[own:top] = sld[...]
    sx[0] = flo[0]
    sx[last] = fhi[0]
    zf[...] = jnp.zeros(zf.shape, zf.dtype)
    zi[...] = jnp.zeros(zi.shape, zi.dtype)
    for c in copies[1:]:
        c.wait()
    si[1:own] = (sx[1:own] > 0.5).astype(jnp.int32)
    si[top:last] = (sx[top:last] > 0.5).astype(jnp.int32)

    from_low, send_low, send_high, from_high = mv[0], mv[1], mv[2], mv[3]
    valid_end = from_low + planes - send_low - send_high + from_high

    def plane_valid(i):
        p = i - own
        low = (p >= -from_low) & (p < 0)
        kept = (p >= send_low) & (p < planes - send_high)
        high = (p >= planes) & (p < planes + from_high)
        return low | kept | high

    def plane_copies(i):
        p = i - own
        s = p + from_low - jnp.where(p >= send_low, send_low, 0) - jnp.where(p >= planes, send_high, 0)
        s = jnp.clip(s, 0, cap - 1)
        srcs = (fx.at[:, i], gx.at[:, i], mx.at[i], si.at[i])
        dsts = (out_f.at[:, s], out_g.at[:, s], out_m.at[s], out_s.at[s])
        return [pltpu.make_async_copy(x, y, osem.at[i, k]) for k, (x, y) in enumerate(zip(srcs, dsts))]

    def zero_copies(s):
        srcs = (zf, zf.at[0:NG], zf.at[0], zi)
        dsts = (out_f.at[:, s], out_g.at[:, s], out_m.at[s], out_s.at[s])
        return [pltpu.make_async_copy(x, y, zsem.at[s, k]) for k, (x, y) in enumerate(zip(srcs, dsts))]

    for s in range(cap):
        @pl.when(s >= valid_end)
        def _():
            for c in zero_copies(s):
                c.start()

    loop(0, last + 1, lambda i: shift_masks(sx, bm, i))

    posts = set_bounds(flo, fhi, sm, cf, fs, gs, last, 1)
    loop(1, last, lambda i: edge_state(sx, gx, mx, cx, sm, cf, i))
    copies[0].wait()

    def step1(i):
        dissolve_plane(sx, mx, cf, m1, i)
        collide_plane(fx, gx, sx, cx, sm, fs, gs, i)

    loop(1, last, step1)
    posts()
    loop(1, last, lambda i: stream_plane(fs, gs, sx, fx, gx, i, bm))

    posts = set_bounds(flo, fhi, sm, cf, fs, gs, last, 4 + len(UP_Q))
    loop(1, last, lambda i: edge_state(sx, gx, m1, cx, sm, cf, i))

    def step2(i):
        dissolve_plane(sx, m1, cf, mx, i)
        collide_plane(fx, gx, sx, cx, sm, fs, gs, i)

    loop(1, last, step2)
    posts()

    def send_plane(i):
        @pl.when(plane_valid(i))
        def _():
            for c in plane_copies(i):
                c.start()

    def final(i):
        stream_plane(fs, gs, sx, fx, gx, i, bm)

        @pl.when(i > 1)
        def _():
            send_plane(i - 1)

    loop(1, last, final)
    send_plane(last - 1)
    for i in range(1, last):
        @pl.when(plane_valid(i))
        def _():
            for c in plane_copies(i):
                c.wait()
    for s in range(cap):
        @pl.when(s >= valid_end)
        def _():
            for c in zero_copies(s):
                c.wait()


def edge_kernel(lo, pop, sol, mnr, sld, out, buf_f, buf_g, buf_ms, sem):
    buf_ms[1] = sld[lo:lo + HALO].astype(jnp.float32)
    srcs = (pop.at[:, lo:lo + HALO], sol.at[:, lo:lo + HALO], mnr.at[lo:lo + HALO])
    bufs = (buf_f, buf_g, buf_ms.at[0])
    dsts = (out.at[0:NF], out.at[NF:NF + NG], out.at[NF + NG:NF + NG + 2])
    reads = [pltpu.make_async_copy(s, b, sem.at[0, k]) for k, (s, b) in enumerate(zip(srcs, bufs))]
    writes = [pltpu.make_async_copy(b, d, sem.at[1, k]) for k, (b, d) in enumerate(zip((buf_f, buf_g, buf_ms), dsts))]
    for c in reads:
        c.start()
    for r, w in zip(reads, writes):
        r.wait()
        w.start()
    for w in writes:
        w.wait()


def shards(populations, solute, mineral, solid, plane_moves):
    planes = populations.shape[1]
    cap = planes + 2 * MOVE_MOST
    ext = planes + 2 * HALO + 2
    count = lax.axis_size("blk")
    forward = [(i, (i + 1) % count) for i in range(count)]
    backward = [(i, (i - 1) % count) for i in range(count)]

    plane = populations.shape[2:]
    f32 = jnp.float32
    any_spec = pl.BlockSpec(memory_space=pl.ANY)
    vmem = pl.BlockSpec(memory_space=pltpu.VMEM)
    smem = pl.BlockSpec(memory_space=pltpu.SMEM)

    def edge(lo):
        return pl.pallas_call(
            functools.partial(edge_kernel, lo),
            out_shape=jax.ShapeDtypeStruct((NF + NG + 2, HALO) + plane, f32),
            in_specs=[any_spec, any_spec, any_spec, vmem],
            out_specs=any_spec,
            scratch_shapes=[
                pltpu.VMEM((NF, HALO) + plane, f32),
                pltpu.VMEM((NG, HALO) + plane, f32),
                pltpu.VMEM((2, HALO) + plane, f32),
                pltpu.SemaphoreType.DMA((2, 3)),
            ],
        )(populations, solute, mineral, solid)

    halo_lo = lax.ppermute(edge(planes - HALO), "blk", forward)
    halo_hi = lax.ppermute(edge(0), "blk", backward)

    up, down = pl.pallas_call(
        flux_kernel,
        out_shape=(
            jax.ShapeDtypeStruct((NFLUX,) + plane, f32),
            jax.ShapeDtypeStruct((NFLUX,) + plane, f32),
        ),
        in_specs=[vmem] * 4,
        out_specs=[vmem] * 2,
        scratch_shapes=[
            pltpu.VMEM((NF, planes) + plane, f32),
            pltpu.VMEM((NG, planes) + plane, f32),
            pltpu.VMEM((NF, planes) + plane, f32),
            pltpu.VMEM((NG, planes) + plane, f32),
        ]
        + [pltpu.VMEM((planes,) + plane, f32)] * 5,
    )(populations, solute, mineral, solid)
    flux_lo = lax.ppermute(up, "blk", forward)
    flux_hi = lax.ppermute(down, "blk", backward)

    me = lax.axis_index("blk")
    from_low = plane_moves[jnp.mod(me - 1, count), 1]
    send_low = plane_moves[me, 0]
    send_high = plane_moves[me, 1]
    from_high = plane_moves[jnp.mod(me + 1, count), 0]
    mv = jnp.stack([from_low, send_low, send_high, from_high]).astype(jnp.int32)

    return pl.pallas_call(
        main_kernel,
        out_shape=(
            jax.ShapeDtypeStruct((NF, cap) + plane, f32),
            jax.ShapeDtypeStruct((NG, cap) + plane, f32),
            jax.ShapeDtypeStruct((cap,) + plane, f32),
            jax.ShapeDtypeStruct((cap,) + plane, jnp.int32),
        ),
        in_specs=[smem, any_spec, any_spec, any_spec, vmem, any_spec, any_spec, vmem, vmem],
        out_specs=[any_spec] * 4,
        scratch_shapes=[
            pltpu.VMEM((NF, ext) + plane, f32),
            pltpu.VMEM((NG, ext) + plane, f32),
            pltpu.VMEM((NF, ext) + plane, f32),
            pltpu.VMEM((NG, ext) + plane, f32),
            pltpu.VMEM((ext,) + plane, f32),
            pltpu.VMEM((ext,) + plane, f32),
            pltpu.VMEM((ext,) + plane, f32),
            pltpu.VMEM((ext,) + plane, jnp.int32),
            pltpu.VMEM((ext,) + plane, f32),
            pltpu.VMEM((ext,) + plane, f32),
            pltpu.VMEM((ext,) + plane, f32),
            pltpu.VMEM((NF,) + plane, f32),
            pltpu.VMEM(plane, jnp.int32),
            pltpu.VMEM((len(SHIFTS), ext) + plane, f32),
            pltpu.SemaphoreType.DMA((11,)),
            pltpu.SemaphoreType.DMA((ext, 4)),
            pltpu.SemaphoreType.DMA((cap, 4)),
        ],
        compiler_params=pltpu.CompilerParams(vmem_limit_bytes=50 * 1024 * 1024),
    )(mv, populations, solute, mineral, solid, halo_lo, halo_hi, flux_lo, flux_hi)


def solution(mesh):
    return jax.shard_map(
        shards,
        mesh=mesh,
        in_specs=(
            P(None, "blk", None, None),
            P(None, "blk", None, None),
            P("blk", None, None),
            P("blk", None, None),
            P(),
        ),
        out_specs=(
            P(None, "blk", None, None),
            P(None, "blk", None, None),
            P("blk", None, None),
            P("blk", None, None),
        ),
        check_vma=False,
    )
```

```python
import functools

import jax
import jax.numpy as jnp
from jax import lax
from jax.experimental import pallas as pl
from jax.experimental.pallas import tpu as pltpu
from jax.sharding import PartitionSpec as P

MOVE_MOST = 3
HALO = 3

flow_vel = [
    (0, 0, 1),
    (1, 0, 1),
    (-1, 0, 1),
    (0, 1, 1),
    (0, -1, 1),
    (0, 0, -1),
    (1, 0, -1),
    (-1, 0, -1),
    (0, 1, -1),
    (0, -1, -1),
    (0, 0, 0),
    (1, 0, 0),
    (-1, 0, 0),
    (0, 1, 0),
    (0, -1, 0),
    (1, 1, 0),
    (-1, -1, 0),
    (1, -1, 0),
    (-1, 1, 0),
]
flow_weight = [
    1.0 / 18,
    1.0 / 36,
    1.0 / 36,
    1.0 / 36,
    1.0 / 36,
    1.0 / 18,
    1.0 / 36,
    1.0 / 36,
    1.0 / 36,
    1.0 / 36,
    1.0 / 3,
    1.0 / 18,
    1.0 / 18,
    1.0 / 18,
    1.0 / 18,
    1.0 / 36,
    1.0 / 36,
    1.0 / 36,
    1.0 / 36,
]
acid_vel = [(0, 0, 1), (0, 0, -1), (0, 0, 0), (1, 0, 0), (-1, 0, 0), (0, 1, 0), (0, -1, 0)]
acid_weight = [0.125, 0.125, 0.25, 0.125, 0.125, 0.125, 0.125]
relax_flow = 1.25
relax_acid = 0.8
body_force = 0.001
react_rate = 0.1
dissolve_rate = 0.5

NF = len(flow_vel)
NG = len(acid_vel)


def roll_xy(a, cx, cy):
    if cx:
        a = pltpu.roll(a, cx % a.shape[0], 0)
    if cy:
        a = pltpu.roll(a, cy % a.shape[1], 1)
    return a


def face_sum(ref, i):
    mid = ref[i]
    total = ref[i - 1] + ref[i + 1]
    total = total + (roll_xy(mid, 1, 0) + roll_xy(mid, -1, 0))
    return total + (roll_xy(mid, 0, 1) + roll_xy(mid, 0, -1))


def edge_state(sx, gx, mx, cx, sm, cf, i):
    conc = gx[0, i]
    for j in range(1, NG):
        conc = conc + gx[j, i]
    cx[i] = conc
    solid = sx[i] > 0.5
    sm[i] = jnp.where(solid, mx[i], 0.0)
    cf[i] = jnp.where(solid, 0.0, conc)


def collide_plane(fx, gx, sx, cx, sm, fs, gs, i):
    solid = sx[i] > 0.5
    f = [fx[q, i] for q in range(NF)]
    density = f[0]
    for q in range(1, NF):
        density = density + f[q]
    moments = []
    for axis in range(3):
        total = None
        for q, vel in enumerate(flow_vel):
            if vel[axis] == 0:
                continue
            term = f[q] if vel[axis] > 0 else -f[q]
            total = term if total is None else total + term
        moments.append(total)
    inv = 1.0 / density
    comps = [m * inv for m in moments]
    base = 1.0 - 1.5 * (comps[0] * comps[0] + comps[1] * comps[1] + comps[2] * comps[2])
    keep = 1.0 - 1.0 / relax_flow
    scaled = {}
    for w in set(flow_weight):
        scaled[w] = (w / relax_flow) * density

    def along(vel):
        total = None
        for axis in range(3):
            if vel[axis] == 0:
                continue
            term = comps[axis] if vel[axis] > 0 else -comps[axis]
            total = term if total is None else total + term
        return total

    done = set()
    for q, vel in enumerate(flow_vel):
        if q in done:
            continue
        opp = flow_vel.index(tuple(-c for c in vel))
        done |= {q, opp}
        weight = scaled[flow_weight[q]]
        if opp == q:
            fs[q, i] = jnp.where(solid, f[q], keep * f[q] + weight * base)
            continue
        cu = along(vel)
        even = base + 4.5 * (cu * cu)
        odd = 3.0 * cu
        if vel[2]:
            odd = odd + 3.0 * body_force * relax_flow * vel[2]
        for member, poly in ((q, even + odd), (opp, even - odd)):
            fs[member, i] = jnp.where(solid, f[member], keep * f[member] + weight * poly)
    conc = cx[i]
    sink = (react_rate * conc) * face_sum(sm, i)
    rate = 1.0 / relax_acid
    shared = rate * conc - sink
    slope = (4.0 * rate) * conc
    done = set()
    for j, vel in enumerate(acid_vel):
        if j in done:
            continue
        opp = acid_vel.index(tuple(-c for c in vel))
        done |= {j, opp}
        if opp == j:
            parts = ((j, shared),)
        else:
            cu = slope * along(vel)
            parts = ((j, shared + cu), (opp, shared - cu))
        for member, inner in parts:
            g = gx[member, i]
            relaxed = acid_weight[member] * inner - (rate - 1.0) * g
            gs[member, i] = jnp.where(solid, g, relaxed)


def dissolve_plane(sx, mx_src, cf, mx_dst, i):
    solid = sx[i] > 0.5
    mineral = mx_src[i]
    loss = (dissolve_rate * react_rate) * mineral * face_sum(cf, i)
    mx_dst[i] = jnp.where(solid, mineral - loss, mineral)


SHIFTS = [(cx, cy) for cx in (-1, 0, 1) for cy in (-1, 0, 1) if cx or cy]


def shift_masks(sx, bm, i):
    for c, (cx, cy) in enumerate(SHIFTS):
        bm[c, i] = roll_xy(sx[i], cx, cy)


def stream_plane(fs, gs, sx, fdst, gdst, i, bm=None):
    solid = sx[i] > 0.5
    masks = {}
    for q, vel in enumerate(flow_vel):
        cx, cy, cz = vel
        if vel == (0, 0, 0):
            fdst[q, i] = fs[q, i]
            continue
        opp = flow_vel.index((-cx, -cy, -cz))
        src = i - cz
        pulled = roll_xy(fs[q, src], cx, cy)
        if bm is None or (cx, cy) == (0, 0):
            blocked = roll_xy(sx[src], cx, cy) > 0.5
        else:
            blocked = bm[SHIFTS.index((cx, cy)), src] > 0.5
        masks[vel] = blocked
        arrived = jnp.where(blocked, fs[opp, i], pulled)
        fdst[q, i] = jnp.where(solid, fs[q, i], arrived)
    for j, vel in enumerate(acid_vel):
        cx, cy, cz = vel
        if vel == (0, 0, 0):
            gdst[j, i] = gs[j, i]
            continue
        opp = acid_vel.index((-cx, -cy, -cz))
        pulled = roll_xy(gs[j, i - cz], cx, cy)
        arrived = jnp.where(masks[vel], gs[opp, i], pulled)
        gdst[j, i] = jnp.where(solid, gs[j, i], arrived)


def loop(lo, hi, fn):
    def body(i, carry):
        fn(i)
        return carry

    lax.fori_loop(lo, hi, body, 0, unroll=2 if hi - lo > 4 else 1)


UP_Q = [q for q, vel in enumerate(flow_vel) if vel[2] == 1]
DOWN_Q = [q for q, vel in enumerate(flow_vel) if vel[2] == -1]
UP_J = acid_vel.index((0, 0, 1))
DOWN_J = acid_vel.index((0, 0, -1))
NFLUX = 3 + 2 * (len(UP_Q) + 1) + 2


def flux_kernel(pop, sol, mnr, sld, up, down, fs, gs, f1, g1, m1, sx, cx, sm, cf):
    planes = sld.shape[0]
    hi, lo = planes - HALO - 1, HALO
    sx[...] = sld[...].astype(jnp.float32)
    loop(lo - 2, hi + 3, lambda i: edge_state(sx, sol, mnr, cx, sm, cf, i))

    def step1(i):
        dissolve_plane(sx, mnr, cf, m1, i)
        collide_plane(pop, sol, sx, cx, sm, fs, gs, i)

    loop(lo - 1, hi + 2, step1)
    for dst, i, qs, j in ((up, hi, UP_Q, UP_J), (down, lo, DOWN_Q, DOWN_J)):
        dst[0] = sx[i]
        dst[1] = sm[i]
        dst[2] = cf[i]
        for n, q in enumerate(qs):
            dst[3 + n] = fs[q, i]
        dst[3 + len(qs)] = gs[j, i]
    loop(lo, hi + 1, lambda i: stream_plane(fs, gs, sx, f1, g1, i))
    for i in range(lo - 1, hi + 2):
        sm[i] = jnp.where(sx[i] > 0.5, m1[i], 0.0)
    for i in range(lo, hi + 1):
        conc = g1[0, i]
        for j in range(1, NG):
            conc = conc + g1[j, i]
        cx[i] = conc
        cf[i] = jnp.where(sx[i] > 0.5, 0.0, conc)
    loop(lo, hi + 1, lambda i: collide_plane(f1, g1, sx, cx, sm, fs, gs, i))
    base = 4 + len(UP_Q)
    for dst, i, qs, j in ((up, hi, UP_Q, UP_J), (down, lo, DOWN_Q, DOWN_J)):
        dst[base] = sm[i]
        dst[base + 1] = cf[i]
        for n, q in enumerate(qs):
            dst[base + 2 + n] = fs[q, i]
        dst[base + 2 + len(qs)] = gs[j, i]


def set_bounds(flo, fhi, sm, cf, fs, gs, last, base):
    sm[0] = flo[base]
    cf[0] = flo[base + 1]
    sm[last] = fhi[base]
    cf[last] = fhi[base + 1]

    def posts():
        for n, q in enumerate(UP_Q):
            fs[q, 0] = flo[base + 2 + n]
        gs[UP_J, 0] = flo[base + 2 + len(UP_Q)]
        for n, q in enumerate(DOWN_Q):
            fs[q, last] = fhi[base + 2 + n]
        gs[DOWN_J, last] = fhi[base + 2 + len(DOWN_Q)]

    return posts


def main_kernel(
    mv, pop, sol, mnr, sld, hlo, hhi, flo, fhi,
    out_f, out_g, out_m, out_s,
    fx, gx, fs, gs, mx, m1, sx, si, cx, sm, cf, zf, zi, bm, sem, osem, zsem,
):
    planes = sld.shape[0]
    cap = out_s.shape[0]
    last = planes + 2 * HALO + 1
    own = HALO + 1
    top = own + planes
    fill = [
        (pop, fx.at[:, own:top]),
        (sol, gx.at[:, own:top]),
        (mnr, mx.at[own:top]),
        (hlo.at[0:NF], fx.at[:, 1:own]),
        (hlo.at[NF:NF + NG], gx.at[:, 1:own]),
        (hlo.at[NF + NG], mx.at[1:own]),
        (hlo.at[NF + NG + 1], sx.at[1:own]),
        (hhi.at[0:NF], fx.at[:, top:last]),
        (hhi.at[NF:NF + NG], gx.at[:, top:last]),
        (hhi.at[NF + NG], mx.at[top:last]),
        (hhi.at[NF + NG + 1], sx.at[top:last]),
    ]
    copies = [pltpu.make_async_copy(s, d, sem.at[k]) for k, (s, d) in enumerate(fill)]
    for c in copies:
        c.start()
    sx[own:top] = sld[...].astype(jnp.float32)
    si[own:top] = sld[...]
    sx[0] = flo[0]
    sx[last] = fhi[0]
    zf[...] = jnp.zeros(zf.shape, zf.dtype)
    zi[...] = jnp.zeros(zi.shape, zi.dtype)
    for c in copies[1:]:
        c.wait()
    si[1:own] = (sx[1:own] > 0.5).astype(jnp.int32)
    si[top:last] = (sx[top:last] > 0.5).astype(jnp.int32)

    from_low, send_low, send_high, from_high = mv[0], mv[1], mv[2], mv[3]
    valid_end = from_low + planes - send_low - send_high + from_high

    def plane_valid(i):
        p = i - own
        low = (p >= -from_low) & (p < 0)
        kept = (p >= send_low) & (p < planes - send_high)
        high = (p >= planes) & (p < planes + from_high)
        return low | kept | high

    def plane_copies(i):
        p = i - own
        s = p + from_low - jnp.where(p >= send_low, send_low, 0) - jnp.where(p >= planes, send_high, 0)
        s = jnp.clip(s, 0, cap - 1)
        srcs = (fx.at[:, i], gx.at[:, i], mx.at[i], si.at[i])
        dsts = (out_f.at[:, s], out_g.at[:, s], out_m.at[s], out_s.at[s])
        return [pltpu.make_async_copy(x, y, osem.at[i, k]) for k, (x, y) in enumerate(zip(srcs, dsts))]

    def zero_copies(s):
        srcs = (zf, zf.at[0:NG], zf.at[0], zi)
        dsts = (out_f.at[:, s], out_g.at[:, s], out_m.at[s], out_s.at[s])
        return [pltpu.make_async_copy(x, y, zsem.at[s, k]) for k, (x, y) in enumerate(zip(srcs, dsts))]

    for s in range(cap):
        @pl.when(s >= valid_end)
        def _():
            for c in zero_copies(s):
                c.start()

    loop(0, last + 1, lambda i: shift_masks(sx, bm, i))

    posts = set_bounds(flo, fhi, sm, cf, fs, gs, last, 1)
    loop(1, last, lambda i: edge_state(sx, gx, mx, cx, sm, cf, i))
    copies[0].wait()

    posts()

    def step1(i):
        dissolve_plane(sx, mx, cf, m1, i)
        collide_plane(fx, gx, sx, cx, sm, fs, gs, i)

        @pl.when(i > 1)
        def _():
            stream_plane(fs, gs, sx, fx, gx, i - 1, bm)

    loop(1, last, step1)
    stream_plane(fs, gs, sx, fx, gx, last - 1, bm)

    posts = set_bounds(flo, fhi, sm, cf, fs, gs, last, 4 + len(UP_Q))
    loop(1, last, lambda i: edge_state(sx, gx, m1, cx, sm, cf, i))

    posts()

    def send_plane(i):
        @pl.when(plane_valid(i))
        def _():
            for c in plane_copies(i):
                c.start()

    def step2(i):
        dissolve_plane(sx, m1, cf, mx, i)
        collide_plane(fx, gx, sx, cx, sm, fs, gs, i)

        @pl.when(i > 1)
        def _():
            stream_plane(fs, gs, sx, fx, gx, i - 1, bm)

        @pl.when(i > 2)
        def _():
            send_plane(i - 2)

    loop(1, last, step2)
    stream_plane(fs, gs, sx, fx, gx, last - 1, bm)
    send_plane(last - 2)
    send_plane(last - 1)
    for i in range(1, last):
        @pl.when(plane_valid(i))
        def _():
            for c in plane_copies(i):
                c.wait()
    for s in range(cap):
        @pl.when(s >= valid_end)
        def _():
            for c in zero_copies(s):
                c.wait()


def edge_kernel(lo, pop, sol, mnr, sld, out, buf_f, buf_g, buf_ms, sem):
    buf_ms[1] = sld[lo:lo + HALO].astype(jnp.float32)
    srcs = (pop.at[:, lo:lo + HALO], sol.at[:, lo:lo + HALO], mnr.at[lo:lo + HALO])
    bufs = (buf_f, buf_g, buf_ms.at[0])
    dsts = (out.at[0:NF], out.at[NF:NF + NG], out.at[NF + NG:NF + NG + 2])
    reads = [pltpu.make_async_copy(s, b, sem.at[0, k]) for k, (s, b) in enumerate(zip(srcs, bufs))]
    writes = [pltpu.make_async_copy(b, d, sem.at[1, k]) for k, (b, d) in enumerate(zip((buf_f, buf_g, buf_ms), dsts))]
    for c in reads:
        c.start()
    for r, w in zip(reads, writes):
        r.wait()
        w.start()
    for w in writes:
        w.wait()


def shards(populations, solute, mineral, solid, plane_moves):
    planes = populations.shape[1]
    cap = planes + 2 * MOVE_MOST
    ext = planes + 2 * HALO + 2
    count = lax.axis_size("blk")
    forward = [(i, (i + 1) % count) for i in range(count)]
    backward = [(i, (i - 1) % count) for i in range(count)]

    plane = populations.shape[2:]
    f32 = jnp.float32
    any_spec = pl.BlockSpec(memory_space=pl.ANY)
    vmem = pl.BlockSpec(memory_space=pltpu.VMEM)
    smem = pl.BlockSpec(memory_space=pltpu.SMEM)

    def edge(lo):
        return pl.pallas_call(
            functools.partial(edge_kernel, lo),
            out_shape=jax.ShapeDtypeStruct((NF + NG + 2, HALO) + plane, f32),
            in_specs=[any_spec, any_spec, any_spec, vmem],
            out_specs=any_spec,
            scratch_shapes=[
                pltpu.VMEM((NF, HALO) + plane, f32),
                pltpu.VMEM((NG, HALO) + plane, f32),
                pltpu.VMEM((2, HALO) + plane, f32),
                pltpu.SemaphoreType.DMA((2, 3)),
            ],
        )(populations, solute, mineral, solid)

    halo_lo = lax.ppermute(edge(planes - HALO), "blk", forward)
    halo_hi = lax.ppermute(edge(0), "blk", backward)

    up, down = pl.pallas_call(
        flux_kernel,
        out_shape=(
            jax.ShapeDtypeStruct((NFLUX,) + plane, f32),
            jax.ShapeDtypeStruct((NFLUX,) + plane, f32),
        ),
        in_specs=[vmem] * 4,
        out_specs=[vmem] * 2,
        scratch_shapes=[
            pltpu.VMEM((NF, planes) + plane, f32),
            pltpu.VMEM((NG, planes) + plane, f32),
            pltpu.VMEM((NF, planes) + plane, f32),
            pltpu.VMEM((NG, planes) + plane, f32),
        ]
        + [pltpu.VMEM((planes,) + plane, f32)] * 5,
    )(populations, solute, mineral, solid)
    flux_lo = lax.ppermute(up, "blk", forward)
    flux_hi = lax.ppermute(down, "blk", backward)

    me = lax.axis_index("blk")
    from_low = plane_moves[jnp.mod(me - 1, count), 1]
    send_low = plane_moves[me, 0]
    send_high = plane_moves[me, 1]
    from_high = plane_moves[jnp.mod(me + 1, count), 0]
    mv = jnp.stack([from_low, send_low, send_high, from_high]).astype(jnp.int32)

    return pl.pallas_call(
        main_kernel,
        out_shape=(
            jax.ShapeDtypeStruct((NF, cap) + plane, f32),
            jax.ShapeDtypeStruct((NG, cap) + plane, f32),
            jax.ShapeDtypeStruct((cap,) + plane, f32),
            jax.ShapeDtypeStruct((cap,) + plane, jnp.int32),
        ),
        in_specs=[smem, any_spec, any_spec, any_spec, vmem, any_spec, any_spec, vmem, vmem],
        out_specs=[any_spec] * 4,
        scratch_shapes=[
            pltpu.VMEM((NF, ext) + plane, f32),
            pltpu.VMEM((NG, ext) + plane, f32),
            pltpu.VMEM((NF, ext) + plane, f32),
            pltpu.VMEM((NG, ext) + plane, f32),
            pltpu.VMEM((ext,) + plane, f32),
            pltpu.VMEM((ext,) + plane, f32),
            pltpu.VMEM((ext,) + plane, f32),
            pltpu.VMEM((ext,) + plane, jnp.int32),
            pltpu.VMEM((ext,) + plane, f32),
            pltpu.VMEM((ext,) + plane, f32),
            pltpu.VMEM((ext,) + plane, f32),
            pltpu.VMEM((NF,) + plane, f32),
            pltpu.VMEM(plane, jnp.int32),
            pltpu.VMEM((len(SHIFTS), ext) + plane, f32),
            pltpu.SemaphoreType.DMA((11,)),
            pltpu.SemaphoreType.DMA((ext, 4)),
            pltpu.SemaphoreType.DMA((cap, 4)),
        ],
        compiler_params=pltpu.CompilerParams(vmem_limit_bytes=50 * 1024 * 1024),
    )(mv, populations, solute, mineral, solid, halo_lo, halo_hi, flux_lo, flux_hi)


def solution(mesh):
    return jax.shard_map(
        shards,
        mesh=mesh,
        in_specs=(
            P(None, "blk", None, None),
            P(None, "blk", None, None),
            P("blk", None, None),
            P("blk", None, None),
            P(),
        ),
        out_specs=(
            P(None, "blk", None, None),
            P(None, "blk", None, None),
            P("blk", None, None),
            P("blk", None, None),
        ),
        check_vma=False,
    )
```

```python
import functools

import jax
import jax.numpy as jnp
from jax import lax
from jax.experimental import pallas as pl
from jax.experimental.pallas import tpu as pltpu
from jax.sharding import PartitionSpec as P

MOVE_MOST = 3
HALO = 3

flow_vel = [
    (0, 0, 1),
    (1, 0, 1),
    (-1, 0, 1),
    (0, 1, 1),
    (0, -1, 1),
    (0, 0, -1),
    (1, 0, -1),
    (-1, 0, -1),
    (0, 1, -1),
    (0, -1, -1),
    (0, 0, 0),
    (1, 0, 0),
    (-1, 0, 0),
    (0, 1, 0),
    (0, -1, 0),
    (1, 1, 0),
    (-1, -1, 0),
    (1, -1, 0),
    (-1, 1, 0),
]
flow_weight = [
    1.0 / 18,
    1.0 / 36,
    1.0 / 36,
    1.0 / 36,
    1.0 / 36,
    1.0 / 18,
    1.0 / 36,
    1.0 / 36,
    1.0 / 36,
    1.0 / 36,
    1.0 / 3,
    1.0 / 18,
    1.0 / 18,
    1.0 / 18,
    1.0 / 18,
    1.0 / 36,
    1.0 / 36,
    1.0 / 36,
    1.0 / 36,
]
acid_vel = [(0, 0, 1), (0, 0, -1), (0, 0, 0), (1, 0, 0), (-1, 0, 0), (0, 1, 0), (0, -1, 0)]
acid_weight = [0.125, 0.125, 0.25, 0.125, 0.125, 0.125, 0.125]
relax_flow = 1.25
relax_acid = 0.8
body_force = 0.001
react_rate = 0.1
dissolve_rate = 0.5

NF = len(flow_vel)
NG = len(acid_vel)


def roll_xy(a, cx, cy):
    if cx:
        a = pltpu.roll(a, cx % a.shape[0], 0)
    if cy:
        a = pltpu.roll(a, cy % a.shape[1], 1)
    return a


def face_sum(ref, i):
    mid = ref[i]
    total = ref[i - 1] + ref[i + 1]
    total = total + (roll_xy(mid, 1, 0) + roll_xy(mid, -1, 0))
    return total + (roll_xy(mid, 0, 1) + roll_xy(mid, 0, -1))


def edge_state(sx, gx, mx, cx, sm, cf, i):
    conc = gx[0, i]
    for j in range(1, NG):
        conc = conc + gx[j, i]
    cx[i] = conc
    solid = sx[i] > 0.5
    sm[i] = jnp.where(solid, mx[i], 0.0)
    cf[i] = jnp.where(solid, 0.0, conc)


def collide_plane(fx, gx, sx, cx, sm, fs, gs, i):
    solid = sx[i] > 0.5
    f = [fx[q, i] for q in range(NF)]
    density = f[0]
    for q in range(1, NF):
        density = density + f[q]
    moments = []
    for axis in range(3):
        total = None
        for q, vel in enumerate(flow_vel):
            if vel[axis] == 0:
                continue
            term = f[q] if vel[axis] > 0 else -f[q]
            total = term if total is None else total + term
        moments.append(total)
    inv = 1.0 / density
    comps = [m * inv for m in moments]
    base = 1.0 - 1.5 * (comps[0] * comps[0] + comps[1] * comps[1] + comps[2] * comps[2])
    keep = 1.0 - 1.0 / relax_flow
    scaled = {}
    for w in set(flow_weight):
        scaled[w] = (w / relax_flow) * density

    def along(vel):
        total = None
        for axis in range(3):
            if vel[axis] == 0:
                continue
            term = comps[axis] if vel[axis] > 0 else -comps[axis]
            total = term if total is None else total + term
        return total

    done = set()
    for q, vel in enumerate(flow_vel):
        if q in done:
            continue
        opp = flow_vel.index(tuple(-c for c in vel))
        done |= {q, opp}
        weight = scaled[flow_weight[q]]
        if opp == q:
            fs[q, i] = jnp.where(solid, f[q], keep * f[q] + weight * base)
            continue
        cu = along(vel)
        even = base + 4.5 * (cu * cu)
        odd = 3.0 * cu
        if vel[2]:
            odd = odd + 3.0 * body_force * relax_flow * vel[2]
        for member, poly in ((q, even + odd), (opp, even - odd)):
            fs[member, i] = jnp.where(solid, f[member], keep * f[member] + weight * poly)
    conc = cx[i]
    sink = (react_rate * conc) * face_sum(sm, i)
    rate = 1.0 / relax_acid
    shared = rate * conc - sink
    slope = (4.0 * rate) * conc
    done = set()
    for j, vel in enumerate(acid_vel):
        if j in done:
            continue
        opp = acid_vel.index(tuple(-c for c in vel))
        done |= {j, opp}
        if opp == j:
            parts = ((j, shared),)
        else:
            cu = slope * along(vel)
            parts = ((j, shared + cu), (opp, shared - cu))
        for member, inner in parts:
            g = gx[member, i]
            relaxed = acid_weight[member] * inner - (rate - 1.0) * g
            gs[member, i] = jnp.where(solid, g, relaxed)


def dissolve_plane(sx, mx_src, cf, mx_dst, i):
    solid = sx[i] > 0.5
    mineral = mx_src[i]
    loss = (dissolve_rate * react_rate) * mineral * face_sum(cf, i)
    mx_dst[i] = jnp.where(solid, mineral - loss, mineral)


SHIFTS = [(cx, cy) for cx in (-1, 0, 1) for cy in (-1, 0, 1) if cx or cy]


def shift_masks(sx, bm, i):
    for c, (cx, cy) in enumerate(SHIFTS):
        bm[c, i] = roll_xy(sx[i], cx, cy)


def stream_plane(fs, gs, sx, fdst, gdst, i, bm=None):
    solid = sx[i] > 0.5
    masks = {}
    for q, vel in enumerate(flow_vel):
        cx, cy, cz = vel
        if vel == (0, 0, 0):
            fdst[q, i] = fs[q, i]
            continue
        opp = flow_vel.index((-cx, -cy, -cz))
        src = i - cz
        pulled = roll_xy(fs[q, src], cx, cy)
        if bm is None or (cx, cy) == (0, 0):
            blocked = roll_xy(sx[src], cx, cy) > 0.5
        else:
            blocked = bm[SHIFTS.index((cx, cy)), src] > 0.5
        masks[vel] = blocked
        arrived = jnp.where(blocked, fs[opp, i], pulled)
        fdst[q, i] = jnp.where(solid, fs[q, i], arrived)
    for j, vel in enumerate(acid_vel):
        cx, cy, cz = vel
        if vel == (0, 0, 0):
            gdst[j, i] = gs[j, i]
            continue
        opp = acid_vel.index((-cx, -cy, -cz))
        pulled = roll_xy(gs[j, i - cz], cx, cy)
        arrived = jnp.where(masks[vel], gs[opp, i], pulled)
        gdst[j, i] = jnp.where(solid, gs[j, i], arrived)


def loop(lo, hi, fn):
    def body(i, carry):
        fn(i)
        return carry

    lax.fori_loop(lo, hi, body, 0, unroll=2 if hi - lo > 4 else 1)


UP_Q = [q for q, vel in enumerate(flow_vel) if vel[2] == 1]
DOWN_Q = [q for q, vel in enumerate(flow_vel) if vel[2] == -1]
UP_J = acid_vel.index((0, 0, 1))
DOWN_J = acid_vel.index((0, 0, -1))
NFLUX = 3 + 2 * (len(UP_Q) + 1) + 2


def flux_kernel(pop, sol, mnr, sld, up, down, fs, gs, f1, g1, m1, sx, cx, sm, cf):
    planes = sld.shape[0]
    hi, lo = planes - HALO - 1, HALO
    sx[...] = sld[...].astype(jnp.float32)
    loop(lo - 2, hi + 3, lambda i: edge_state(sx, sol, mnr, cx, sm, cf, i))

    def step1(i):
        dissolve_plane(sx, mnr, cf, m1, i)
        collide_plane(pop, sol, sx, cx, sm, fs, gs, i)

    loop(lo - 1, hi + 2, step1)
    for dst, i, qs, j in ((up, hi, UP_Q, UP_J), (down, lo, DOWN_Q, DOWN_J)):
        dst[0] = sx[i]
        dst[1] = sm[i]
        dst[2] = cf[i]
        for n, q in enumerate(qs):
            dst[3 + n] = fs[q, i]
        dst[3 + len(qs)] = gs[j, i]
    loop(lo, hi + 1, lambda i: stream_plane(fs, gs, sx, f1, g1, i))
    for i in range(lo - 1, hi + 2):
        sm[i] = jnp.where(sx[i] > 0.5, m1[i], 0.0)
    for i in range(lo, hi + 1):
        conc = g1[0, i]
        for j in range(1, NG):
            conc = conc + g1[j, i]
        cx[i] = conc
        cf[i] = jnp.where(sx[i] > 0.5, 0.0, conc)
    loop(lo, hi + 1, lambda i: collide_plane(f1, g1, sx, cx, sm, fs, gs, i))
    base = 4 + len(UP_Q)
    for dst, i, qs, j in ((up, hi, UP_Q, UP_J), (down, lo, DOWN_Q, DOWN_J)):
        dst[base] = sm[i]
        dst[base + 1] = cf[i]
        for n, q in enumerate(qs):
            dst[base + 2 + n] = fs[q, i]
        dst[base + 2 + len(qs)] = gs[j, i]


def set_bounds(flo, fhi, sm, cf, fs, gs, last, base):
    sm[0] = flo[base]
    cf[0] = flo[base + 1]
    sm[last] = fhi[base]
    cf[last] = fhi[base + 1]

    def posts():
        for n, q in enumerate(UP_Q):
            fs[q, 0] = flo[base + 2 + n]
        gs[UP_J, 0] = flo[base + 2 + len(UP_Q)]
        for n, q in enumerate(DOWN_Q):
            fs[q, last] = fhi[base + 2 + n]
        gs[DOWN_J, last] = fhi[base + 2 + len(DOWN_Q)]

    return posts


def main_kernel(
    mv, pop, sol, mnr, sld, hlo, hhi, flo, fhi,
    out_f, out_g, out_m, out_s,
    fx, gx, fs, gs, mx, m1, sx, si, cx, sm, cf, zf, zi, bm, sem, osem, zsem,
):
    planes = sld.shape[0]
    cap = out_s.shape[0]
    last = planes + 2 * HALO + 1
    own = HALO + 1
    top = own + planes
    fill = [
        (pop, fx.at[:, own:top]),
        (sol, gx.at[:, own:top]),
        (mnr, mx.at[own:top]),
        (hlo.at[0:NF], fx.at[:, 1:own]),
        (hlo.at[NF:NF + NG], gx.at[:, 1:own]),
        (hlo.at[NF + NG], mx.at[1:own]),
        (hlo.at[NF + NG + 1], sx.at[1:own]),
        (hhi.at[0:NF], fx.at[:, top:last]),
        (hhi.at[NF:NF + NG], gx.at[:, top:last]),
        (hhi.at[NF + NG], mx.at[top:last]),
        (hhi.at[NF + NG + 1], sx.at[top:last]),
    ]
    copies = [pltpu.make_async_copy(s, d, sem.at[k]) for k, (s, d) in enumerate(fill)]
    for c in copies:
        c.start()
    sx[own:top] = sld[...].astype(jnp.float32)
    si[own:top] = sld[...]
    sx[0] = flo[0]
    sx[last] = fhi[0]
    zf[...] = jnp.zeros(zf.shape, zf.dtype)
    zi[...] = jnp.zeros(zi.shape, zi.dtype)
    for c in copies[1:]:
        c.wait()
    si[1:own] = (sx[1:own] > 0.5).astype(jnp.int32)
    si[top:last] = (sx[top:last] > 0.5).astype(jnp.int32)

    from_low, send_low, send_high, from_high = mv[0], mv[1], mv[2], mv[3]
    valid_end = from_low + planes - send_low - send_high + from_high

    def plane_valid(i):
        p = i - own
        low = (p >= -from_low) & (p < 0)
        kept = (p >= send_low) & (p < planes - send_high)
        high = (p >= planes) & (p < planes + from_high)
        return low | kept | high

    def plane_copies(i):
        p = i - own
        s = p + from_low - jnp.where(p >= send_low, send_low, 0) - jnp.where(p >= planes, send_high, 0)
        s = jnp.clip(s, 0, cap - 1)
        srcs = (fx.at[:, i], gx.at[:, i], mx.at[i], si.at[i])
        dsts = (out_f.at[:, s], out_g.at[:, s], out_m.at[s], out_s.at[s])
        return [pltpu.make_async_copy(x, y, osem.at[i, k]) for k, (x, y) in enumerate(zip(srcs, dsts))]

    def zero_copies(s):
        srcs = (zf, zf.at[0:NG], zf.at[0], zi)
        dsts = (out_f.at[:, s], out_g.at[:, s], out_m.at[s], out_s.at[s])
        return [pltpu.make_async_copy(x, y, zsem.at[s, k]) for k, (x, y) in enumerate(zip(srcs, dsts))]

    for s in range(cap):
        @pl.when(s >= valid_end)
        def _():
            for c in zero_copies(s):
                c.start()

    loop(0, last + 1, lambda i: shift_masks(sx, bm, i))

    posts = set_bounds(flo, fhi, sm, cf, fs, gs, last, 1)
    loop(1, last, lambda i: edge_state(sx, gx, mx, cx, sm, cf, i))
    copies[0].wait()

    posts()

    def collide1(i):
        dissolve_plane(sx, mx, cf, m1, i)
        collide_plane(fx, gx, sx, cx, sm, fs, gs, i)

    def step1(i):
        collide1(i)
        stream_plane(fs, gs, sx, fx, gx, i - 1, bm)

    collide1(1)
    loop(2, last, step1)
    stream_plane(fs, gs, sx, fx, gx, last - 1, bm)

    posts = set_bounds(flo, fhi, sm, cf, fs, gs, last, 4 + len(UP_Q))
    loop(1, last, lambda i: edge_state(sx, gx, m1, cx, sm, cf, i))

    posts()

    def send_plane(i):
        @pl.when(plane_valid(i))
        def _():
            for c in plane_copies(i):
                c.start()

    def collide2(i):
        dissolve_plane(sx, m1, cf, mx, i)
        collide_plane(fx, gx, sx, cx, sm, fs, gs, i)

    def step2(i):
        collide2(i)
        stream_plane(fs, gs, sx, fx, gx, i - 1, bm)

        @pl.when(i > 2)
        def _():
            send_plane(i - 2)

    collide2(1)
    loop(2, last, step2)
    stream_plane(fs, gs, sx, fx, gx, last - 1, bm)
    send_plane(last - 2)
    send_plane(last - 1)
    for i in range(1, last):
        @pl.when(plane_valid(i))
        def _():
            for c in plane_copies(i):
                c.wait()
    for s in range(cap):
        @pl.when(s >= valid_end)
        def _():
            for c in zero_copies(s):
                c.wait()


def edge_kernel(lo, pop, sol, mnr, sld, out, buf_f, buf_g, buf_ms, sem):
    buf_ms[1] = sld[lo:lo + HALO].astype(jnp.float32)
    srcs = (pop.at[:, lo:lo + HALO], sol.at[:, lo:lo + HALO], mnr.at[lo:lo + HALO])
    bufs = (buf_f, buf_g, buf_ms.at[0])
    dsts = (out.at[0:NF], out.at[NF:NF + NG], out.at[NF + NG:NF + NG + 2])
    reads = [pltpu.make_async_copy(s, b, sem.at[0, k]) for k, (s, b) in enumerate(zip(srcs, bufs))]
    writes = [pltpu.make_async_copy(b, d, sem.at[1, k]) for k, (b, d) in enumerate(zip((buf_f, buf_g, buf_ms), dsts))]
    for c in reads:
        c.start()
    for r, w in zip(reads, writes):
        r.wait()
        w.start()
    for w in writes:
        w.wait()


def shards(populations, solute, mineral, solid, plane_moves):
    planes = populations.shape[1]
    cap = planes + 2 * MOVE_MOST
    ext = planes + 2 * HALO + 2
    count = lax.axis_size("blk")
    forward = [(i, (i + 1) % count) for i in range(count)]
    backward = [(i, (i - 1) % count) for i in range(count)]

    plane = populations.shape[2:]
    f32 = jnp.float32
    any_spec = pl.BlockSpec(memory_space=pl.ANY)
    vmem = pl.BlockSpec(memory_space=pltpu.VMEM)
    smem = pl.BlockSpec(memory_space=pltpu.SMEM)

    def edge(lo):
        return pl.pallas_call(
            functools.partial(edge_kernel, lo),
            out_shape=jax.ShapeDtypeStruct((NF + NG + 2, HALO) + plane, f32),
            in_specs=[any_spec, any_spec, any_spec, vmem],
            out_specs=any_spec,
            scratch_shapes=[
                pltpu.VMEM((NF, HALO) + plane, f32),
                pltpu.VMEM((NG, HALO) + plane, f32),
                pltpu.VMEM((2, HALO) + plane, f32),
                pltpu.SemaphoreType.DMA((2, 3)),
            ],
        )(populations, solute, mineral, solid)

    halo_lo = lax.ppermute(edge(planes - HALO), "blk", forward)
    halo_hi = lax.ppermute(edge(0), "blk", backward)

    up, down = pl.pallas_call(
        flux_kernel,
        out_shape=(
            jax.ShapeDtypeStruct((NFLUX,) + plane, f32),
            jax.ShapeDtypeStruct((NFLUX,) + plane, f32),
        ),
        in_specs=[vmem] * 4,
        out_specs=[vmem] * 2,
        scratch_shapes=[
            pltpu.VMEM((NF, planes) + plane, f32),
            pltpu.VMEM((NG, planes) + plane, f32),
            pltpu.VMEM((NF, planes) + plane, f32),
            pltpu.VMEM((NG, planes) + plane, f32),
        ]
        + [pltpu.VMEM((planes,) + plane, f32)] * 5,
    )(populations, solute, mineral, solid)
    flux_lo = lax.ppermute(up, "blk", forward)
    flux_hi = lax.ppermute(down, "blk", backward)

    me = lax.axis_index("blk")
    from_low = plane_moves[jnp.mod(me - 1, count), 1]
    send_low = plane_moves[me, 0]
    send_high = plane_moves[me, 1]
    from_high = plane_moves[jnp.mod(me + 1, count), 0]
    mv = jnp.stack([from_low, send_low, send_high, from_high]).astype(jnp.int32)

    return pl.pallas_call(
        main_kernel,
        out_shape=(
            jax.ShapeDtypeStruct((NF, cap) + plane, f32),
            jax.ShapeDtypeStruct((NG, cap) + plane, f32),
            jax.ShapeDtypeStruct((cap,) + plane, f32),
            jax.ShapeDtypeStruct((cap,) + plane, jnp.int32),
        ),
        in_specs=[smem, any_spec, any_spec, any_spec, vmem, any_spec, any_spec, vmem, vmem],
        out_specs=[any_spec] * 4,
        scratch_shapes=[
            pltpu.VMEM((NF, ext) + plane, f32),
            pltpu.VMEM((NG, ext) + plane, f32),
            pltpu.VMEM((NF, ext) + plane, f32),
            pltpu.VMEM((NG, ext) + plane, f32),
            pltpu.VMEM((ext,) + plane, f32),
            pltpu.VMEM((ext,) + plane, f32),
            pltpu.VMEM((ext,) + plane, f32),
            pltpu.VMEM((ext,) + plane, jnp.int32),
            pltpu.VMEM((ext,) + plane, f32),
            pltpu.VMEM((ext,) + plane, f32),
            pltpu.VMEM((ext,) + plane, f32),
            pltpu.VMEM((NF,) + plane, f32),
            pltpu.VMEM(plane, jnp.int32),
            pltpu.VMEM((len(SHIFTS), ext) + plane, f32),
            pltpu.SemaphoreType.DMA((11,)),
            pltpu.SemaphoreType.DMA((ext, 4)),
            pltpu.SemaphoreType.DMA((cap, 4)),
        ],
        compiler_params=pltpu.CompilerParams(vmem_limit_bytes=50 * 1024 * 1024),
    )(mv, populations, solute, mineral, solid, halo_lo, halo_hi, flux_lo, flux_hi)


def solution(mesh):
    return jax.shard_map(
        shards,
        mesh=mesh,
        in_specs=(
            P(None, "blk", None, None),
            P(None, "blk", None, None),
            P("blk", None, None),
            P("blk", None, None),
            P(),
        ),
        out_specs=(
            P(None, "blk", None, None),
            P(None, "blk", None, None),
            P("blk", None, None),
            P("blk", None, None),
        ),
        check_vma=False,
    )
```

```python
import functools

import jax
import jax.numpy as jnp
from jax import lax
from jax.experimental import pallas as pl
from jax.experimental.pallas import tpu as pltpu
from jax.sharding import PartitionSpec as P

MOVE_MOST = 3
HALO = 3

flow_vel = [
    (0, 0, 1),
    (1, 0, 1),
    (-1, 0, 1),
    (0, 1, 1),
    (0, -1, 1),
    (0, 0, -1),
    (1, 0, -1),
    (-1, 0, -1),
    (0, 1, -1),
    (0, -1, -1),
    (0, 0, 0),
    (1, 0, 0),
    (-1, 0, 0),
    (0, 1, 0),
    (0, -1, 0),
    (1, 1, 0),
    (-1, -1, 0),
    (1, -1, 0),
    (-1, 1, 0),
]
flow_weight = [
    1.0 / 18,
    1.0 / 36,
    1.0 / 36,
    1.0 / 36,
    1.0 / 36,
    1.0 / 18,
    1.0 / 36,
    1.0 / 36,
    1.0 / 36,
    1.0 / 36,
    1.0 / 3,
    1.0 / 18,
    1.0 / 18,
    1.0 / 18,
    1.0 / 18,
    1.0 / 36,
    1.0 / 36,
    1.0 / 36,
    1.0 / 36,
]
acid_vel = [(0, 0, 1), (0, 0, -1), (0, 0, 0), (1, 0, 0), (-1, 0, 0), (0, 1, 0), (0, -1, 0)]
acid_weight = [0.125, 0.125, 0.25, 0.125, 0.125, 0.125, 0.125]
relax_flow = 1.25
relax_acid = 0.8
body_force = 0.001
react_rate = 0.1
dissolve_rate = 0.5

NF = len(flow_vel)
NG = len(acid_vel)


def roll_xy(a, cx, cy):
    if cx:
        a = pltpu.roll(a, cx % a.shape[0], 0)
    if cy:
        a = pltpu.roll(a, cy % a.shape[1], 1)
    return a


def face_sum(ref, i):
    mid = ref[i]
    total = ref[i - 1] + ref[i + 1]
    total = total + (roll_xy(mid, 1, 0) + roll_xy(mid, -1, 0))
    return total + (roll_xy(mid, 0, 1) + roll_xy(mid, 0, -1))


def edge_state(sx, gx, mx, cx, sm, cf, i):
    conc = gx[0, i]
    for j in range(1, NG):
        conc = conc + gx[j, i]
    cx[i] = conc
    solid = sx[i] > 0.5
    sm[i] = jnp.where(solid, mx[i], 0.0)
    cf[i] = jnp.where(solid, 0.0, conc)


def collide_plane(fx, gx, sx, cx, sm, fs, gs, i):
    solid = sx[i] > 0.5
    f = [fx[q, i] for q in range(NF)]
    density = f[0]
    for q in range(1, NF):
        density = density + f[q]
    moments = []
    for axis in range(3):
        total = None
        for q, vel in enumerate(flow_vel):
            if vel[axis] == 0:
                continue
            term = f[q] if vel[axis] > 0 else -f[q]
            total = term if total is None else total + term
        moments.append(total)
    inv = 1.0 / density
    comps = [m * inv for m in moments]
    base = 1.0 - 1.5 * (comps[0] * comps[0] + comps[1] * comps[1] + comps[2] * comps[2])
    keep = 1.0 - 1.0 / relax_flow
    scaled = {}
    for w in set(flow_weight):
        scaled[w] = (w / relax_flow) * density

    def along(vel):
        total = None
        for axis in range(3):
            if vel[axis] == 0:
                continue
            term = comps[axis] if vel[axis] > 0 else -comps[axis]
            total = term if total is None else total + term
        return total

    done = set()
    for q, vel in enumerate(flow_vel):
        if q in done:
            continue
        opp = flow_vel.index(tuple(-c for c in vel))
        done |= {q, opp}
        weight = scaled[flow_weight[q]]
        if opp == q:
            fs[q, i] = jnp.where(solid, f[q], keep * f[q] + weight * base)
            continue
        cu = along(vel)
        even = base + 4.5 * (cu * cu)
        odd = 3.0 * cu
        if vel[2]:
            odd = odd + 3.0 * body_force * relax_flow * vel[2]
        for member, poly in ((q, even + odd), (opp, even - odd)):
            fs[member, i] = jnp.where(solid, f[member], keep * f[member] + weight * poly)
    conc = cx[i]
    sink = (react_rate * conc) * face_sum(sm, i)
    rate = 1.0 / relax_acid
    shared = rate * conc - sink
    slope = (4.0 * rate) * conc
    done = set()
    for j, vel in enumerate(acid_vel):
        if j in done:
            continue
        opp = acid_vel.index(tuple(-c for c in vel))
        done |= {j, opp}
        if opp == j:
            parts = ((j, shared),)
        else:
            cu = slope * along(vel)
            parts = ((j, shared + cu), (opp, shared - cu))
        for member, inner in parts:
            g = gx[member, i]
            relaxed = acid_weight[member] * inner - (rate - 1.0) * g
            gs[member, i] = jnp.where(solid, g, relaxed)


def dissolve_plane(sx, mx_src, cf, mx_dst, i):
    solid = sx[i] > 0.5
    mineral = mx_src[i]
    loss = (dissolve_rate * react_rate) * mineral * face_sum(cf, i)
    mx_dst[i] = jnp.where(solid, mineral - loss, mineral)


SHIFTS = [(cx, cy) for cx in (-1, 0, 1) for cy in (-1, 0, 1) if cx or cy]


def shift_masks(sx, bm, i):
    for c, (cx, cy) in enumerate(SHIFTS):
        bm[c, i] = roll_xy(sx[i], cx, cy)


def stream_plane(fs, gs, sx, fdst, gdst, i, bm=None):
    solid = sx[i] > 0.5
    masks = {}
    for q, vel in enumerate(flow_vel):
        cx, cy, cz = vel
        if vel == (0, 0, 0):
            fdst[q, i] = fs[q, i]
            continue
        opp = flow_vel.index((-cx, -cy, -cz))
        src = i - cz
        pulled = roll_xy(fs[q, src], cx, cy)
        if bm is None or (cx, cy) == (0, 0):
            blocked = roll_xy(sx[src], cx, cy) > 0.5
        else:
            blocked = bm[SHIFTS.index((cx, cy)), src] > 0.5
        masks[vel] = blocked
        arrived = jnp.where(blocked, fs[opp, i], pulled)
        fdst[q, i] = jnp.where(solid, fs[q, i], arrived)
    for j, vel in enumerate(acid_vel):
        cx, cy, cz = vel
        if vel == (0, 0, 0):
            gdst[j, i] = gs[j, i]
            continue
        opp = acid_vel.index((-cx, -cy, -cz))
        pulled = roll_xy(gs[j, i - cz], cx, cy)
        arrived = jnp.where(masks[vel], gs[opp, i], pulled)
        gdst[j, i] = jnp.where(solid, gs[j, i], arrived)


def loop(lo, hi, fn):
    def body(i, carry):
        fn(i)
        return carry

    lax.fori_loop(lo, hi, body, 0, unroll=2 if hi - lo > 4 else 1)


UP_Q = [q for q, vel in enumerate(flow_vel) if vel[2] == 1]
DOWN_Q = [q for q, vel in enumerate(flow_vel) if vel[2] == -1]
UP_J = acid_vel.index((0, 0, 1))
DOWN_J = acid_vel.index((0, 0, -1))
NFLUX = 3 + 2 * (len(UP_Q) + 1) + 2


def flux_kernel(pop, sol, mnr, sld, up, down, fs, gs, f1, g1, m1, sx, cx, sm, cf):
    planes = sld.shape[0]
    hi, lo = planes - HALO - 1, HALO
    sx[...] = sld[...].astype(jnp.float32)
    loop(lo - 2, hi + 3, lambda i: edge_state(sx, sol, mnr, cx, sm, cf, i))

    def step1(i):
        dissolve_plane(sx, mnr, cf, m1, i)
        collide_plane(pop, sol, sx, cx, sm, fs, gs, i)

    loop(lo - 1, hi + 2, step1)
    for dst, i, qs, j in ((up, hi, UP_Q, UP_J), (down, lo, DOWN_Q, DOWN_J)):
        dst[0] = sx[i]
        dst[1] = sm[i]
        dst[2] = cf[i]
        for n, q in enumerate(qs):
            dst[3 + n] = fs[q, i]
        dst[3 + len(qs)] = gs[j, i]
    loop(lo, hi + 1, lambda i: stream_plane(fs, gs, sx, f1, g1, i))
    for i in range(lo - 1, hi + 2):
        sm[i] = jnp.where(sx[i] > 0.5, m1[i], 0.0)
    for i in range(lo, hi + 1):
        conc = g1[0, i]
        for j in range(1, NG):
            conc = conc + g1[j, i]
        cx[i] = conc
        cf[i] = jnp.where(sx[i] > 0.5, 0.0, conc)
    loop(lo, hi + 1, lambda i: collide_plane(f1, g1, sx, cx, sm, fs, gs, i))
    base = 4 + len(UP_Q)
    for dst, i, qs, j in ((up, hi, UP_Q, UP_J), (down, lo, DOWN_Q, DOWN_J)):
        dst[base] = sm[i]
        dst[base + 1] = cf[i]
        for n, q in enumerate(qs):
            dst[base + 2 + n] = fs[q, i]
        dst[base + 2 + len(qs)] = gs[j, i]


def set_bounds(flo, fhi, sm, cf, fs, gs, last, base):
    sm[0] = flo[base]
    cf[0] = flo[base + 1]
    sm[last] = fhi[base]
    cf[last] = fhi[base + 1]

    def posts():
        for n, q in enumerate(UP_Q):
            fs[q, 0] = flo[base + 2 + n]
        gs[UP_J, 0] = flo[base + 2 + len(UP_Q)]
        for n, q in enumerate(DOWN_Q):
            fs[q, last] = fhi[base + 2 + n]
        gs[DOWN_J, last] = fhi[base + 2 + len(DOWN_Q)]

    return posts


def main_kernel(
    mv, pop, sol, mnr, sld, hlo, hhi, flo, fhi,
    out_f, out_g, out_m, out_s,
    fx, gx, fs, gs, mx, m1, sx, si, cx, sm, cf, zf, zi, bm, sem, osem, zsem,
):
    planes = sld.shape[0]
    cap = out_s.shape[0]
    last = planes + 2 * HALO + 1
    own = HALO + 1
    top = own + planes
    fill = [
        (pop, fx.at[:, own:top]),
        (sol, gx.at[:, own:top]),
        (mnr, mx.at[own:top]),
        (hlo.at[0:NF], fx.at[:, 1:own]),
        (hlo.at[NF:NF + NG], gx.at[:, 1:own]),
        (hlo.at[NF + NG], mx.at[1:own]),
        (hlo.at[NF + NG + 1], sx.at[1:own]),
        (hhi.at[0:NF], fx.at[:, top:last]),
        (hhi.at[NF:NF + NG], gx.at[:, top:last]),
        (hhi.at[NF + NG], mx.at[top:last]),
        (hhi.at[NF + NG + 1], sx.at[top:last]),
    ]
    copies = [pltpu.make_async_copy(s, d, sem.at[k]) for k, (s, d) in enumerate(fill)]
    for c in copies:
        c.start()
    sx[own:top] = sld[...].astype(jnp.float32)
    si[own:top] = sld[...]
    sx[0] = flo[0]
    sx[last] = fhi[0]
    zf[...] = jnp.zeros(zf.shape, zf.dtype)
    zi[...] = jnp.zeros(zi.shape, zi.dtype)
    for c in copies[1:]:
        c.wait()
    si[1:own] = (sx[1:own] > 0.5).astype(jnp.int32)
    si[top:last] = (sx[top:last] > 0.5).astype(jnp.int32)

    from_low, send_low, send_high, from_high = mv[0], mv[1], mv[2], mv[3]
    valid_end = from_low + planes - send_low - send_high + from_high

    def plane_valid(i):
        p = i - own
        low = (p >= -from_low) & (p < 0)
        kept = (p >= send_low) & (p < planes - send_high)
        high = (p >= planes) & (p < planes + from_high)
        return low | kept | high

    def plane_copies(i):
        p = i - own
        s = p + from_low - jnp.where(p >= send_low, send_low, 0) - jnp.where(p >= planes, send_high, 0)
        s = jnp.clip(s, 0, cap - 1)
        srcs = (fx.at[:, i], gx.at[:, i], mx.at[i], si.at[i])
        dsts = (out_f.at[:, s], out_g.at[:, s], out_m.at[s], out_s.at[s])
        return [pltpu.make_async_copy(x, y, osem.at[i, k]) for k, (x, y) in enumerate(zip(srcs, dsts))]

    def zero_copies(s):
        srcs = (zf, zf.at[0:NG], zf.at[0], zi)
        dsts = (out_f.at[:, s], out_g.at[:, s], out_m.at[s], out_s.at[s])
        return [pltpu.make_async_copy(x, y, zsem.at[s, k]) for k, (x, y) in enumerate(zip(srcs, dsts))]

    for s in range(cap):
        @pl.when(s >= valid_end)
        def _():
            for c in zero_copies(s):
                c.start()

    loop(0, last + 1, lambda i: shift_masks(sx, bm, i))

    posts = set_bounds(flo, fhi, sm, cf, fs, gs, last, 1)
    loop(1, last, lambda i: edge_state(sx, gx, mx, cx, sm, cf, i))
    copies[0].wait()

    posts()

    def collide1(i):
        dissolve_plane(sx, mx, cf, m1, i)
        collide_plane(fx, gx, sx, cx, sm, fs, gs, i)

    def step1(i):
        collide1(i)
        stream_plane(fs, gs, sx, fx, gx, i - 1, bm)
        edge_state(sx, gx, m1, cx, sm, cf, i - 1)

    collide1(1)
    loop(2, last, step1)
    stream_plane(fs, gs, sx, fx, gx, last - 1, bm)
    edge_state(sx, gx, m1, cx, sm, cf, last - 1)

    posts = set_bounds(flo, fhi, sm, cf, fs, gs, last, 4 + len(UP_Q))

    posts()

    def send_plane(i):
        @pl.when(plane_valid(i))
        def _():
            for c in plane_copies(i):
                c.start()

    def collide2(i):
        dissolve_plane(sx, m1, cf, mx, i)
        collide_plane(fx, gx, sx, cx, sm, fs, gs, i)

    def step2(i):
        collide2(i)
        stream_plane(fs, gs, sx, fx, gx, i - 1, bm)

        @pl.when(i > 2)
        def _():
            send_plane(i - 2)

    collide2(1)
    loop(2, last, step2)
    stream_plane(fs, gs, sx, fx, gx, last - 1, bm)
    send_plane(last - 2)
    send_plane(last - 1)
    for i in range(1, last):
        @pl.when(plane_valid(i))
        def _():
            for c in plane_copies(i):
                c.wait()
    for s in range(cap):
        @pl.when(s >= valid_end)
        def _():
            for c in zero_copies(s):
                c.wait()


def edge_kernel(lo, pop, sol, mnr, sld, out, buf_f, buf_g, buf_ms, sem):
    buf_ms[1] = sld[lo:lo + HALO].astype(jnp.float32)
    srcs = (pop.at[:, lo:lo + HALO], sol.at[:, lo:lo + HALO], mnr.at[lo:lo + HALO])
    bufs = (buf_f, buf_g, buf_ms.at[0])
    dsts = (out.at[0:NF], out.at[NF:NF + NG], out.at[NF + NG:NF + NG + 2])
    reads = [pltpu.make_async_copy(s, b, sem.at[0, k]) for k, (s, b) in enumerate(zip(srcs, bufs))]
    writes = [pltpu.make_async_copy(b, d, sem.at[1, k]) for k, (b, d) in enumerate(zip((buf_f, buf_g, buf_ms), dsts))]
    for c in reads:
        c.start()
    for r, w in zip(reads, writes):
        r.wait()
        w.start()
    for w in writes:
        w.wait()


def shards(populations, solute, mineral, solid, plane_moves):
    planes = populations.shape[1]
    cap = planes + 2 * MOVE_MOST
    ext = planes + 2 * HALO + 2
    count = lax.axis_size("blk")
    forward = [(i, (i + 1) % count) for i in range(count)]
    backward = [(i, (i - 1) % count) for i in range(count)]

    plane = populations.shape[2:]
    f32 = jnp.float32
    any_spec = pl.BlockSpec(memory_space=pl.ANY)
    vmem = pl.BlockSpec(memory_space=pltpu.VMEM)
    smem = pl.BlockSpec(memory_space=pltpu.SMEM)

    def edge(lo):
        return pl.pallas_call(
            functools.partial(edge_kernel, lo),
            out_shape=jax.ShapeDtypeStruct((NF + NG + 2, HALO) + plane, f32),
            in_specs=[any_spec, any_spec, any_spec, vmem],
            out_specs=any_spec,
            scratch_shapes=[
                pltpu.VMEM((NF, HALO) + plane, f32),
                pltpu.VMEM((NG, HALO) + plane, f32),
                pltpu.VMEM((2, HALO) + plane, f32),
                pltpu.SemaphoreType.DMA((2, 3)),
            ],
        )(populations, solute, mineral, solid)

    halo_lo = lax.ppermute(edge(planes - HALO), "blk", forward)
    halo_hi = lax.ppermute(edge(0), "blk", backward)

    up, down = pl.pallas_call(
        flux_kernel,
        out_shape=(
            jax.ShapeDtypeStruct((NFLUX,) + plane, f32),
            jax.ShapeDtypeStruct((NFLUX,) + plane, f32),
        ),
        in_specs=[vmem] * 4,
        out_specs=[vmem] * 2,
        scratch_shapes=[
            pltpu.VMEM((NF, planes) + plane, f32),
            pltpu.VMEM((NG, planes) + plane, f32),
            pltpu.VMEM((NF, planes) + plane, f32),
            pltpu.VMEM((NG, planes) + plane, f32),
        ]
        + [pltpu.VMEM((planes,) + plane, f32)] * 5,
    )(populations, solute, mineral, solid)
    flux_lo = lax.ppermute(up, "blk", forward)
    flux_hi = lax.ppermute(down, "blk", backward)

    me = lax.axis_index("blk")
    from_low = plane_moves[jnp.mod(me - 1, count), 1]
    send_low = plane_moves[me, 0]
    send_high = plane_moves[me, 1]
    from_high = plane_moves[jnp.mod(me + 1, count), 0]
    mv = jnp.stack([from_low, send_low, send_high, from_high]).astype(jnp.int32)

    return pl.pallas_call(
        main_kernel,
        out_shape=(
            jax.ShapeDtypeStruct((NF, cap) + plane, f32),
            jax.ShapeDtypeStruct((NG, cap) + plane, f32),
            jax.ShapeDtypeStruct((cap,) + plane, f32),
            jax.ShapeDtypeStruct((cap,) + plane, jnp.int32),
        ),
        in_specs=[smem, any_spec, any_spec, any_spec, vmem, any_spec, any_spec, vmem, vmem],
        out_specs=[any_spec] * 4,
        scratch_shapes=[
            pltpu.VMEM((NF, ext) + plane, f32),
            pltpu.VMEM((NG, ext) + plane, f32),
            pltpu.VMEM((NF, ext) + plane, f32),
            pltpu.VMEM((NG, ext) + plane, f32),
            pltpu.VMEM((ext,) + plane, f32),
            pltpu.VMEM((ext,) + plane, f32),
            pltpu.VMEM((ext,) + plane, f32),
            pltpu.VMEM((ext,) + plane, jnp.int32),
            pltpu.VMEM((ext,) + plane, f32),
            pltpu.VMEM((ext,) + plane, f32),
            pltpu.VMEM((ext,) + plane, f32),
            pltpu.VMEM((NF,) + plane, f32),
            pltpu.VMEM(plane, jnp.int32),
            pltpu.VMEM((len(SHIFTS), ext) + plane, f32),
            pltpu.SemaphoreType.DMA((11,)),
            pltpu.SemaphoreType.DMA((ext, 4)),
            pltpu.SemaphoreType.DMA((cap, 4)),
        ],
        compiler_params=pltpu.CompilerParams(vmem_limit_bytes=50 * 1024 * 1024),
    )(mv, populations, solute, mineral, solid, halo_lo, halo_hi, flux_lo, flux_hi)


def solution(mesh):
    return jax.shard_map(
        shards,
        mesh=mesh,
        in_specs=(
            P(None, "blk", None, None),
            P(None, "blk", None, None),
            P("blk", None, None),
            P("blk", None, None),
            P(),
        ),
        out_specs=(
            P(None, "blk", None, None),
            P(None, "blk", None, None),
            P("blk", None, None),
            P("blk", None, None),
        ),
        check_vma=False,
    )
```

```python
import functools

import jax
import jax.numpy as jnp
from jax import lax
from jax.experimental import pallas as pl
from jax.experimental.pallas import tpu as pltpu
from jax.sharding import PartitionSpec as P

MOVE_MOST = 3
HALO = 3

flow_vel = [
    (0, 0, 1),
    (1, 0, 1),
    (-1, 0, 1),
    (0, 1, 1),
    (0, -1, 1),
    (0, 0, -1),
    (1, 0, -1),
    (-1, 0, -1),
    (0, 1, -1),
    (0, -1, -1),
    (0, 0, 0),
    (1, 0, 0),
    (-1, 0, 0),
    (0, 1, 0),
    (0, -1, 0),
    (1, 1, 0),
    (-1, -1, 0),
    (1, -1, 0),
    (-1, 1, 0),
]
flow_weight = [
    1.0 / 18,
    1.0 / 36,
    1.0 / 36,
    1.0 / 36,
    1.0 / 36,
    1.0 / 18,
    1.0 / 36,
    1.0 / 36,
    1.0 / 36,
    1.0 / 36,
    1.0 / 3,
    1.0 / 18,
    1.0 / 18,
    1.0 / 18,
    1.0 / 18,
    1.0 / 36,
    1.0 / 36,
    1.0 / 36,
    1.0 / 36,
]
acid_vel = [(0, 0, 1), (0, 0, -1), (0, 0, 0), (1, 0, 0), (-1, 0, 0), (0, 1, 0), (0, -1, 0)]
acid_weight = [0.125, 0.125, 0.25, 0.125, 0.125, 0.125, 0.125]
relax_flow = 1.25
relax_acid = 0.8
body_force = 0.001
react_rate = 0.1
dissolve_rate = 0.5

NF = len(flow_vel)
NG = len(acid_vel)


def roll_xy(a, cx, cy):
    if cx:
        a = pltpu.roll(a, cx % a.shape[0], 0)
    if cy:
        a = pltpu.roll(a, cy % a.shape[1], 1)
    return a


def face_sum(ref, i):
    mid = ref[i]
    total = ref[i - 1] + ref[i + 1]
    total = total + (roll_xy(mid, 1, 0) + roll_xy(mid, -1, 0))
    return total + (roll_xy(mid, 0, 1) + roll_xy(mid, 0, -1))


def edge_state(sx, gx, mx, cx, sm, cf, i):
    conc = gx[0, i]
    for j in range(1, NG):
        conc = conc + gx[j, i]
    cx[i] = conc
    solid = sx[i] > 0.5
    sm[i] = jnp.where(solid, mx[i], 0.0)
    cf[i] = jnp.where(solid, 0.0, conc)


def collide_plane(fx, gx, sx, cx, sm, fs, gs, i):
    solid = sx[i] > 0.5
    f = [fx[q, i] for q in range(NF)]
    density = f[0]
    for q in range(1, NF):
        density = density + f[q]
    moments = []
    for axis in range(3):
        total = None
        for q, vel in enumerate(flow_vel):
            if vel[axis] == 0:
                continue
            term = f[q] if vel[axis] > 0 else -f[q]
            total = term if total is None else total + term
        moments.append(total)
    inv = 1.0 / density
    comps = [m * inv for m in moments]
    base = 1.0 - 1.5 * (comps[0] * comps[0] + comps[1] * comps[1] + comps[2] * comps[2])
    keep = 1.0 - 1.0 / relax_flow
    scaled = {}
    for w in set(flow_weight):
        scaled[w] = (w / relax_flow) * density

    def along(vel):
        total = None
        for axis in range(3):
            if vel[axis] == 0:
                continue
            term = comps[axis] if vel[axis] > 0 else -comps[axis]
            total = term if total is None else total + term
        return total

    done = set()
    for q, vel in enumerate(flow_vel):
        if q in done:
            continue
        opp = flow_vel.index(tuple(-c for c in vel))
        done |= {q, opp}
        weight = scaled[flow_weight[q]]
        if opp == q:
            fs[q, i] = jnp.where(solid, f[q], keep * f[q] + weight * base)
            continue
        cu = along(vel)
        even = base + 4.5 * (cu * cu)
        odd = 3.0 * cu
        if vel[2]:
            odd = odd + 3.0 * body_force * relax_flow * vel[2]
        for member, poly in ((q, even + odd), (opp, even - odd)):
            fs[member, i] = jnp.where(solid, f[member], keep * f[member] + weight * poly)
    conc = cx[i]
    sink = (react_rate * conc) * face_sum(sm, i)
    rate = 1.0 / relax_acid
    shared = rate * conc - sink
    slope = (4.0 * rate) * conc
    done = set()
    for j, vel in enumerate(acid_vel):
        if j in done:
            continue
        opp = acid_vel.index(tuple(-c for c in vel))
        done |= {j, opp}
        if opp == j:
            parts = ((j, shared),)
        else:
            cu = slope * along(vel)
            parts = ((j, shared + cu), (opp, shared - cu))
        for member, inner in parts:
            g = gx[member, i]
            relaxed = acid_weight[member] * inner - (rate - 1.0) * g
            gs[member, i] = jnp.where(solid, g, relaxed)


def dissolve_plane(sx, mx_src, cf, mx_dst, i):
    solid = sx[i] > 0.5
    mineral = mx_src[i]
    loss = (dissolve_rate * react_rate) * mineral * face_sum(cf, i)
    mx_dst[i] = jnp.where(solid, mineral - loss, mineral)


SHIFTS = [(cx, cy) for cx in (-1, 0, 1) for cy in (-1, 0, 1) if cx or cy]


def shift_masks(sx, bm, i):
    for c, (cx, cy) in enumerate(SHIFTS):
        bm[c, i] = roll_xy(sx[i], cx, cy)


def stream_plane(fs, gs, sx, fdst, gdst, i, bm=None):
    solid = sx[i] > 0.5
    masks = {}
    for q, vel in enumerate(flow_vel):
        cx, cy, cz = vel
        if vel == (0, 0, 0):
            fdst[q, i] = fs[q, i]
            continue
        opp = flow_vel.index((-cx, -cy, -cz))
        src = i - cz
        pulled = roll_xy(fs[q, src], cx, cy)
        if bm is None or (cx, cy) == (0, 0):
            blocked = roll_xy(sx[src], cx, cy) > 0.5
        else:
            blocked = bm[SHIFTS.index((cx, cy)), src] > 0.5
        masks[vel] = blocked
        arrived = jnp.where(blocked, fs[opp, i], pulled)
        fdst[q, i] = jnp.where(solid, fs[q, i], arrived)
    for j, vel in enumerate(acid_vel):
        cx, cy, cz = vel
        if vel == (0, 0, 0):
            gdst[j, i] = gs[j, i]
            continue
        opp = acid_vel.index((-cx, -cy, -cz))
        pulled = roll_xy(gs[j, i - cz], cx, cy)
        arrived = jnp.where(masks[vel], gs[opp, i], pulled)
        gdst[j, i] = jnp.where(solid, gs[j, i], arrived)


def loop(lo, hi, fn):
    def body(i, carry):
        fn(i)
        return carry

    lax.fori_loop(lo, hi, body, 0, unroll=2 if hi - lo > 4 else 1)


UP_Q = [q for q, vel in enumerate(flow_vel) if vel[2] == 1]
DOWN_Q = [q for q, vel in enumerate(flow_vel) if vel[2] == -1]
UP_J = acid_vel.index((0, 0, 1))
DOWN_J = acid_vel.index((0, 0, -1))
NFLUX = 3 + 2 * (len(UP_Q) + 1) + 2


def flux_kernel(pop, sol, mnr, sld, up, down, fs, gs, f1, g1, m1, sx, cx, sm, cf):
    planes = sld.shape[0]
    hi, lo = planes - HALO - 1, HALO
    sx[...] = sld[...].astype(jnp.float32)
    loop(lo - 2, hi + 3, lambda i: edge_state(sx, sol, mnr, cx, sm, cf, i))

    def step1(i):
        dissolve_plane(sx, mnr, cf, m1, i)
        collide_plane(pop, sol, sx, cx, sm, fs, gs, i)

    loop(lo - 1, hi + 2, step1)
    for dst, i, qs, j in ((up, hi, UP_Q, UP_J), (down, lo, DOWN_Q, DOWN_J)):
        dst[0] = sx[i]
        dst[1] = sm[i]
        dst[2] = cf[i]
        for n, q in enumerate(qs):
            dst[3 + n] = fs[q, i]
        dst[3 + len(qs)] = gs[j, i]
    loop(lo, hi + 1, lambda i: stream_plane(fs, gs, sx, f1, g1, i))
    for i in range(lo - 1, hi + 2):
        sm[i] = jnp.where(sx[i] > 0.5, m1[i], 0.0)
    for i in range(lo, hi + 1):
        conc = g1[0, i]
        for j in range(1, NG):
            conc = conc + g1[j, i]
        cx[i] = conc
        cf[i] = jnp.where(sx[i] > 0.5, 0.0, conc)
    loop(lo, hi + 1, lambda i: collide_plane(f1, g1, sx, cx, sm, fs, gs, i))
    base = 4 + len(UP_Q)
    for dst, i, qs, j in ((up, hi, UP_Q, UP_J), (down, lo, DOWN_Q, DOWN_J)):
        dst[base] = sm[i]
        dst[base + 1] = cf[i]
        for n, q in enumerate(qs):
            dst[base + 2 + n] = fs[q, i]
        dst[base + 2 + len(qs)] = gs[j, i]
    up[NFLUX:NFLUX + HALO] = sx[planes - HALO:planes]
    down[NFLUX:NFLUX + HALO] = sx[0:HALO]


def set_bounds(flo, fhi, sm, cf, fs, gs, last, base):
    sm[0] = flo[base]
    cf[0] = flo[base + 1]
    sm[last] = fhi[base]
    cf[last] = fhi[base + 1]

    def posts():
        for n, q in enumerate(UP_Q):
            fs[q, 0] = flo[base + 2 + n]
        gs[UP_J, 0] = flo[base + 2 + len(UP_Q)]
        for n, q in enumerate(DOWN_Q):
            fs[q, last] = fhi[base + 2 + n]
        gs[DOWN_J, last] = fhi[base + 2 + len(DOWN_Q)]

    return posts


def main_kernel(
    mv, pop, sol, mnr, sld, hlo, hhi, flo, fhi,
    out_f, out_g, out_m, out_s,
    fx, gx, fs, gs, mx, m1, sx, si, cx, sm, cf, zf, zi, bm, sem, osem, zsem,
):
    planes = sld.shape[0]
    cap = out_s.shape[0]
    last = planes + 2 * HALO + 1
    own = HALO + 1
    top = own + planes
    fill = [
        (pop, fx.at[:, own:top]),
        (sol, gx.at[:, own:top]),
        (mnr, mx.at[own:top]),
        (hlo.at[0:NF], fx.at[:, 1:own]),
        (hlo.at[NF:NF + NG], gx.at[:, 1:own]),
        (hlo.at[NF + NG], mx.at[1:own]),
        (hhi.at[0:NF], fx.at[:, top:last]),
        (hhi.at[NF:NF + NG], gx.at[:, top:last]),
        (hhi.at[NF + NG], mx.at[top:last]),
    ]
    copies = [pltpu.make_async_copy(s, d, sem.at[k]) for k, (s, d) in enumerate(fill)]
    for c in copies:
        c.start()
    sx[own:top] = sld[...].astype(jnp.float32)
    si[own:top] = sld[...]
    sx[0] = flo[0]
    sx[last] = fhi[0]
    sx[1:own] = flo[NFLUX:NFLUX + HALO]
    sx[top:last] = fhi[NFLUX:NFLUX + HALO]
    zf[...] = jnp.zeros(zf.shape, zf.dtype)
    zi[...] = jnp.zeros(zi.shape, zi.dtype)
    for c in copies[1:]:
        c.wait()
    si[1:own] = (sx[1:own] > 0.5).astype(jnp.int32)
    si[top:last] = (sx[top:last] > 0.5).astype(jnp.int32)

    from_low, send_low, send_high, from_high = mv[0], mv[1], mv[2], mv[3]
    valid_end = from_low + planes - send_low - send_high + from_high

    def plane_valid(i):
        p = i - own
        low = (p >= -from_low) & (p < 0)
        kept = (p >= send_low) & (p < planes - send_high)
        high = (p >= planes) & (p < planes + from_high)
        return low | kept | high

    def plane_copies(i):
        p = i - own
        s = p + from_low - jnp.where(p >= send_low, send_low, 0) - jnp.where(p >= planes, send_high, 0)
        s = jnp.clip(s, 0, cap - 1)
        srcs = (fx.at[:, i], gx.at[:, i], mx.at[i], si.at[i])
        dsts = (out_f.at[:, s], out_g.at[:, s], out_m.at[s], out_s.at[s])
        return [pltpu.make_async_copy(x, y, osem.at[i, k]) for k, (x, y) in enumerate(zip(srcs, dsts))]

    def zero_copies(s):
        srcs = (zf, zf.at[0:NG], zf.at[0], zi)
        dsts = (out_f.at[:, s], out_g.at[:, s], out_m.at[s], out_s.at[s])
        return [pltpu.make_async_copy(x, y, zsem.at[s, k]) for k, (x, y) in enumerate(zip(srcs, dsts))]

    for s in range(cap):
        @pl.when(s >= valid_end)
        def _():
            for c in zero_copies(s):
                c.start()

    loop(0, last + 1, lambda i: shift_masks(sx, bm, i))

    posts = set_bounds(flo, fhi, sm, cf, fs, gs, last, 1)
    loop(1, last, lambda i: edge_state(sx, gx, mx, cx, sm, cf, i))
    copies[0].wait()

    posts()

    def collide1(i):
        dissolve_plane(sx, mx, cf, m1, i)
        collide_plane(fx, gx, sx, cx, sm, fs, gs, i)

    def step1(i):
        collide1(i)
        stream_plane(fs, gs, sx, fx, gx, i - 1, bm)
        edge_state(sx, gx, m1, cx, sm, cf, i - 1)

    collide1(1)
    loop(2, last, step1)
    stream_plane(fs, gs, sx, fx, gx, last - 1, bm)
    edge_state(sx, gx, m1, cx, sm, cf, last - 1)

    posts = set_bounds(flo, fhi, sm, cf, fs, gs, last, 4 + len(UP_Q))

    posts()

    def send_plane(i):
        @pl.when(plane_valid(i))
        def _():
            for c in plane_copies(i):
                c.start()

    def collide2(i):
        dissolve_plane(sx, m1, cf, mx, i)
        collide_plane(fx, gx, sx, cx, sm, fs, gs, i)

    def step2(i):
        collide2(i)
        stream_plane(fs, gs, sx, fx, gx, i - 1, bm)

        @pl.when(i > 2)
        def _():
            send_plane(i - 2)

    collide2(1)
    loop(2, last, step2)
    stream_plane(fs, gs, sx, fx, gx, last - 1, bm)
    send_plane(last - 2)
    send_plane(last - 1)
    for i in range(1, last):
        @pl.when(plane_valid(i))
        def _():
            for c in plane_copies(i):
                c.wait()
    for s in range(cap):
        @pl.when(s >= valid_end)
        def _():
            for c in zero_copies(s):
                c.wait()


def edge_kernel(lo, pop, sol, mnr, out, buf_f, buf_g, buf_m, sem):
    srcs = (pop.at[:, lo:lo + HALO], sol.at[:, lo:lo + HALO], mnr.at[lo:lo + HALO])
    bufs = (buf_f, buf_g, buf_m)
    dsts = (out.at[0:NF], out.at[NF:NF + NG], out.at[NF + NG])
    reads = [pltpu.make_async_copy(s, b, sem.at[0, k]) for k, (s, b) in enumerate(zip(srcs, bufs))]
    writes = [pltpu.make_async_copy(b, d, sem.at[1, k]) for k, (b, d) in enumerate(zip(bufs, dsts))]
    for c in reads:
        c.start()
    for r, w in zip(reads, writes):
        r.wait()
        w.start()
    for w in writes:
        w.wait()


def shards(populations, solute, mineral, solid, plane_moves):
    planes = populations.shape[1]
    cap = planes + 2 * MOVE_MOST
    ext = planes + 2 * HALO + 2
    count = lax.axis_size("blk")
    forward = [(i, (i + 1) % count) for i in range(count)]
    backward = [(i, (i - 1) % count) for i in range(count)]

    plane = populations.shape[2:]
    f32 = jnp.float32
    any_spec = pl.BlockSpec(memory_space=pl.ANY)
    vmem = pl.BlockSpec(memory_space=pltpu.VMEM)
    smem = pl.BlockSpec(memory_space=pltpu.SMEM)

    def edge(lo):
        return pl.pallas_call(
            functools.partial(edge_kernel, lo),
            out_shape=jax.ShapeDtypeStruct((NF + NG + 1, HALO) + plane, f32),
            in_specs=[any_spec, any_spec, any_spec],
            out_specs=any_spec,
            scratch_shapes=[
                pltpu.VMEM((NF, HALO) + plane, f32),
                pltpu.VMEM((NG, HALO) + plane, f32),
                pltpu.VMEM((HALO,) + plane, f32),
                pltpu.SemaphoreType.DMA((2, 3)),
            ],
        )(populations, solute, mineral)

    halo_lo = lax.ppermute(edge(planes - HALO), "blk", forward)
    halo_hi = lax.ppermute(edge(0), "blk", backward)

    up, down = pl.pallas_call(
        flux_kernel,
        out_shape=(
            jax.ShapeDtypeStruct((NFLUX + HALO,) + plane, f32),
            jax.ShapeDtypeStruct((NFLUX + HALO,) + plane, f32),
        ),
        in_specs=[vmem] * 4,
        out_specs=[vmem] * 2,
        scratch_shapes=[
            pltpu.VMEM((NF, planes) + plane, f32),
            pltpu.VMEM((NG, planes) + plane, f32),
            pltpu.VMEM((NF, planes) + plane, f32),
            pltpu.VMEM((NG, planes) + plane, f32),
        ]
        + [pltpu.VMEM((planes,) + plane, f32)] * 5,
    )(populations, solute, mineral, solid)
    flux_lo = lax.ppermute(up, "blk", forward)
    flux_hi = lax.ppermute(down, "blk", backward)

    me = lax.axis_index("blk")
    from_low = plane_moves[jnp.mod(me - 1, count), 1]
    send_low = plane_moves[me, 0]
    send_high = plane_moves[me, 1]
    from_high = plane_moves[jnp.mod(me + 1, count), 0]
    mv = jnp.stack([from_low, send_low, send_high, from_high]).astype(jnp.int32)

    return pl.pallas_call(
        main_kernel,
        out_shape=(
            jax.ShapeDtypeStruct((NF, cap) + plane, f32),
            jax.ShapeDtypeStruct((NG, cap) + plane, f32),
            jax.ShapeDtypeStruct((cap,) + plane, f32),
            jax.ShapeDtypeStruct((cap,) + plane, jnp.int32),
        ),
        in_specs=[smem, any_spec, any_spec, any_spec, vmem, any_spec, any_spec, vmem, vmem],
        out_specs=[any_spec] * 4,
        scratch_shapes=[
            pltpu.VMEM((NF, ext) + plane, f32),
            pltpu.VMEM((NG, ext) + plane, f32),
            pltpu.VMEM((NF, ext) + plane, f32),
            pltpu.VMEM((NG, ext) + plane, f32),
            pltpu.VMEM((ext,) + plane, f32),
            pltpu.VMEM((ext,) + plane, f32),
            pltpu.VMEM((ext,) + plane, f32),
            pltpu.VMEM((ext,) + plane, jnp.int32),
            pltpu.VMEM((ext,) + plane, f32),
            pltpu.VMEM((ext,) + plane, f32),
            pltpu.VMEM((ext,) + plane, f32),
            pltpu.VMEM((NF,) + plane, f32),
            pltpu.VMEM(plane, jnp.int32),
            pltpu.VMEM((len(SHIFTS), ext) + plane, f32),
            pltpu.SemaphoreType.DMA((9,)),
            pltpu.SemaphoreType.DMA((ext, 4)),
            pltpu.SemaphoreType.DMA((cap, 4)),
        ],
        compiler_params=pltpu.CompilerParams(vmem_limit_bytes=50 * 1024 * 1024),
    )(mv, populations, solute, mineral, solid, halo_lo, halo_hi, flux_lo, flux_hi)


def solution(mesh):
    return jax.shard_map(
        shards,
        mesh=mesh,
        in_specs=(
            P(None, "blk", None, None),
            P(None, "blk", None, None),
            P("blk", None, None),
            P("blk", None, None),
            P(),
        ),
        out_specs=(
            P(None, "blk", None, None),
            P(None, "blk", None, None),
            P("blk", None, None),
            P("blk", None, None),
        ),
        check_vma=False,
    )
```

```python
import functools

import jax
import jax.numpy as jnp
from jax import lax
from jax.experimental import pallas as pl
from jax.experimental.pallas import tpu as pltpu
from jax.sharding import PartitionSpec as P

MOVE_MOST = 3
HALO = 3

flow_vel = [
    (0, 0, 1),
    (1, 0, 1),
    (-1, 0, 1),
    (0, 1, 1),
    (0, -1, 1),
    (0, 0, -1),
    (1, 0, -1),
    (-1, 0, -1),
    (0, 1, -1),
    (0, -1, -1),
    (0, 0, 0),
    (1, 0, 0),
    (-1, 0, 0),
    (0, 1, 0),
    (0, -1, 0),
    (1, 1, 0),
    (-1, -1, 0),
    (1, -1, 0),
    (-1, 1, 0),
]
flow_weight = [
    1.0 / 18,
    1.0 / 36,
    1.0 / 36,
    1.0 / 36,
    1.0 / 36,
    1.0 / 18,
    1.0 / 36,
    1.0 / 36,
    1.0 / 36,
    1.0 / 36,
    1.0 / 3,
    1.0 / 18,
    1.0 / 18,
    1.0 / 18,
    1.0 / 18,
    1.0 / 36,
    1.0 / 36,
    1.0 / 36,
    1.0 / 36,
]
acid_vel = [(0, 0, 1), (0, 0, -1), (0, 0, 0), (1, 0, 0), (-1, 0, 0), (0, 1, 0), (0, -1, 0)]
acid_weight = [0.125, 0.125, 0.25, 0.125, 0.125, 0.125, 0.125]
relax_flow = 1.25
relax_acid = 0.8
body_force = 0.001
react_rate = 0.1
dissolve_rate = 0.5

NF = len(flow_vel)
NG = len(acid_vel)


def roll_xy(a, cx, cy):
    if cx:
        a = pltpu.roll(a, cx % a.shape[0], 0)
    if cy:
        a = pltpu.roll(a, cy % a.shape[1], 1)
    return a


def face_sum(ref, i):
    mid = ref[i]
    total = ref[i - 1] + ref[i + 1]
    total = total + (roll_xy(mid, 1, 0) + roll_xy(mid, -1, 0))
    return total + (roll_xy(mid, 0, 1) + roll_xy(mid, 0, -1))


def edge_state(sx, gx, mx, cx, sm, cf, i):
    conc = gx[0, i]
    for j in range(1, NG):
        conc = conc + gx[j, i]
    cx[i] = conc
    solid = sx[i] > 0.5
    sm[i] = jnp.where(solid, mx[i], 0.0)
    cf[i] = jnp.where(solid, 0.0, conc)


def collide_plane(fx, gx, sx, cx, sm, fs, gs, i):
    solid = sx[i] > 0.5
    f = [fx[q, i] for q in range(NF)]
    density = f[0]
    for q in range(1, NF):
        density = density + f[q]
    moments = []
    for axis in range(3):
        total = None
        for q, vel in enumerate(flow_vel):
            if vel[axis] == 0:
                continue
            term = f[q] if vel[axis] > 0 else -f[q]
            total = term if total is None else total + term
        moments.append(total)
    inv = 1.0 / density
    comps = [m * inv for m in moments]
    base = 1.0 - 1.5 * (comps[0] * comps[0] + comps[1] * comps[1] + comps[2] * comps[2])
    keep = 1.0 - 1.0 / relax_flow
    scaled = {}
    for w in set(flow_weight):
        scaled[w] = (w / relax_flow) * density

    def along(vel):
        total = None
        for axis in range(3):
            if vel[axis] == 0:
                continue
            term = comps[axis] if vel[axis] > 0 else -comps[axis]
            total = term if total is None else total + term
        return total

    done = set()
    for q, vel in enumerate(flow_vel):
        if q in done:
            continue
        opp = flow_vel.index(tuple(-c for c in vel))
        done |= {q, opp}
        weight = scaled[flow_weight[q]]
        if opp == q:
            fs[q, i] = jnp.where(solid, f[q], keep * f[q] + weight * base)
            continue
        cu = along(vel)
        even = base + 4.5 * (cu * cu)
        odd = 3.0 * cu
        if vel[2]:
            odd = odd + 3.0 * body_force * relax_flow * vel[2]
        for member, poly in ((q, even + odd), (opp, even - odd)):
            fs[member, i] = jnp.where(solid, f[member], keep * f[member] + weight * poly)
    conc = cx[i]
    sink = (react_rate * conc) * face_sum(sm, i)
    rate = 1.0 / relax_acid
    shared = rate * conc - sink
    slope = (4.0 * rate) * conc
    done = set()
    for j, vel in enumerate(acid_vel):
        if j in done:
            continue
        opp = acid_vel.index(tuple(-c for c in vel))
        done |= {j, opp}
        if opp == j:
            parts = ((j, shared),)
        else:
            cu = slope * along(vel)
            parts = ((j, shared + cu), (opp, shared - cu))
        for member, inner in parts:
            g = gx[member, i]
            relaxed = acid_weight[member] * inner - (rate - 1.0) * g
            gs[member, i] = jnp.where(solid, g, relaxed)


def dissolve_plane(sx, mx_src, cf, mx_dst, i):
    solid = sx[i] > 0.5
    mineral = mx_src[i]
    loss = (dissolve_rate * react_rate) * mineral * face_sum(cf, i)
    mx_dst[i] = jnp.where(solid, mineral - loss, mineral)


SHIFTS = [(cx, cy) for cx in (-1, 0, 1) for cy in (-1, 0, 1) if cx or cy]


def shift_masks(sx, bm, i):
    for c, (cx, cy) in enumerate(SHIFTS):
        bm[c, i] = roll_xy(sx[i], cx, cy)


def stream_plane(fs, gs, sx, fdst, gdst, i, bm=None):
    solid = sx[i] > 0.5
    masks = {}
    for q, vel in enumerate(flow_vel):
        cx, cy, cz = vel
        if vel == (0, 0, 0):
            fdst[q, i] = fs[q, i]
            continue
        opp = flow_vel.index((-cx, -cy, -cz))
        src = i - cz
        pulled = roll_xy(fs[q, src], cx, cy)
        if bm is None or (cx, cy) == (0, 0):
            blocked = roll_xy(sx[src], cx, cy) > 0.5
        else:
            blocked = bm[SHIFTS.index((cx, cy)), src] > 0.5
        masks[vel] = blocked
        arrived = jnp.where(blocked, fs[opp, i], pulled)
        fdst[q, i] = jnp.where(solid, fs[q, i], arrived)
    for j, vel in enumerate(acid_vel):
        cx, cy, cz = vel
        if vel == (0, 0, 0):
            gdst[j, i] = gs[j, i]
            continue
        opp = acid_vel.index((-cx, -cy, -cz))
        pulled = roll_xy(gs[j, i - cz], cx, cy)
        arrived = jnp.where(masks[vel], gs[opp, i], pulled)
        gdst[j, i] = jnp.where(solid, gs[j, i], arrived)


def loop(lo, hi, fn):
    def body(i, carry):
        fn(i)
        return carry

    lax.fori_loop(lo, hi, body, 0, unroll=2 if hi - lo > 4 else 1)


UP_Q = [q for q, vel in enumerate(flow_vel) if vel[2] == 1]
DOWN_Q = [q for q, vel in enumerate(flow_vel) if vel[2] == -1]
UP_J = acid_vel.index((0, 0, 1))
DOWN_J = acid_vel.index((0, 0, -1))
NFLUX = 3 + 2 * (len(UP_Q) + 1) + 2


def flux_kernel(pop, sol, mnr, sld, up, down, fs, gs, f1, g1, m1, sx, cx, sm, cf):
    planes = sld.shape[0]
    hi, lo = planes - HALO - 1, HALO
    sx[...] = sld[...].astype(jnp.float32)
    loop(lo - 2, hi + 3, lambda i: edge_state(sx, sol, mnr, cx, sm, cf, i))

    def step1(i):
        dissolve_plane(sx, mnr, cf, m1, i)
        collide_plane(pop, sol, sx, cx, sm, fs, gs, i)

    loop(lo - 1, hi + 2, step1)
    for dst, i, qs, j in ((up, hi, UP_Q, UP_J), (down, lo, DOWN_Q, DOWN_J)):
        dst[0] = sx[i]
        dst[1] = sm[i]
        dst[2] = cf[i]
        for n, q in enumerate(qs):
            dst[3 + n] = fs[q, i]
        dst[3 + len(qs)] = gs[j, i]
    loop(lo, hi + 1, lambda i: stream_plane(fs, gs, sx, f1, g1, i))
    for i in range(lo - 1, hi + 2):
        sm[i] = jnp.where(sx[i] > 0.5, m1[i], 0.0)
    for i in range(lo, hi + 1):
        conc = g1[0, i]
        for j in range(1, NG):
            conc = conc + g1[j, i]
        cx[i] = conc
        cf[i] = jnp.where(sx[i] > 0.5, 0.0, conc)
    loop(lo, hi + 1, lambda i: collide_plane(f1, g1, sx, cx, sm, fs, gs, i))
    base = 4 + len(UP_Q)
    for dst, i, qs, j in ((up, hi, UP_Q, UP_J), (down, lo, DOWN_Q, DOWN_J)):
        dst[base] = sm[i]
        dst[base + 1] = cf[i]
        for n, q in enumerate(qs):
            dst[base + 2 + n] = fs[q, i]
        dst[base + 2 + len(qs)] = gs[j, i]
    up[NFLUX:NFLUX + HALO] = sx[planes - HALO:planes]
    down[NFLUX:NFLUX + HALO] = sx[0:HALO]


def set_bounds(flo, fhi, sm, cf, fs, gs, last, base):
    sm[0] = flo[base]
    cf[0] = flo[base + 1]
    sm[last] = fhi[base]
    cf[last] = fhi[base + 1]

    def posts():
        for n, q in enumerate(UP_Q):
            fs[q, 0] = flo[base + 2 + n]
        gs[UP_J, 0] = flo[base + 2 + len(UP_Q)]
        for n, q in enumerate(DOWN_Q):
            fs[q, last] = fhi[base + 2 + n]
        gs[DOWN_J, last] = fhi[base + 2 + len(DOWN_Q)]

    return posts


def main_kernel(
    mv, pop, sol, mnr, sld, hlo, hhi, flo, fhi,
    out_f, out_g, out_m, out_s,
    fx, gx, fs, gs, mx, m1, sx, si, cx, sm, cf, zf, zi, bm, sem, osem, zsem,
):
    planes = sld.shape[0]
    cap = out_s.shape[0]
    last = planes + 2 * HALO + 1
    own = HALO + 1
    top = own + planes
    fill = [
        (pop, fx.at[:, own:top]),
        (sol, gx.at[:, own:top]),
        (mnr, mx.at[own:top]),
        (hlo.at[0:NF], fx.at[:, 1:own]),
        (hlo.at[NF:NF + NG], gx.at[:, 1:own]),
        (hlo.at[NF + NG], mx.at[1:own]),
        (hhi.at[0:NF], fx.at[:, top:last]),
        (hhi.at[NF:NF + NG], gx.at[:, top:last]),
        (hhi.at[NF + NG], mx.at[top:last]),
    ]
    copies = [pltpu.make_async_copy(s, d, sem.at[k]) for k, (s, d) in enumerate(fill)]
    for c in copies:
        c.start()
    sx[own:top] = sld[...].astype(jnp.float32)
    si[own:top] = sld[...]
    sx[0] = flo[0]
    sx[last] = fhi[0]
    sx[1:own] = flo[NFLUX:NFLUX + HALO]
    sx[top:last] = fhi[NFLUX:NFLUX + HALO]
    zf[...] = jnp.zeros(zf.shape, zf.dtype)
    zi[...] = jnp.zeros(zi.shape, zi.dtype)
    for c in copies[1:]:
        c.wait()
    si[1:own] = (sx[1:own] > 0.5).astype(jnp.int32)
    si[top:last] = (sx[top:last] > 0.5).astype(jnp.int32)

    from_low, send_low, send_high, from_high = mv[0], mv[1], mv[2], mv[3]
    valid_end = from_low + planes - send_low - send_high + from_high

    def plane_valid(i):
        p = i - own
        low = (p >= -from_low) & (p < 0)
        kept = (p >= send_low) & (p < planes - send_high)
        high = (p >= planes) & (p < planes + from_high)
        return low | kept | high

    def plane_copies(i):
        p = i - own
        s = p + from_low - jnp.where(p >= send_low, send_low, 0) - jnp.where(p >= planes, send_high, 0)
        s = jnp.clip(s, 0, cap - 1)
        srcs = (fx.at[:, i], gx.at[:, i], mx.at[i], si.at[i])
        dsts = (out_f.at[:, s], out_g.at[:, s], out_m.at[s], out_s.at[s])
        return [pltpu.make_async_copy(x, y, osem.at[i, k]) for k, (x, y) in enumerate(zip(srcs, dsts))]

    def zero_copies(s):
        srcs = (zf, zf.at[0:NG], zf.at[0], zi)
        dsts = (out_f.at[:, s], out_g.at[:, s], out_m.at[s], out_s.at[s])
        return [pltpu.make_async_copy(x, y, zsem.at[s, k]) for k, (x, y) in enumerate(zip(srcs, dsts))]

    for s in range(cap):
        @pl.when(s >= valid_end)
        def _():
            for c in zero_copies(s):
                c.start()

    loop(0, last + 1, lambda i: shift_masks(sx, bm, i))

    posts = set_bounds(flo, fhi, sm, cf, fs, gs, last, 1)
    loop(1, last, lambda i: edge_state(sx, gx, mx, cx, sm, cf, i))
    copies[0].wait()

    posts()

    def collide1(i):
        dissolve_plane(sx, mx, cf, m1, i)
        collide_plane(fx, gx, sx, cx, sm, fs, gs, i)

    def step1(i):
        collide1(i)
        stream_plane(fs, gs, sx, fx, gx, i - 1, bm)
        edge_state(sx, gx, m1, cx, sm, cf, i - 1)

    collide1(1)
    loop(2, last, step1)
    stream_plane(fs, gs, sx, fx, gx, last - 1, bm)
    edge_state(sx, gx, m1, cx, sm, cf, last - 1)

    posts = set_bounds(flo, fhi, sm, cf, fs, gs, last, 4 + len(UP_Q))

    posts()

    def send_plane(i):
        @pl.when(plane_valid(i))
        def _():
            for c in plane_copies(i):
                c.start()

    def collide2(i):
        dissolve_plane(sx, m1, cf, mx, i)
        collide_plane(fx, gx, sx, cx, sm, fs, gs, i)

    def step2(i):
        collide2(i)
        stream_plane(fs, gs, sx, fx, gx, i - 1, bm)

        @pl.when(i > 2)
        def _():
            send_plane(i - 2)

    collide2(1)
    loop(2, last, step2)
    stream_plane(fs, gs, sx, fx, gx, last - 1, bm)
    send_plane(last - 2)
    send_plane(last - 1)
    for i in range(1, last):
        @pl.when(plane_valid(i))
        def _():
            for c in plane_copies(i):
                c.wait()
    for s in range(cap):
        @pl.when(s >= valid_end)
        def _():
            for c in zero_copies(s):
                c.wait()


def edge_kernel(lo, pop, sol, mnr, out, buf_f, buf_g, buf_m, sem):
    cuts = (0, 7, 13, NF)
    srcs = [pop.at[a:b, lo:lo + HALO] for a, b in zip(cuts[:-1], cuts[1:])]
    bufs = [buf_f.at[a:b] for a, b in zip(cuts[:-1], cuts[1:])]
    dsts = [out.at[a:b] for a, b in zip(cuts[:-1], cuts[1:])]
    srcs += [sol.at[:, lo:lo + HALO], mnr.at[lo:lo + HALO]]
    bufs += [buf_g, buf_m]
    dsts += [out.at[NF:NF + NG], out.at[NF + NG]]
    reads = [pltpu.make_async_copy(s, b, sem.at[0, k]) for k, (s, b) in enumerate(zip(srcs, bufs))]
    writes = [pltpu.make_async_copy(b, d, sem.at[1, k]) for k, (b, d) in enumerate(zip(bufs, dsts))]
    for c in reads:
        c.start()
    for r, w in zip(reads, writes):
        r.wait()
        w.start()
    for w in writes:
        w.wait()


def shards(populations, solute, mineral, solid, plane_moves):
    planes = populations.shape[1]
    cap = planes + 2 * MOVE_MOST
    ext = planes + 2 * HALO + 2
    count = lax.axis_size("blk")
    forward = [(i, (i + 1) % count) for i in range(count)]
    backward = [(i, (i - 1) % count) for i in range(count)]

    plane = populations.shape[2:]
    f32 = jnp.float32
    any_spec = pl.BlockSpec(memory_space=pl.ANY)
    vmem = pl.BlockSpec(memory_space=pltpu.VMEM)
    smem = pl.BlockSpec(memory_space=pltpu.SMEM)

    def edge(lo):
        return pl.pallas_call(
            functools.partial(edge_kernel, lo),
            out_shape=jax.ShapeDtypeStruct((NF + NG + 1, HALO) + plane, f32),
            in_specs=[any_spec, any_spec, any_spec],
            out_specs=any_spec,
            scratch_shapes=[
                pltpu.VMEM((NF, HALO) + plane, f32),
                pltpu.VMEM((NG, HALO) + plane, f32),
                pltpu.VMEM((HALO,) + plane, f32),
                pltpu.SemaphoreType.DMA((2, 5)),
            ],
        )(populations, solute, mineral)

    halo_lo = lax.ppermute(edge(planes - HALO), "blk", forward)
    halo_hi = lax.ppermute(edge(0), "blk", backward)

    up, down = pl.pallas_call(
        flux_kernel,
        out_shape=(
            jax.ShapeDtypeStruct((NFLUX + HALO,) + plane, f32),
            jax.ShapeDtypeStruct((NFLUX + HALO,) + plane, f32),
        ),
        in_specs=[vmem] * 4,
        out_specs=[vmem] * 2,
        scratch_shapes=[
            pltpu.VMEM((NF, planes) + plane, f32),
            pltpu.VMEM((NG, planes) + plane, f32),
            pltpu.VMEM((NF, planes) + plane, f32),
            pltpu.VMEM((NG, planes) + plane, f32),
        ]
        + [pltpu.VMEM((planes,) + plane, f32)] * 5,
    )(populations, solute, mineral, solid)
    flux_lo = lax.ppermute(up, "blk", forward)
    flux_hi = lax.ppermute(down, "blk", backward)

    me = lax.axis_index("blk")
    from_low = plane_moves[jnp.mod(me - 1, count), 1]
    send_low = plane_moves[me, 0]
    send_high = plane_moves[me, 1]
    from_high = plane_moves[jnp.mod(me + 1, count), 0]
    mv = jnp.stack([from_low, send_low, send_high, from_high]).astype(jnp.int32)

    return pl.pallas_call(
        main_kernel,
        out_shape=(
            jax.ShapeDtypeStruct((NF, cap) + plane, f32),
            jax.ShapeDtypeStruct((NG, cap) + plane, f32),
            jax.ShapeDtypeStruct((cap,) + plane, f32),
            jax.ShapeDtypeStruct((cap,) + plane, jnp.int32),
        ),
        in_specs=[smem, any_spec, any_spec, any_spec, vmem, any_spec, any_spec, vmem, vmem],
        out_specs=[any_spec] * 4,
        scratch_shapes=[
            pltpu.VMEM((NF, ext) + plane, f32),
            pltpu.VMEM((NG, ext) + plane, f32),
            pltpu.VMEM((NF, ext) + plane, f32),
            pltpu.VMEM((NG, ext) + plane, f32),
            pltpu.VMEM((ext,) + plane, f32),
            pltpu.VMEM((ext,) + plane, f32),
            pltpu.VMEM((ext,) + plane, f32),
            pltpu.VMEM((ext,) + plane, jnp.int32),
            pltpu.VMEM((ext,) + plane, f32),
            pltpu.VMEM((ext,) + plane, f32),
            pltpu.VMEM((ext,) + plane, f32),
            pltpu.VMEM((NF,) + plane, f32),
            pltpu.VMEM(plane, jnp.int32),
            pltpu.VMEM((len(SHIFTS), ext) + plane, f32),
            pltpu.SemaphoreType.DMA((9,)),
            pltpu.SemaphoreType.DMA((ext, 4)),
            pltpu.SemaphoreType.DMA((cap, 4)),
        ],
        compiler_params=pltpu.CompilerParams(vmem_limit_bytes=50 * 1024 * 1024),
    )(mv, populations, solute, mineral, solid, halo_lo, halo_hi, flux_lo, flux_hi)


def solution(mesh):
    return jax.shard_map(
        shards,
        mesh=mesh,
        in_specs=(
            P(None, "blk", None, None),
            P(None, "blk", None, None),
            P("blk", None, None),
            P("blk", None, None),
            P(),
        ),
        out_specs=(
            P(None, "blk", None, None),
            P(None, "blk", None, None),
            P("blk", None, None),
            P("blk", None, None),
        ),
        check_vma=False,
    )
```

```python
import functools

import jax
import jax.numpy as jnp
from jax import lax
from jax.experimental import pallas as pl
from jax.experimental.pallas import tpu as pltpu
from jax.sharding import PartitionSpec as P

MOVE_MOST = 3
HALO = 3

flow_vel = [
    (0, 0, 1),
    (1, 0, 1),
    (-1, 0, 1),
    (0, 1, 1),
    (0, -1, 1),
    (0, 0, -1),
    (1, 0, -1),
    (-1, 0, -1),
    (0, 1, -1),
    (0, -1, -1),
    (0, 0, 0),
    (1, 0, 0),
    (-1, 0, 0),
    (0, 1, 0),
    (0, -1, 0),
    (1, 1, 0),
    (-1, -1, 0),
    (1, -1, 0),
    (-1, 1, 0),
]
flow_weight = [
    1.0 / 18,
    1.0 / 36,
    1.0 / 36,
    1.0 / 36,
    1.0 / 36,
    1.0 / 18,
    1.0 / 36,
    1.0 / 36,
    1.0 / 36,
    1.0 / 36,
    1.0 / 3,
    1.0 / 18,
    1.0 / 18,
    1.0 / 18,
    1.0 / 18,
    1.0 / 36,
    1.0 / 36,
    1.0 / 36,
    1.0 / 36,
]
acid_vel = [(0, 0, 1), (0, 0, -1), (0, 0, 0), (1, 0, 0), (-1, 0, 0), (0, 1, 0), (0, -1, 0)]
acid_weight = [0.125, 0.125, 0.25, 0.125, 0.125, 0.125, 0.125]
relax_flow = 1.25
relax_acid = 0.8
body_force = 0.001
react_rate = 0.1
dissolve_rate = 0.5

NF = len(flow_vel)
NG = len(acid_vel)


def roll_xy(a, cx, cy):
    if cx:
        a = pltpu.roll(a, cx % a.shape[0], 0)
    if cy:
        a = pltpu.roll(a, cy % a.shape[1], 1)
    return a


def face_sum(ref, i):
    mid = ref[i]
    total = ref[i - 1] + ref[i + 1]
    total = total + (roll_xy(mid, 1, 0) + roll_xy(mid, -1, 0))
    return total + (roll_xy(mid, 0, 1) + roll_xy(mid, 0, -1))


def edge_state(sx, gx, mx, cx, sm, cf, i):
    conc = gx[0, i]
    for j in range(1, NG):
        conc = conc + gx[j, i]
    cx[i] = conc
    solid = sx[i] > 0.5
    sm[i] = jnp.where(solid, mx[i], 0.0)
    cf[i] = jnp.where(solid, 0.0, conc)


def collide_plane(fx, gx, sx, cx, sm, fs, gs, i):
    solid = sx[i] > 0.5
    f = [fx[q, i] for q in range(NF)]
    density = f[0]
    for q in range(1, NF):
        density = density + f[q]
    moments = []
    for axis in range(3):
        total = None
        for q, vel in enumerate(flow_vel):
            if vel[axis] == 0:
                continue
            term = f[q] if vel[axis] > 0 else -f[q]
            total = term if total is None else total + term
        moments.append(total)
    inv = 1.0 / density
    comps = [m * inv for m in moments]
    base = 1.0 - 1.5 * (comps[0] * comps[0] + comps[1] * comps[1] + comps[2] * comps[2])
    keep = 1.0 - 1.0 / relax_flow
    scaled = {}
    for w in set(flow_weight):
        scaled[w] = (w / relax_flow) * density

    def along(vel):
        total = None
        for axis in range(3):
            if vel[axis] == 0:
                continue
            term = comps[axis] if vel[axis] > 0 else -comps[axis]
            total = term if total is None else total + term
        return total

    done = set()
    for q, vel in enumerate(flow_vel):
        if q in done:
            continue
        opp = flow_vel.index(tuple(-c for c in vel))
        done |= {q, opp}
        weight = scaled[flow_weight[q]]
        if opp == q:
            fs[q, i] = jnp.where(solid, f[q], keep * f[q] + weight * base)
            continue
        cu = along(vel)
        even = base + 4.5 * (cu * cu)
        odd = 3.0 * cu
        if vel[2]:
            odd = odd + 3.0 * body_force * relax_flow * vel[2]
        for member, poly in ((q, even + odd), (opp, even - odd)):
            fs[member, i] = jnp.where(solid, f[member], keep * f[member] + weight * poly)
    conc = cx[i]
    sink = (react_rate * conc) * face_sum(sm, i)
    rate = 1.0 / relax_acid
    shared = rate * conc - sink
    slope = (4.0 * rate) * conc
    done = set()
    for j, vel in enumerate(acid_vel):
        if j in done:
            continue
        opp = acid_vel.index(tuple(-c for c in vel))
        done |= {j, opp}
        if opp == j:
            parts = ((j, shared),)
        else:
            cu = slope * along(vel)
            parts = ((j, shared + cu), (opp, shared - cu))
        for member, inner in parts:
            g = gx[member, i]
            relaxed = acid_weight[member] * inner - (rate - 1.0) * g
            gs[member, i] = jnp.where(solid, g, relaxed)


def dissolve_plane(sx, mx_src, cf, mx_dst, i):
    solid = sx[i] > 0.5
    mineral = mx_src[i]
    loss = (dissolve_rate * react_rate) * mineral * face_sum(cf, i)
    mx_dst[i] = jnp.where(solid, mineral - loss, mineral)


SHIFTS = [(cx, cy) for cx in (-1, 0, 1) for cy in (-1, 0, 1) if cx or cy]


def shift_masks(sx, bm, i):
    for c, (cx, cy) in enumerate(SHIFTS):
        bm[c, i] = roll_xy(sx[i], cx, cy)


def stream_plane(fs, gs, sx, fdst, gdst, i, bm=None):
    solid = sx[i] > 0.5
    masks = {}
    for q, vel in enumerate(flow_vel):
        cx, cy, cz = vel
        if vel == (0, 0, 0):
            fdst[q, i] = fs[q, i]
            continue
        opp = flow_vel.index((-cx, -cy, -cz))
        src = i - cz
        pulled = roll_xy(fs[q, src], cx, cy)
        if bm is None or (cx, cy) == (0, 0):
            blocked = roll_xy(sx[src], cx, cy) > 0.5
        else:
            blocked = bm[SHIFTS.index((cx, cy)), src] > 0.5
        masks[vel] = blocked
        arrived = jnp.where(blocked, fs[opp, i], pulled)
        fdst[q, i] = jnp.where(solid, fs[q, i], arrived)
    for j, vel in enumerate(acid_vel):
        cx, cy, cz = vel
        if vel == (0, 0, 0):
            gdst[j, i] = gs[j, i]
            continue
        opp = acid_vel.index((-cx, -cy, -cz))
        pulled = roll_xy(gs[j, i - cz], cx, cy)
        arrived = jnp.where(masks[vel], gs[opp, i], pulled)
        gdst[j, i] = jnp.where(solid, gs[j, i], arrived)


def loop(lo, hi, fn):
    def body(i, carry):
        fn(i)
        return carry

    lax.fori_loop(lo, hi, body, 0, unroll=2 if hi - lo > 4 else 1)


UP_Q = [q for q, vel in enumerate(flow_vel) if vel[2] == 1]
DOWN_Q = [q for q, vel in enumerate(flow_vel) if vel[2] == -1]
UP_J = acid_vel.index((0, 0, 1))
DOWN_J = acid_vel.index((0, 0, -1))
NFLUX = 3 + 2 * (len(UP_Q) + 1) + 2


def flux_kernel(pop, sol, mnr, sld, up, down, fs, gs, f1, g1, m1, sx, cx, sm, cf):
    planes = sld.shape[0]
    hi, lo = planes - HALO - 1, HALO
    sx[...] = sld[...].astype(jnp.float32)
    loop(lo - 2, hi + 3, lambda i: edge_state(sx, sol, mnr, cx, sm, cf, i))

    def step1(i):
        dissolve_plane(sx, mnr, cf, m1, i)
        collide_plane(pop, sol, sx, cx, sm, fs, gs, i)

    loop(lo - 1, hi + 2, step1)
    for dst, i, qs, j in ((up, hi, UP_Q, UP_J), (down, lo, DOWN_Q, DOWN_J)):
        dst[0] = sx[i]
        dst[1] = sm[i]
        dst[2] = cf[i]
        for n, q in enumerate(qs):
            dst[3 + n] = fs[q, i]
        dst[3 + len(qs)] = gs[j, i]
    loop(lo, hi + 1, lambda i: stream_plane(fs, gs, sx, f1, g1, i))
    for i in range(lo - 1, hi + 2):
        sm[i] = jnp.where(sx[i] > 0.5, m1[i], 0.0)
    for i in range(lo, hi + 1):
        conc = g1[0, i]
        for j in range(1, NG):
            conc = conc + g1[j, i]
        cx[i] = conc
        cf[i] = jnp.where(sx[i] > 0.5, 0.0, conc)
    loop(lo, hi + 1, lambda i: collide_plane(f1, g1, sx, cx, sm, fs, gs, i))
    base = 4 + len(UP_Q)
    for dst, i, qs, j in ((up, hi, UP_Q, UP_J), (down, lo, DOWN_Q, DOWN_J)):
        dst[base] = sm[i]
        dst[base + 1] = cf[i]
        for n, q in enumerate(qs):
            dst[base + 2 + n] = fs[q, i]
        dst[base + 2 + len(qs)] = gs[j, i]
    up[NFLUX:NFLUX + HALO] = sx[planes - HALO:planes]
    down[NFLUX:NFLUX + HALO] = sx[0:HALO]


def set_bounds(flo, fhi, sm, cf, fs, gs, last, base):
    sm[0] = flo[base]
    cf[0] = flo[base + 1]
    sm[last] = fhi[base]
    cf[last] = fhi[base + 1]

    def posts():
        for n, q in enumerate(UP_Q):
            fs[q, 0] = flo[base + 2 + n]
        gs[UP_J, 0] = flo[base + 2 + len(UP_Q)]
        for n, q in enumerate(DOWN_Q):
            fs[q, last] = fhi[base + 2 + n]
        gs[DOWN_J, last] = fhi[base + 2 + len(DOWN_Q)]

    return posts


def main_kernel(
    mv, pop, sol, mnr, sld, hlo, hhi, flo, fhi,
    out_f, out_g, out_m, out_s,
    fx, gx, fs, gs, mx, m1, sx, si, cx, sm, cf, zf, zi, bm, sem, osem, zsem,
):
    planes = sld.shape[0]
    cap = out_s.shape[0]
    last = planes + 2 * HALO + 1
    own = HALO + 1
    top = own + planes
    fill = [
        (pop, fx.at[:, own:top]),
        (sol, gx.at[:, own:top]),
        (mnr, mx.at[own:top]),
        (hlo.at[0:NF], fx.at[:, 1:own]),
        (hlo.at[NF:NF + NG], gx.at[:, 1:own]),
        (hlo.at[NF + NG], mx.at[1:own]),
        (hhi.at[0:NF], fx.at[:, top:last]),
        (hhi.at[NF:NF + NG], gx.at[:, top:last]),
        (hhi.at[NF + NG], mx.at[top:last]),
    ]
    copies = [pltpu.make_async_copy(s, d, sem.at[k]) for k, (s, d) in enumerate(fill)]
    for c in copies:
        c.start()
    sx[own:top] = sld[...].astype(jnp.float32)
    si[own:top] = sld[...]
    sx[0] = flo[0]
    sx[last] = fhi[0]
    sx[1:own] = flo[NFLUX:NFLUX + HALO]
    sx[top:last] = fhi[NFLUX:NFLUX + HALO]
    zf[...] = jnp.zeros(zf.shape, zf.dtype)
    zi[...] = jnp.zeros(zi.shape, zi.dtype)
    for c in copies[1:]:
        c.wait()
    si[1:own] = (sx[1:own] > 0.5).astype(jnp.int32)
    si[top:last] = (sx[top:last] > 0.5).astype(jnp.int32)

    from_low, send_low, send_high, from_high = mv[0], mv[1], mv[2], mv[3]
    valid_end = from_low + planes - send_low - send_high + from_high

    def plane_valid(i):
        p = i - own
        low = (p >= -from_low) & (p < 0)
        kept = (p >= send_low) & (p < planes - send_high)
        high = (p >= planes) & (p < planes + from_high)
        return low | kept | high

    def plane_copies(i):
        p = i - own
        s = p + from_low - jnp.where(p >= send_low, send_low, 0) - jnp.where(p >= planes, send_high, 0)
        s = jnp.clip(s, 0, cap - 1)
        srcs = (fx.at[:, i], gx.at[:, i], mx.at[i], si.at[i])
        dsts = (out_f.at[:, s], out_g.at[:, s], out_m.at[s], out_s.at[s])
        return [pltpu.make_async_copy(x, y, osem.at[i, k]) for k, (x, y) in enumerate(zip(srcs, dsts))]

    def zero_copies(s):
        srcs = (zf, zf.at[0:NG], zf.at[0], zi)
        dsts = (out_f.at[:, s], out_g.at[:, s], out_m.at[s], out_s.at[s])
        return [pltpu.make_async_copy(x, y, zsem.at[s, k]) for k, (x, y) in enumerate(zip(srcs, dsts))]

    for s in range(cap):
        @pl.when(s >= valid_end)
        def _():
            for c in zero_copies(s):
                c.start()

    loop(0, last + 1, lambda i: shift_masks(sx, bm, i))

    posts = set_bounds(flo, fhi, sm, cf, fs, gs, last, 1)
    loop(1, last, lambda i: edge_state(sx, gx, mx, cx, sm, cf, i))
    copies[0].wait()

    posts()

    def collide1(i):
        dissolve_plane(sx, mx, cf, m1, i)
        collide_plane(fx, gx, sx, cx, sm, fs, gs, i)

    def step1(i):
        collide1(i)
        stream_plane(fs, gs, sx, fx, gx, i - 1, bm)
        edge_state(sx, gx, m1, cx, sm, cf, i - 1)

    collide1(1)
    loop(2, last, step1)
    stream_plane(fs, gs, sx, fx, gx, last - 1, bm)
    edge_state(sx, gx, m1, cx, sm, cf, last - 1)

    posts = set_bounds(flo, fhi, sm, cf, fs, gs, last, 4 + len(UP_Q))

    posts()

    def send_plane(i):
        @pl.when(plane_valid(i))
        def _():
            for c in plane_copies(i):
                c.start()

    def collide2(i):
        dissolve_plane(sx, m1, cf, mx, i)
        collide_plane(fx, gx, sx, cx, sm, fs, gs, i)

    def step2(i):
        collide2(i)
        stream_plane(fs, gs, sx, fx, gx, i - 1, bm)

        @pl.when(i > 2)
        def _():
            send_plane(i - 2)

    collide2(1)
    loop(2, last, step2)
    stream_plane(fs, gs, sx, fx, gx, last - 1, bm)
    send_plane(last - 2)
    send_plane(last - 1)
    for i in range(1, last):
        @pl.when(plane_valid(i))
        def _():
            for c in plane_copies(i):
                c.wait()
    for s in range(cap):
        @pl.when(s >= valid_end)
        def _():
            for c in zero_copies(s):
                c.wait()


def edge_kernel(lo, pop, sol, mnr, out, buf_f, buf_g, buf_m, sem):
    cuts = (0, 3, 7, 11, 15, NF)
    srcs = [pop.at[a:b, lo:lo + HALO] for a, b in zip(cuts[:-1], cuts[1:])]
    bufs = [buf_f.at[a:b] for a, b in zip(cuts[:-1], cuts[1:])]
    dsts = [out.at[a:b] for a, b in zip(cuts[:-1], cuts[1:])]
    for a, b in ((0, 4), (4, NG)):
        srcs.append(sol.at[a:b, lo:lo + HALO])
        bufs.append(buf_g.at[a:b])
        dsts.append(out.at[NF + a:NF + b])
    srcs.append(mnr.at[lo:lo + HALO])
    bufs.append(buf_m)
    dsts.append(out.at[NF + NG])
    reads = [pltpu.make_async_copy(s, b, sem.at[0, k]) for k, (s, b) in enumerate(zip(srcs, bufs))]
    writes = [pltpu.make_async_copy(b, d, sem.at[1, k]) for k, (b, d) in enumerate(zip(bufs, dsts))]
    for c in reads:
        c.start()
    for r, w in zip(reads, writes):
        r.wait()
        w.start()
    for w in writes:
        w.wait()


def shards(populations, solute, mineral, solid, plane_moves):
    planes = populations.shape[1]
    cap = planes + 2 * MOVE_MOST
    ext = planes + 2 * HALO + 2
    count = lax.axis_size("blk")
    forward = [(i, (i + 1) % count) for i in range(count)]
    backward = [(i, (i - 1) % count) for i in range(count)]

    plane = populations.shape[2:]
    f32 = jnp.float32
    any_spec = pl.BlockSpec(memory_space=pl.ANY)
    vmem = pl.BlockSpec(memory_space=pltpu.VMEM)
    smem = pl.BlockSpec(memory_space=pltpu.SMEM)

    def edge(lo):
        return pl.pallas_call(
            functools.partial(edge_kernel, lo),
            out_shape=jax.ShapeDtypeStruct((NF + NG + 1, HALO) + plane, f32),
            in_specs=[any_spec, any_spec, any_spec],
            out_specs=any_spec,
            scratch_shapes=[
                pltpu.VMEM((NF, HALO) + plane, f32),
                pltpu.VMEM((NG, HALO) + plane, f32),
                pltpu.VMEM((HALO,) + plane, f32),
                pltpu.SemaphoreType.DMA((2, 8)),
            ],
        )(populations, solute, mineral)

    halo_lo = lax.ppermute(edge(planes - HALO), "blk", forward)
    halo_hi = lax.ppermute(edge(0), "blk", backward)

    up, down = pl.pallas_call(
        flux_kernel,
        out_shape=(
            jax.ShapeDtypeStruct((NFLUX + HALO,) + plane, f32),
            jax.ShapeDtypeStruct((NFLUX + HALO,) + plane, f32),
        ),
        in_specs=[vmem] * 4,
        out_specs=[vmem] * 2,
        scratch_shapes=[
            pltpu.VMEM((NF, planes) + plane, f32),
            pltpu.VMEM((NG, planes) + plane, f32),
            pltpu.VMEM((NF, planes) + plane, f32),
            pltpu.VMEM((NG, planes) + plane, f32),
        ]
        + [pltpu.VMEM((planes,) + plane, f32)] * 5,
    )(populations, solute, mineral, solid)
    flux_lo = lax.ppermute(up, "blk", forward)
    flux_hi = lax.ppermute(down, "blk", backward)

    me = lax.axis_index("blk")
    from_low = plane_moves[jnp.mod(me - 1, count), 1]
    send_low = plane_moves[me, 0]
    send_high = plane_moves[me, 1]
    from_high = plane_moves[jnp.mod(me + 1, count), 0]
    mv = jnp.stack([from_low, send_low, send_high, from_high]).astype(jnp.int32)

    return pl.pallas_call(
        main_kernel,
        out_shape=(
            jax.ShapeDtypeStruct((NF, cap) + plane, f32),
            jax.ShapeDtypeStruct((NG, cap) + plane, f32),
            jax.ShapeDtypeStruct((cap,) + plane, f32),
            jax.ShapeDtypeStruct((cap,) + plane, jnp.int32),
        ),
        in_specs=[smem, any_spec, any_spec, any_spec, vmem, any_spec, any_spec, vmem, vmem],
        out_specs=[any_spec] * 4,
        scratch_shapes=[
            pltpu.VMEM((NF, ext) + plane, f32),
            pltpu.VMEM((NG, ext) + plane, f32),
            pltpu.VMEM((NF, ext) + plane, f32),
            pltpu.VMEM((NG, ext) + plane, f32),
            pltpu.VMEM((ext,) + plane, f32),
            pltpu.VMEM((ext,) + plane, f32),
            pltpu.VMEM((ext,) + plane, f32),
            pltpu.VMEM((ext,) + plane, jnp.int32),
            pltpu.VMEM((ext,) + plane, f32),
            pltpu.VMEM((ext,) + plane, f32),
            pltpu.VMEM((ext,) + plane, f32),
            pltpu.VMEM((NF,) + plane, f32),
            pltpu.VMEM(plane, jnp.int32),
            pltpu.VMEM((len(SHIFTS), ext) + plane, f32),
            pltpu.SemaphoreType.DMA((9,)),
            pltpu.SemaphoreType.DMA((ext, 4)),
            pltpu.SemaphoreType.DMA((cap, 4)),
        ],
        compiler_params=pltpu.CompilerParams(vmem_limit_bytes=50 * 1024 * 1024),
    )(mv, populations, solute, mineral, solid, halo_lo, halo_hi, flux_lo, flux_hi)


def solution(mesh):
    return jax.shard_map(
        shards,
        mesh=mesh,
        in_specs=(
            P(None, "blk", None, None),
            P(None, "blk", None, None),
            P("blk", None, None),
            P("blk", None, None),
            P(),
        ),
        out_specs=(
            P(None, "blk", None, None),
            P(None, "blk", None, None),
            P("blk", None, None),
            P("blk", None, None),
        ),
        check_vma=False,
    )
```

```python
import functools

import jax
import jax.numpy as jnp
from jax import lax
from jax.experimental import pallas as pl
from jax.experimental.pallas import tpu as pltpu
from jax.sharding import PartitionSpec as P

MOVE_MOST = 3
HALO = 3

flow_vel = [
    (0, 0, 1),
    (1, 0, 1),
    (-1, 0, 1),
    (0, 1, 1),
    (0, -1, 1),
    (0, 0, -1),
    (1, 0, -1),
    (-1, 0, -1),
    (0, 1, -1),
    (0, -1, -1),
    (0, 0, 0),
    (1, 0, 0),
    (-1, 0, 0),
    (0, 1, 0),
    (0, -1, 0),
    (1, 1, 0),
    (-1, -1, 0),
    (1, -1, 0),
    (-1, 1, 0),
]
flow_weight = [
    1.0 / 18,
    1.0 / 36,
    1.0 / 36,
    1.0 / 36,
    1.0 / 36,
    1.0 / 18,
    1.0 / 36,
    1.0 / 36,
    1.0 / 36,
    1.0 / 36,
    1.0 / 3,
    1.0 / 18,
    1.0 / 18,
    1.0 / 18,
    1.0 / 18,
    1.0 / 36,
    1.0 / 36,
    1.0 / 36,
    1.0 / 36,
]
acid_vel = [(0, 0, 1), (0, 0, -1), (0, 0, 0), (1, 0, 0), (-1, 0, 0), (0, 1, 0), (0, -1, 0)]
acid_weight = [0.125, 0.125, 0.25, 0.125, 0.125, 0.125, 0.125]
relax_flow = 1.25
relax_acid = 0.8
body_force = 0.001
react_rate = 0.1
dissolve_rate = 0.5

NF = len(flow_vel)
NG = len(acid_vel)


def roll_xy(a, cx, cy):
    if cx:
        a = pltpu.roll(a, cx % a.shape[0], 0)
    if cy:
        a = pltpu.roll(a, cy % a.shape[1], 1)
    return a


def face_sum(ref, i):
    mid = ref[i]
    total = ref[i - 1] + ref[i + 1]
    total = total + (roll_xy(mid, 1, 0) + roll_xy(mid, -1, 0))
    return total + (roll_xy(mid, 0, 1) + roll_xy(mid, 0, -1))


def edge_state(sx, gx, mx, cx, sm, cf, i):
    conc = gx[0, i]
    for j in range(1, NG):
        conc = conc + gx[j, i]
    cx[i] = conc
    solid = sx[i] > 0.5
    sm[i] = jnp.where(solid, mx[i], 0.0)
    cf[i] = jnp.where(solid, 0.0, conc)


def collide_plane(fx, gx, sx, cx, sm, fs, gs, i):
    solid = sx[i] > 0.5
    f = [fx[q, i] for q in range(NF)]
    density = f[0]
    for q in range(1, NF):
        density = density + f[q]
    moments = []
    for axis in range(3):
        total = None
        for q, vel in enumerate(flow_vel):
            if vel[axis] == 0:
                continue
            term = f[q] if vel[axis] > 0 else -f[q]
            total = term if total is None else total + term
        moments.append(total)
    inv = 1.0 / density
    comps = [m * inv for m in moments]
    base = 1.0 - 1.5 * (comps[0] * comps[0] + comps[1] * comps[1] + comps[2] * comps[2])
    keep = 1.0 - 1.0 / relax_flow
    scaled = {}
    for w in set(flow_weight):
        scaled[w] = (w / relax_flow) * density

    def along(vel):
        total = None
        for axis in range(3):
            if vel[axis] == 0:
                continue
            term = comps[axis] if vel[axis] > 0 else -comps[axis]
            total = term if total is None else total + term
        return total

    done = set()
    for q, vel in enumerate(flow_vel):
        if q in done:
            continue
        opp = flow_vel.index(tuple(-c for c in vel))
        done |= {q, opp}
        weight = scaled[flow_weight[q]]
        if opp == q:
            fs[q, i] = jnp.where(solid, f[q], keep * f[q] + weight * base)
            continue
        cu = along(vel)
        even = base + 4.5 * (cu * cu)
        odd = 3.0 * cu
        if vel[2]:
            odd = odd + 3.0 * body_force * relax_flow * vel[2]
        for member, poly in ((q, even + odd), (opp, even - odd)):
            fs[member, i] = jnp.where(solid, f[member], keep * f[member] + weight * poly)
    conc = cx[i]
    sink = (react_rate * conc) * face_sum(sm, i)
    rate = 1.0 / relax_acid
    shared = rate * conc - sink
    slope = (4.0 * rate) * conc
    done = set()
    for j, vel in enumerate(acid_vel):
        if j in done:
            continue
        opp = acid_vel.index(tuple(-c for c in vel))
        done |= {j, opp}
        if opp == j:
            parts = ((j, shared),)
        else:
            cu = slope * along(vel)
            parts = ((j, shared + cu), (opp, shared - cu))
        for member, inner in parts:
            g = gx[member, i]
            relaxed = acid_weight[member] * inner - (rate - 1.0) * g
            gs[member, i] = jnp.where(solid, g, relaxed)


def dissolve_plane(sx, mx_src, cf, mx_dst, i):
    solid = sx[i] > 0.5
    mineral = mx_src[i]
    loss = (dissolve_rate * react_rate) * mineral * face_sum(cf, i)
    mx_dst[i] = jnp.where(solid, mineral - loss, mineral)


SHIFTS = [(cx, cy) for cx in (-1, 0, 1) for cy in (-1, 0, 1) if cx or cy]


def shift_masks(sx, bm, i):
    for c, (cx, cy) in enumerate(SHIFTS):
        bm[c, i] = roll_xy(sx[i], cx, cy)


def stream_plane(fs, gs, sx, fdst, gdst, i, bm=None):
    solid = sx[i] > 0.5
    masks = {}
    for q, vel in enumerate(flow_vel):
        cx, cy, cz = vel
        if vel == (0, 0, 0):
            fdst[q, i] = fs[q, i]
            continue
        opp = flow_vel.index((-cx, -cy, -cz))
        src = i - cz
        pulled = roll_xy(fs[q, src], cx, cy)
        if bm is None or (cx, cy) == (0, 0):
            blocked = roll_xy(sx[src], cx, cy) > 0.5
        else:
            blocked = bm[SHIFTS.index((cx, cy)), src] > 0.5
        masks[vel] = blocked
        arrived = jnp.where(blocked, fs[opp, i], pulled)
        fdst[q, i] = jnp.where(solid, fs[q, i], arrived)
    for j, vel in enumerate(acid_vel):
        cx, cy, cz = vel
        if vel == (0, 0, 0):
            gdst[j, i] = gs[j, i]
            continue
        opp = acid_vel.index((-cx, -cy, -cz))
        pulled = roll_xy(gs[j, i - cz], cx, cy)
        arrived = jnp.where(masks[vel], gs[opp, i], pulled)
        gdst[j, i] = jnp.where(solid, gs[j, i], arrived)


def loop(lo, hi, fn, unroll=None):
    def body(i, carry):
        fn(i)
        return carry

    if unroll is None:
        unroll = 2 if hi - lo > 4 else 1
    lax.fori_loop(lo, hi, body, 0, unroll=unroll)


UP_Q = [q for q, vel in enumerate(flow_vel) if vel[2] == 1]
DOWN_Q = [q for q, vel in enumerate(flow_vel) if vel[2] == -1]
UP_J = acid_vel.index((0, 0, 1))
DOWN_J = acid_vel.index((0, 0, -1))
NFLUX = 3 + 2 * (len(UP_Q) + 1) + 2


def flux_kernel(pop, sol, mnr, sld, up, down, fs, gs, f1, g1, m1, sx, cx, sm, cf):
    planes = sld.shape[0]
    hi, lo = planes - HALO - 1, HALO
    sx[...] = sld[...].astype(jnp.float32)
    loop(lo - 2, hi + 3, lambda i: edge_state(sx, sol, mnr, cx, sm, cf, i))

    def step1(i):
        dissolve_plane(sx, mnr, cf, m1, i)
        collide_plane(pop, sol, sx, cx, sm, fs, gs, i)

    loop(lo - 1, hi + 2, step1)
    for dst, i, qs, j in ((up, hi, UP_Q, UP_J), (down, lo, DOWN_Q, DOWN_J)):
        dst[0] = sx[i]
        dst[1] = sm[i]
        dst[2] = cf[i]
        for n, q in enumerate(qs):
            dst[3 + n] = fs[q, i]
        dst[3 + len(qs)] = gs[j, i]
    loop(lo, hi + 1, lambda i: stream_plane(fs, gs, sx, f1, g1, i))
    for i in range(lo - 1, hi + 2):
        sm[i] = jnp.where(sx[i] > 0.5, m1[i], 0.0)
    for i in range(lo, hi + 1):
        conc = g1[0, i]
        for j in range(1, NG):
            conc = conc + g1[j, i]
        cx[i] = conc
        cf[i] = jnp.where(sx[i] > 0.5, 0.0, conc)
    loop(lo, hi + 1, lambda i: collide_plane(f1, g1, sx, cx, sm, fs, gs, i))
    base = 4 + len(UP_Q)
    for dst, i, qs, j in ((up, hi, UP_Q, UP_J), (down, lo, DOWN_Q, DOWN_J)):
        dst[base] = sm[i]
        dst[base + 1] = cf[i]
        for n, q in enumerate(qs):
            dst[base + 2 + n] = fs[q, i]
        dst[base + 2 + len(qs)] = gs[j, i]
    up[NFLUX:NFLUX + HALO] = sx[planes - HALO:planes]
    down[NFLUX:NFLUX + HALO] = sx[0:HALO]


def set_bounds(flo, fhi, sm, cf, fs, gs, last, base):
    sm[0] = flo[base]
    cf[0] = flo[base + 1]
    sm[last] = fhi[base]
    cf[last] = fhi[base + 1]

    def posts():
        for n, q in enumerate(UP_Q):
            fs[q, 0] = flo[base + 2 + n]
        gs[UP_J, 0] = flo[base + 2 + len(UP_Q)]
        for n, q in enumerate(DOWN_Q):
            fs[q, last] = fhi[base + 2 + n]
        gs[DOWN_J, last] = fhi[base + 2 + len(DOWN_Q)]

    return posts


def main_kernel(
    mv, pop, sol, mnr, sld, hlo, hhi, flo, fhi,
    out_f, out_g, out_m, out_s,
    fx, gx, fs, gs, mx, m1, sx, si, cx, sm, cf, zf, zi, bm, sem, osem, zsem,
):
    planes = sld.shape[0]
    cap = out_s.shape[0]
    last = planes + 2 * HALO + 1
    own = HALO + 1
    top = own + planes
    fill = [
        (pop, fx.at[:, own:top]),
        (sol, gx.at[:, own:top]),
        (mnr, mx.at[own:top]),
        (hlo.at[0:NF], fx.at[:, 1:own]),
        (hlo.at[NF:NF + NG], gx.at[:, 1:own]),
        (hlo.at[NF + NG], mx.at[1:own]),
        (hhi.at[0:NF], fx.at[:, top:last]),
        (hhi.at[NF:NF + NG], gx.at[:, top:last]),
        (hhi.at[NF + NG], mx.at[top:last]),
    ]
    copies = [pltpu.make_async_copy(s, d, sem.at[k]) for k, (s, d) in enumerate(fill)]
    for c in copies:
        c.start()
    sx[own:top] = sld[...].astype(jnp.float32)
    si[own:top] = sld[...]
    sx[0] = flo[0]
    sx[last] = fhi[0]
    sx[1:own] = flo[NFLUX:NFLUX + HALO]
    sx[top:last] = fhi[NFLUX:NFLUX + HALO]
    zf[...] = jnp.zeros(zf.shape, zf.dtype)
    zi[...] = jnp.zeros(zi.shape, zi.dtype)
    for c in copies[1:]:
        c.wait()
    si[1:own] = (sx[1:own] > 0.5).astype(jnp.int32)
    si[top:last] = (sx[top:last] > 0.5).astype(jnp.int32)

    from_low, send_low, send_high, from_high = mv[0], mv[1], mv[2], mv[3]
    valid_end = from_low + planes - send_low - send_high + from_high

    def plane_valid(i):
        p = i - own
        low = (p >= -from_low) & (p < 0)
        kept = (p >= send_low) & (p < planes - send_high)
        high = (p >= planes) & (p < planes + from_high)
        return low | kept | high

    def plane_copies(i):
        p = i - own
        s = p + from_low - jnp.where(p >= send_low, send_low, 0) - jnp.where(p >= planes, send_high, 0)
        s = jnp.clip(s, 0, cap - 1)
        srcs = (fx.at[:, i], gx.at[:, i], mx.at[i], si.at[i])
        dsts = (out_f.at[:, s], out_g.at[:, s], out_m.at[s], out_s.at[s])
        return [pltpu.make_async_copy(x, y, osem.at[i, k]) for k, (x, y) in enumerate(zip(srcs, dsts))]

    def zero_copies(s):
        srcs = (zf, zf.at[0:NG], zf.at[0], zi)
        dsts = (out_f.at[:, s], out_g.at[:, s], out_m.at[s], out_s.at[s])
        return [pltpu.make_async_copy(x, y, zsem.at[s, k]) for k, (x, y) in enumerate(zip(srcs, dsts))]

    for s in range(cap):
        @pl.when(s >= valid_end)
        def _():
            for c in zero_copies(s):
                c.start()

    loop(0, last + 1, lambda i: shift_masks(sx, bm, i))

    posts = set_bounds(flo, fhi, sm, cf, fs, gs, last, 1)
    loop(1, last, lambda i: edge_state(sx, gx, mx, cx, sm, cf, i))
    copies[0].wait()

    posts()

    def collide1(i):
        dissolve_plane(sx, mx, cf, m1, i)
        collide_plane(fx, gx, sx, cx, sm, fs, gs, i)

    def step1(i):
        collide1(i)
        stream_plane(fs, gs, sx, fx, gx, i - 1, bm)
        edge_state(sx, gx, m1, cx, sm, cf, i - 1)

    collide1(1)
    loop(2, last, step1, unroll=1)
    stream_plane(fs, gs, sx, fx, gx, last - 1, bm)
    edge_state(sx, gx, m1, cx, sm, cf, last - 1)

    posts = set_bounds(flo, fhi, sm, cf, fs, gs, last, 4 + len(UP_Q))

    posts()

    def send_plane(i):
        @pl.when(plane_valid(i))
        def _():
            for c in plane_copies(i):
                c.start()

    def collide2(i):
        dissolve_plane(sx, m1, cf, mx, i)
        collide_plane(fx, gx, sx, cx, sm, fs, gs, i)

    def step2(i):
        collide2(i)
        stream_plane(fs, gs, sx, fx, gx, i - 1, bm)

        @pl.when(i > 2)
        def _():
            send_plane(i - 2)

    collide2(1)
    loop(2, last, step2, unroll=1)
    stream_plane(fs, gs, sx, fx, gx, last - 1, bm)
    send_plane(last - 2)
    send_plane(last - 1)
    for i in range(1, last):
        @pl.when(plane_valid(i))
        def _():
            for c in plane_copies(i):
                c.wait()
    for s in range(cap):
        @pl.when(s >= valid_end)
        def _():
            for c in zero_copies(s):
                c.wait()


def edge_kernel(lo, pop, sol, mnr, out, buf_f, buf_g, buf_m, sem):
    cuts = (0, 7, 13, NF)
    srcs = [pop.at[a:b, lo:lo + HALO] for a, b in zip(cuts[:-1], cuts[1:])]
    bufs = [buf_f.at[a:b] for a, b in zip(cuts[:-1], cuts[1:])]
    dsts = [out.at[a:b] for a, b in zip(cuts[:-1], cuts[1:])]
    srcs += [sol.at[:, lo:lo + HALO], mnr.at[lo:lo + HALO]]
    bufs += [buf_g, buf_m]
    dsts += [out.at[NF:NF + NG], out.at[NF + NG]]
    reads = [pltpu.make_async_copy(s, b, sem.at[0, k]) for k, (s, b) in enumerate(zip(srcs, bufs))]
    writes = [pltpu.make_async_copy(b, d, sem.at[1, k]) for k, (b, d) in enumerate(zip(bufs, dsts))]
    for c in reads:
        c.start()
    for r, w in zip(reads, writes):
        r.wait()
        w.start()
    for w in writes:
        w.wait()


def shards(populations, solute, mineral, solid, plane_moves):
    planes = populations.shape[1]
    cap = planes + 2 * MOVE_MOST
    ext = planes + 2 * HALO + 2
    count = lax.axis_size("blk")
    forward = [(i, (i + 1) % count) for i in range(count)]
    backward = [(i, (i - 1) % count) for i in range(count)]

    plane = populations.shape[2:]
    f32 = jnp.float32
    any_spec = pl.BlockSpec(memory_space=pl.ANY)
    vmem = pl.BlockSpec(memory_space=pltpu.VMEM)
    smem = pl.BlockSpec(memory_space=pltpu.SMEM)

    def edge(lo):
        return pl.pallas_call(
            functools.partial(edge_kernel, lo),
            out_shape=jax.ShapeDtypeStruct((NF + NG + 1, HALO) + plane, f32),
            in_specs=[any_spec, any_spec, any_spec],
            out_specs=any_spec,
            scratch_shapes=[
                pltpu.VMEM((NF, HALO) + plane, f32),
                pltpu.VMEM((NG, HALO) + plane, f32),
                pltpu.VMEM((HALO,) + plane, f32),
                pltpu.SemaphoreType.DMA((2, 5)),
            ],
        )(populations, solute, mineral)

    halo_lo = lax.ppermute(edge(planes - HALO), "blk", forward)
    halo_hi = lax.ppermute(edge(0), "blk", backward)

    up, down = pl.pallas_call(
        flux_kernel,
        out_shape=(
            jax.ShapeDtypeStruct((NFLUX + HALO,) + plane, f32),
            jax.ShapeDtypeStruct((NFLUX + HALO,) + plane, f32),
        ),
        in_specs=[vmem] * 4,
        out_specs=[vmem] * 2,
        scratch_shapes=[
            pltpu.VMEM((NF, planes) + plane, f32),
            pltpu.VMEM((NG, planes) + plane, f32),
            pltpu.VMEM((NF, planes) + plane, f32),
            pltpu.VMEM((NG, planes) + plane, f32),
        ]
        + [pltpu.VMEM((planes,) + plane, f32)] * 5,
    )(populations, solute, mineral, solid)
    flux_lo = lax.ppermute(up, "blk", forward)
    flux_hi = lax.ppermute(down, "blk", backward)

    me = lax.axis_index("blk")
    from_low = plane_moves[jnp.mod(me - 1, count), 1]
    send_low = plane_moves[me, 0]
    send_high = plane_moves[me, 1]
    from_high = plane_moves[jnp.mod(me + 1, count), 0]
    mv = jnp.stack([from_low, send_low, send_high, from_high]).astype(jnp.int32)

    return pl.pallas_call(
        main_kernel,
        out_shape=(
            jax.ShapeDtypeStruct((NF, cap) + plane, f32),
            jax.ShapeDtypeStruct((NG, cap) + plane, f32),
            jax.ShapeDtypeStruct((cap,) + plane, f32),
            jax.ShapeDtypeStruct((cap,) + plane, jnp.int32),
        ),
        in_specs=[smem, any_spec, any_spec, any_spec, vmem, any_spec, any_spec, vmem, vmem],
        out_specs=[any_spec] * 4,
        scratch_shapes=[
            pltpu.VMEM((NF, ext) + plane, f32),
            pltpu.VMEM((NG, ext) + plane, f32),
            pltpu.VMEM((NF, ext) + plane, f32),
            pltpu.VMEM((NG, ext) + plane, f32),
            pltpu.VMEM((ext,) + plane, f32),
            pltpu.VMEM((ext,) + plane, f32),
            pltpu.VMEM((ext,) + plane, f32),
            pltpu.VMEM((ext,) + plane, jnp.int32),
            pltpu.VMEM((ext,) + plane, f32),
            pltpu.VMEM((ext,) + plane, f32),
            pltpu.VMEM((ext,) + plane, f32),
            pltpu.VMEM((NF,) + plane, f32),
            pltpu.VMEM(plane, jnp.int32),
            pltpu.VMEM((len(SHIFTS), ext) + plane, f32),
            pltpu.SemaphoreType.DMA((9,)),
            pltpu.SemaphoreType.DMA((ext, 4)),
            pltpu.SemaphoreType.DMA((cap, 4)),
        ],
        compiler_params=pltpu.CompilerParams(vmem_limit_bytes=50 * 1024 * 1024),
    )(mv, populations, solute, mineral, solid, halo_lo, halo_hi, flux_lo, flux_hi)


def solution(mesh):
    return jax.shard_map(
        shards,
        mesh=mesh,
        in_specs=(
            P(None, "blk", None, None),
            P(None, "blk", None, None),
            P("blk", None, None),
            P("blk", None, None),
            P(),
        ),
        out_specs=(
            P(None, "blk", None, None),
            P(None, "blk", None, None),
            P("blk", None, None),
            P("blk", None, None),
        ),
        check_vma=False,
    )
```

```python
import functools

import jax
import jax.numpy as jnp
from jax import lax
from jax.experimental import pallas as pl
from jax.experimental.pallas import tpu as pltpu
from jax.sharding import PartitionSpec as P

MOVE_MOST = 3
HALO = 3

flow_vel = [
    (0, 0, 1),
    (1, 0, 1),
    (-1, 0, 1),
    (0, 1, 1),
    (0, -1, 1),
    (0, 0, -1),
    (1, 0, -1),
    (-1, 0, -1),
    (0, 1, -1),
    (0, -1, -1),
    (0, 0, 0),
    (1, 0, 0),
    (-1, 0, 0),
    (0, 1, 0),
    (0, -1, 0),
    (1, 1, 0),
    (-1, -1, 0),
    (1, -1, 0),
    (-1, 1, 0),
]
flow_weight = [
    1.0 / 18,
    1.0 / 36,
    1.0 / 36,
    1.0 / 36,
    1.0 / 36,
    1.0 / 18,
    1.0 / 36,
    1.0 / 36,
    1.0 / 36,
    1.0 / 36,
    1.0 / 3,
    1.0 / 18,
    1.0 / 18,
    1.0 / 18,
    1.0 / 18,
    1.0 / 36,
    1.0 / 36,
    1.0 / 36,
    1.0 / 36,
]
acid_vel = [(0, 0, 1), (0, 0, -1), (0, 0, 0), (1, 0, 0), (-1, 0, 0), (0, 1, 0), (0, -1, 0)]
acid_weight = [0.125, 0.125, 0.25, 0.125, 0.125, 0.125, 0.125]
relax_flow = 1.25
relax_acid = 0.8
body_force = 0.001
react_rate = 0.1
dissolve_rate = 0.5

NF = len(flow_vel)
NG = len(acid_vel)


def roll_xy(a, cx, cy):
    if cx:
        a = pltpu.roll(a, cx % a.shape[0], 0)
    if cy:
        a = pltpu.roll(a, cy % a.shape[1], 1)
    return a


def face_sum(ref, i):
    mid = ref[i]
    total = ref[i - 1] + ref[i + 1]
    total = total + (roll_xy(mid, 1, 0) + roll_xy(mid, -1, 0))
    return total + (roll_xy(mid, 0, 1) + roll_xy(mid, 0, -1))


def edge_state(sx, gx, mx, cx, sm, cf, i):
    conc = gx[0, i]
    for j in range(1, NG):
        conc = conc + gx[j, i]
    cx[i] = conc
    solid = sx[i] > 0.5
    sm[i] = jnp.where(solid, mx[i], 0.0)
    cf[i] = jnp.where(solid, 0.0, conc)


def collide_plane(fx, gx, sx, cx, sm, fs, gs, i):
    solid = sx[i] > 0.5
    f = [fx[q, i] for q in range(NF)]
    density = f[0]
    for q in range(1, NF):
        density = density + f[q]
    moments = []
    for axis in range(3):
        total = None
        for q, vel in enumerate(flow_vel):
            if vel[axis] == 0:
                continue
            term = f[q] if vel[axis] > 0 else -f[q]
            total = term if total is None else total + term
        moments.append(total)
    inv = 1.0 / density
    comps = [m * inv for m in moments]
    base = 1.0 - 1.5 * (comps[0] * comps[0] + comps[1] * comps[1] + comps[2] * comps[2])
    keep = 1.0 - 1.0 / relax_flow
    scaled = {}
    for w in set(flow_weight):
        scaled[w] = (w / relax_flow) * density

    def along(vel):
        total = None
        for axis in range(3):
            if vel[axis] == 0:
                continue
            term = comps[axis] if vel[axis] > 0 else -comps[axis]
            total = term if total is None else total + term
        return total

    done = set()
    for q, vel in enumerate(flow_vel):
        if q in done:
            continue
        opp = flow_vel.index(tuple(-c for c in vel))
        done |= {q, opp}
        weight = scaled[flow_weight[q]]
        if opp == q:
            fs[q, i] = jnp.where(solid, f[q], keep * f[q] + weight * base)
            continue
        cu = along(vel)
        even = base + 4.5 * (cu * cu)
        odd = 3.0 * cu
        if vel[2]:
            odd = odd + 3.0 * body_force * relax_flow * vel[2]
        for member, poly in ((q, even + odd), (opp, even - odd)):
            fs[member, i] = jnp.where(solid, f[member], keep * f[member] + weight * poly)
    conc = cx[i]
    sink = (react_rate * conc) * face_sum(sm, i)
    rate = 1.0 / relax_acid
    shared = rate * conc - sink
    slope = (4.0 * rate) * conc
    done = set()
    for j, vel in enumerate(acid_vel):
        if j in done:
            continue
        opp = acid_vel.index(tuple(-c for c in vel))
        done |= {j, opp}
        if opp == j:
            parts = ((j, shared),)
        else:
            cu = slope * along(vel)
            parts = ((j, shared + cu), (opp, shared - cu))
        for member, inner in parts:
            g = gx[member, i]
            relaxed = acid_weight[member] * inner - (rate - 1.0) * g
            gs[member, i] = jnp.where(solid, g, relaxed)


def dissolve_plane(sx, mx_src, cf, mx_dst, i):
    solid = sx[i] > 0.5
    mineral = mx_src[i]
    loss = (dissolve_rate * react_rate) * mineral * face_sum(cf, i)
    mx_dst[i] = jnp.where(solid, mineral - loss, mineral)


SHIFTS = [(cx, cy) for cx in (-1, 0, 1) for cy in (-1, 0, 1) if cx or cy]


def shift_masks(sx, bm, i):
    for c, (cx, cy) in enumerate(SHIFTS):
        bm[c, i] = roll_xy(sx[i], cx, cy)


def stream_plane(fs, gs, sx, fdst, gdst, i, bm=None):
    solid = sx[i] > 0.5
    masks = {}
    for q, vel in enumerate(flow_vel):
        cx, cy, cz = vel
        if vel == (0, 0, 0):
            fdst[q, i] = fs[q, i]
            continue
        opp = flow_vel.index((-cx, -cy, -cz))
        src = i - cz
        pulled = roll_xy(fs[q, src], cx, cy)
        if bm is None or (cx, cy) == (0, 0):
            blocked = roll_xy(sx[src], cx, cy) > 0.5
        else:
            blocked = bm[SHIFTS.index((cx, cy)), src] > 0.5
        masks[vel] = blocked
        arrived = jnp.where(blocked, fs[opp, i], pulled)
        fdst[q, i] = jnp.where(solid, fs[q, i], arrived)
    for j, vel in enumerate(acid_vel):
        cx, cy, cz = vel
        if vel == (0, 0, 0):
            gdst[j, i] = gs[j, i]
            continue
        opp = acid_vel.index((-cx, -cy, -cz))
        pulled = roll_xy(gs[j, i - cz], cx, cy)
        arrived = jnp.where(masks[vel], gs[opp, i], pulled)
        gdst[j, i] = jnp.where(solid, gs[j, i], arrived)


def loop(lo, hi, fn, unroll=None):
    def body(i, carry):
        fn(i)
        return carry

    if unroll is None:
        unroll = 2 if hi - lo > 4 else 1
    lax.fori_loop(lo, hi, body, 0, unroll=unroll)


UP_Q = [q for q, vel in enumerate(flow_vel) if vel[2] == 1]
DOWN_Q = [q for q, vel in enumerate(flow_vel) if vel[2] == -1]
UP_J = acid_vel.index((0, 0, 1))
DOWN_J = acid_vel.index((0, 0, -1))
NFLUX = 3 + 2 * (len(UP_Q) + 1) + 2


def flux_kernel(pop, sol, mnr, sld, up, down, fs, gs, f1, g1, m1, sx, cx, sm, cf):
    planes = sld.shape[0]
    hi, lo = planes - HALO - 1, HALO
    sx[...] = sld[...].astype(jnp.float32)
    loop(lo - 2, hi + 3, lambda i: edge_state(sx, sol, mnr, cx, sm, cf, i))

    def step1(i):
        dissolve_plane(sx, mnr, cf, m1, i)
        collide_plane(pop, sol, sx, cx, sm, fs, gs, i)

    loop(lo - 1, hi + 2, step1)
    for dst, i, qs, j in ((up, hi, UP_Q, UP_J), (down, lo, DOWN_Q, DOWN_J)):
        dst[0] = sx[i]
        dst[1] = sm[i]
        dst[2] = cf[i]
        for n, q in enumerate(qs):
            dst[3 + n] = fs[q, i]
        dst[3 + len(qs)] = gs[j, i]
    loop(lo, hi + 1, lambda i: stream_plane(fs, gs, sx, f1, g1, i))
    for i in range(lo - 1, hi + 2):
        sm[i] = jnp.where(sx[i] > 0.5, m1[i], 0.0)
    for i in range(lo, hi + 1):
        conc = g1[0, i]
        for j in range(1, NG):
            conc = conc + g1[j, i]
        cx[i] = conc
        cf[i] = jnp.where(sx[i] > 0.5, 0.0, conc)
    loop(lo, hi + 1, lambda i: collide_plane(f1, g1, sx, cx, sm, fs, gs, i))
    base = 4 + len(UP_Q)
    for dst, i, qs, j in ((up, hi, UP_Q, UP_J), (down, lo, DOWN_Q, DOWN_J)):
        dst[base] = sm[i]
        dst[base + 1] = cf[i]
        for n, q in enumerate(qs):
            dst[base + 2 + n] = fs[q, i]
        dst[base + 2 + len(qs)] = gs[j, i]
    up[NFLUX:NFLUX + HALO] = sx[planes - HALO:planes]
    down[NFLUX:NFLUX + HALO] = sx[0:HALO]


def set_bounds(flo, fhi, sm, cf, fs, gs, last, base):
    sm[0] = flo[base]
    cf[0] = flo[base + 1]
    sm[last] = fhi[base]
    cf[last] = fhi[base + 1]

    def posts():
        for n, q in enumerate(UP_Q):
            fs[q, 0] = flo[base + 2 + n]
        gs[UP_J, 0] = flo[base + 2 + len(UP_Q)]
        for n, q in enumerate(DOWN_Q):
            fs[q, last] = fhi[base + 2 + n]
        gs[DOWN_J, last] = fhi[base + 2 + len(DOWN_Q)]

    return posts


def main_kernel(
    mv, pop, sol, mnr, sld, hlo, hhi, flo, fhi,
    out_f, out_g, out_m, out_s,
    fx, gx, fs, gs, mx, m1, sx, si, cx, sm, cf, zf, zi, bm, sem, osem, zsem,
):
    planes = sld.shape[0]
    cap = out_s.shape[0]
    last = planes + 2 * HALO + 1
    own = HALO + 1
    top = own + planes
    fill = [
        (pop, fx.at[:, own:top]),
        (sol, gx.at[:, own:top]),
        (mnr, mx.at[own:top]),
        (hlo.at[0:NF], fx.at[:, 1:own]),
        (hlo.at[NF:NF + NG], gx.at[:, 1:own]),
        (hlo.at[NF + NG], mx.at[1:own]),
        (hhi.at[0:NF], fx.at[:, top:last]),
        (hhi.at[NF:NF + NG], gx.at[:, top:last]),
        (hhi.at[NF + NG], mx.at[top:last]),
    ]
    copies = [pltpu.make_async_copy(s, d, sem.at[k]) for k, (s, d) in enumerate(fill)]
    for c in copies:
        c.start()
    sx[own:top] = sld[...].astype(jnp.float32)
    si[own:top] = sld[...]
    sx[0] = flo[0]
    sx[last] = fhi[0]
    sx[1:own] = flo[NFLUX:NFLUX + HALO]
    sx[top:last] = fhi[NFLUX:NFLUX + HALO]
    zf[...] = jnp.zeros(zf.shape, zf.dtype)
    zi[...] = jnp.zeros(zi.shape, zi.dtype)
    for c in copies[1:]:
        c.wait()
    si[1:own] = (sx[1:own] > 0.5).astype(jnp.int32)
    si[top:last] = (sx[top:last] > 0.5).astype(jnp.int32)

    from_low, send_low, send_high, from_high = mv[0], mv[1], mv[2], mv[3]
    valid_end = from_low + planes - send_low - send_high + from_high

    def plane_valid(i):
        p = i - own
        low = (p >= -from_low) & (p < 0)
        kept = (p >= send_low) & (p < planes - send_high)
        high = (p >= planes) & (p < planes + from_high)
        return low | kept | high

    def plane_copies(i):
        p = i - own
        s = p + from_low - jnp.where(p >= send_low, send_low, 0) - jnp.where(p >= planes, send_high, 0)
        s = jnp.clip(s, 0, cap - 1)
        srcs = (fx.at[:, i], gx.at[:, i], mx.at[i], si.at[i])
        dsts = (out_f.at[:, s], out_g.at[:, s], out_m.at[s], out_s.at[s])
        return [pltpu.make_async_copy(x, y, osem.at[i, k]) for k, (x, y) in enumerate(zip(srcs, dsts))]

    def zero_copies(s):
        srcs = (zf, zf.at[0:NG], zf.at[0], zi)
        dsts = (out_f.at[:, s], out_g.at[:, s], out_m.at[s], out_s.at[s])
        return [pltpu.make_async_copy(x, y, zsem.at[s, k]) for k, (x, y) in enumerate(zip(srcs, dsts))]

    for s in range(cap):
        @pl.when(s >= valid_end)
        def _():
            for c in zero_copies(s):
                c.start()

    loop(0, last + 1, lambda i: shift_masks(sx, bm, i))

    posts = set_bounds(flo, fhi, sm, cf, fs, gs, last, 1)
    loop(1, last, lambda i: edge_state(sx, gx, mx, cx, sm, cf, i))
    copies[0].wait()

    posts()

    def collide1(i):
        dissolve_plane(sx, mx, cf, m1, i)
        collide_plane(fx, gx, sx, cx, sm, fs, gs, i)

    def step1(i):
        collide1(i)
        stream_plane(fs, gs, sx, fx, gx, i - 1, bm)
        edge_state(sx, gx, m1, cx, sm, cf, i - 1)

    collide1(1)
    loop(2, last, step1, unroll=1)
    stream_plane(fs, gs, sx, fx, gx, last - 1, bm)
    edge_state(sx, gx, m1, cx, sm, cf, last - 1)

    posts = set_bounds(flo, fhi, sm, cf, fs, gs, last, 4 + len(UP_Q))

    posts()

    def send_plane(i):
        @pl.when(plane_valid(i))
        def _():
            for c in plane_copies(i):
                c.start()

    def collide2(i):
        dissolve_plane(sx, m1, cf, mx, i)
        collide_plane(fx, gx, sx, cx, sm, fs, gs, i)

    def step2(i):
        collide2(i)
        stream_plane(fs, gs, sx, fx, gx, i - 1, bm)

        @pl.when(i > 2)
        def _():
            send_plane(i - 2)

    collide2(1)
    loop(2, last, step2, unroll=1)
    send_plane(last - 2)
    stream_plane(fs, gs, sx, fx, gx, last - 1, bm)
    send_plane(last - 1)
    for i in range(1, last):
        @pl.when(plane_valid(i))
        def _():
            for c in plane_copies(i):
                c.wait()
    for s in range(cap):
        @pl.when(s >= valid_end)
        def _():
            for c in zero_copies(s):
                c.wait()


def edge_kernel(lo, pop, sol, mnr, out, buf_f, buf_g, buf_m, sem):
    cuts = (0, 7, 13, NF)
    srcs = [pop.at[a:b, lo:lo + HALO] for a, b in zip(cuts[:-1], cuts[1:])]
    bufs = [buf_f.at[a:b] for a, b in zip(cuts[:-1], cuts[1:])]
    dsts = [out.at[a:b] for a, b in zip(cuts[:-1], cuts[1:])]
    srcs += [sol.at[:, lo:lo + HALO], mnr.at[lo:lo + HALO]]
    bufs += [buf_g, buf_m]
    dsts += [out.at[NF:NF + NG], out.at[NF + NG]]
    reads = [pltpu.make_async_copy(s, b, sem.at[0, k]) for k, (s, b) in enumerate(zip(srcs, bufs))]
    writes = [pltpu.make_async_copy(b, d, sem.at[1, k]) for k, (b, d) in enumerate(zip(bufs, dsts))]
    for c in reads:
        c.start()
    for r, w in zip(reads, writes):
        r.wait()
        w.start()
    for w in writes:
        w.wait()


def shards(populations, solute, mineral, solid, plane_moves):
    planes = populations.shape[1]
    cap = planes + 2 * MOVE_MOST
    ext = planes + 2 * HALO + 2
    count = lax.axis_size("blk")
    forward = [(i, (i + 1) % count) for i in range(count)]
    backward = [(i, (i - 1) % count) for i in range(count)]

    plane = populations.shape[2:]
    f32 = jnp.float32
    any_spec = pl.BlockSpec(memory_space=pl.ANY)
    vmem = pl.BlockSpec(memory_space=pltpu.VMEM)
    smem = pl.BlockSpec(memory_space=pltpu.SMEM)

    def edge(lo):
        return pl.pallas_call(
            functools.partial(edge_kernel, lo),
            out_shape=jax.ShapeDtypeStruct((NF + NG + 1, HALO) + plane, f32),
            in_specs=[any_spec, any_spec, any_spec],
            out_specs=any_spec,
            scratch_shapes=[
                pltpu.VMEM((NF, HALO) + plane, f32),
                pltpu.VMEM((NG, HALO) + plane, f32),
                pltpu.VMEM((HALO,) + plane, f32),
                pltpu.SemaphoreType.DMA((2, 5)),
            ],
        )(populations, solute, mineral)

    halo_lo = lax.ppermute(edge(planes - HALO), "blk", forward)
    halo_hi = lax.ppermute(edge(0), "blk", backward)

    up, down = pl.pallas_call(
        flux_kernel,
        out_shape=(
            jax.ShapeDtypeStruct((NFLUX + HALO,) + plane, f32),
            jax.ShapeDtypeStruct((NFLUX + HALO,) + plane, f32),
        ),
        in_specs=[vmem] * 4,
        out_specs=[vmem] * 2,
        scratch_shapes=[
            pltpu.VMEM((NF, planes) + plane, f32),
            pltpu.VMEM((NG, planes) + plane, f32),
            pltpu.VMEM((NF, planes) + plane, f32),
            pltpu.VMEM((NG, planes) + plane, f32),
        ]
        + [pltpu.VMEM((planes,) + plane, f32)] * 5,
    )(populations, solute, mineral, solid)
    flux_lo = lax.ppermute(up, "blk", forward)
    flux_hi = lax.ppermute(down, "blk", backward)

    me = lax.axis_index("blk")
    from_low = plane_moves[jnp.mod(me - 1, count), 1]
    send_low = plane_moves[me, 0]
    send_high = plane_moves[me, 1]
    from_high = plane_moves[jnp.mod(me + 1, count), 0]
    mv = jnp.stack([from_low, send_low, send_high, from_high]).astype(jnp.int32)

    return pl.pallas_call(
        main_kernel,
        out_shape=(
            jax.ShapeDtypeStruct((NF, cap) + plane, f32),
            jax.ShapeDtypeStruct((NG, cap) + plane, f32),
            jax.ShapeDtypeStruct((cap,) + plane, f32),
            jax.ShapeDtypeStruct((cap,) + plane, jnp.int32),
        ),
        in_specs=[smem, any_spec, any_spec, any_spec, vmem, any_spec, any_spec, vmem, vmem],
        out_specs=[any_spec] * 4,
        scratch_shapes=[
            pltpu.VMEM((NF, ext) + plane, f32),
            pltpu.VMEM((NG, ext) + plane, f32),
            pltpu.VMEM((NF, ext) + plane, f32),
            pltpu.VMEM((NG, ext) + plane, f32),
            pltpu.VMEM((ext,) + plane, f32),
            pltpu.VMEM((ext,) + plane, f32),
            pltpu.VMEM((ext,) + plane, f32),
            pltpu.VMEM((ext,) + plane, jnp.int32),
            pltpu.VMEM((ext,) + plane, f32),
            pltpu.VMEM((ext,) + plane, f32),
            pltpu.VMEM((ext,) + plane, f32),
            pltpu.VMEM((NF,) + plane, f32),
            pltpu.VMEM(plane, jnp.int32),
            pltpu.VMEM((len(SHIFTS), ext) + plane, f32),
            pltpu.SemaphoreType.DMA((9,)),
            pltpu.SemaphoreType.DMA((ext, 4)),
            pltpu.SemaphoreType.DMA((cap, 4)),
        ],
        compiler_params=pltpu.CompilerParams(vmem_limit_bytes=50 * 1024 * 1024),
    )(mv, populations, solute, mineral, solid, halo_lo, halo_hi, flux_lo, flux_hi)


def solution(mesh):
    return jax.shard_map(
        shards,
        mesh=mesh,
        in_specs=(
            P(None, "blk", None, None),
            P(None, "blk", None, None),
            P("blk", None, None),
            P("blk", None, None),
            P(),
        ),
        out_specs=(
            P(None, "blk", None, None),
            P(None, "blk", None, None),
            P("blk", None, None),
            P("blk", None, None),
        ),
        check_vma=False,
    )
```
